32 devices in a mesh: dp: 2 (over core), ctx: 4 (over z), expert: 4 (over y, x).
Axes of the slice: x: 2, y: 2, z: 4, core: 2. Of those that a mesh axis runs over, the one named last changes fastest.
Arguments:
- x_in: bfloat16 [4, 64, 8192], P('dp', 'ctx', 'expert'), may hold values from -6 to 6
- z_in: bfloat16 [4, 64, 8192], P('dp', 'ctx', 'expert'), may hold values from -6 to 6
- b_in: bfloat16 [4, 64, 128], P('dp', 'ctx'), may hold values from -0.5 to 0.5
- c_in: bfloat16 [4, 64, 128], P('dp', 'ctx'), may hold values from -0.75 to 0.75
- decay_log: float32 [4, 64, 128], P('dp', 'ctx', 'expert'), may hold values from -2 to 0, as said below
- skip: float32 [128], P('expert'), may hold values from 0.5 to 1.5
- out_weight: bfloat16 [8192, 4096], P('expert', 'ctx'), may hold values from -1 to 1
- moe_gain: float32 [4096], replicated, may hold values from 0.5 to 1.5
- gate_up: bfloat16 [4, 2, 7168, 4096], P('expert', None, ('dp', 'ctx')), may hold values from -0.09375 to 0.09375
- expert_ids: int32 [4, 64, 2], P('dp', ('ctx', 'expert')), may hold values from 0 to 3, as said below
- slot_ids: int32 [4, 64, 2], P('dp', ('ctx', 'expert')), may hold values from 0 to 7, as said below
Outputs:
- mamba_out: bfloat16 [4, 64, 4096], P('dp', ('ctx', 'expert'))
- expert_hidden: bfloat16 [4, 7168, 256], P('expert', ('dp', 'ctx'))
The draws below stay inside these ranges and needn't reach their ends.
Inputs may be any that keep to these rules, and one draw needn't show every extreme that they name: `decay_log`: its values are negative. `expert_ids`: each token names two different experts. In the rows of one device (streams s with the same s // 2, positions t with the same t // 4) one expert, the same for all devices, is named by exactly 8 rows, and no expert by more than 8 rows. `slot_ids`: in the rows of one device the pairs (expert, slot) are all different.
All inputs are finite; a program needn't handle non-finite values.
Results may differ from the reference program's by a relative error of at most 0.0085.
Values may be sent and summed in bfloat16 or wider, within the bound.
No kernel may reach another device: no remote copies, remote signals or barrier semaphores. Data moves between devices by JAX's collectives and lax.ppermute only.
A program may use at most 128 MiB of HBM per device.

```python
import math
import jax
import jax.numpy as jnp
from jax import lax

D = 4096
HEADS = 128
P_SIZE = 64
N = 128
FF = 7168
TOPK = 2
STREAMS_DEV = 2
PB = 4
EXPERTS = 4
CH = 16
LEN = 64
STREAMS = 4
CAP = 8
SLOTS = 256


def draw_decay_log(key, part):
    keys = jax.random.split(key, 7)
    share = 0.5
    fast_flag = jax.random.uniform(keys[0], (HEADS,)) < share
    quick_decay_rate = jnp.exp(jax.random.uniform(keys[1], (HEADS,), minval=math.log(1.0 / 50.0), maxval=math.log(1.0 / 30.0)))
    slow_rate = jnp.exp(jax.random.uniform(keys[2], (HEADS,), minval=math.log(0.05 / LEN), maxval=math.log(0.4 / LEN)))
    forgetting_factor = jnp.where(fast_flag, quick_decay_rate, slow_rate)
    per_place = jnp.exp(jax.random.uniform(keys[3], (STREAMS, LEN // CH, CH, HEADS), minval=-math.log(2.0), maxval=math.log(2.0)))
    per_block = jnp.exp(jax.random.uniform(keys[4], (STREAMS, LEN // CH, 1, HEADS), minval=-math.log(2.0), maxval=math.log(2.0)))
    element_distribution = (per_place * per_block).reshape(STREAMS, LEN, HEADS)
    capacity_indices = jax.random.randint(keys[5], (STREAMS, 2, 1), 0, LEN)
    dispatch_shares = jax.random.uniform(keys[6], (STREAMS, 2, 1), minval=0.22, maxval=0.69)
    specialist_positions_table = jnp.arange(LEN)[None, None, :]
    sequence_element_batch = jnp.sum(jnp.where(specialist_positions_table == capacity_indices, dispatch_shares, 0.0), axis=1)
    return -(forgetting_factor[None, None, :] * element_distribution) - sequence_element_batch[:, :, None]


def draw_out_weight(key, part):
    keys = jax.random.split(key, 2)
    entries = jnp.clip(jax.random.normal(keys[0], (HEADS * P_SIZE, D)), -4.0, 4.0)
    column_scale = jnp.exp(jax.random.uniform(keys[1], (1, D), minval=math.log(1.0 / 3.0), maxval=math.log(3.0)))
    return (entries * column_scale * (1.0 / math.sqrt(HEADS * P_SIZE))).astype(jnp.bfloat16)


def route_table(key):
    row_count = STREAMS_DEV * PB
    stream_groups = STREAMS // STREAMS_DEV
    place_groups = LEN // PB
    segment_number = stream_groups * place_groups
    hot = jax.random.randint(jax.random.fold_in(key, 7), (), 0, EXPERTS)
    block_keys = jax.random.split(jax.random.fold_in(key, 11), segment_number)
    extra = 2 * row_count - CAP

    def one_block(block_key):
        keys = jax.random.split(block_key, 3)
        others = jax.random.permutation(keys[0], EXPERTS - 1)
        others = others + (others >= hot).astype(others.dtype)
        picks = jnp.arange(extra)
        select_specialist = others[picks % (EXPERTS - 1)]
        pick_slot = picks // (EXPERTS - 1)
        rows = jnp.arange(row_count)
        first_pick = jnp.where(rows < CAP, rows, CAP + 2 * (rows - CAP))
        second_pick = jnp.where(rows < CAP, rows, CAP + 2 * (rows - CAP) + 1)
        expert_a = jnp.where(rows < CAP, hot, select_specialist[first_pick])
        slot_a = jnp.where(rows < CAP, rows, pick_slot[first_pick])
        expert_b = jnp.where(rows < CAP, select_specialist[first_pick], select_specialist[second_pick])
        slot_b = jnp.where(rows < CAP, pick_slot[first_pick], pick_slot[second_pick])
        flips = jax.random.randint(keys[1], (row_count,), 0, 2)
        ids = jnp.stack([jnp.where(flips == 1, expert_b, expert_a), jnp.where(flips == 1, expert_a, expert_b)], axis=1)
        slots = jnp.stack([jnp.where(flips == 1, slot_b, slot_a), jnp.where(flips == 1, slot_a, slot_b)], axis=1)
        order = jax.random.permutation(keys[2], row_count)
        return (ids[order], slots[order])
    ids, slots = jax.vmap(one_block)(block_keys)
    ids = ids.reshape(stream_groups, place_groups, STREAMS_DEV, PB, TOPK).transpose(0, 2, 1, 3, 4).reshape(STREAMS, LEN, TOPK)
    slots = slots.reshape(stream_groups, place_groups, STREAMS_DEV, PB, TOPK).transpose(0, 2, 1, 3, 4).reshape(STREAMS, LEN, TOPK)
    return (ids.astype(jnp.int32), slots.astype(jnp.int32))


def draw_expert_ids(key, part):
    return route_table(key)[0]


def draw_slot_ids(key, part):
    return route_table(key)[1]


def level_of(key, shape, cuts, low, high):
    factor_of = 1.0
    for dim, blocks in cuts:
        steps = jax.random.uniform(jax.random.fold_in(jax.random.fold_in(key, 6), dim), (blocks,), jnp.float32, low / len(cuts), high / len(cuts))
        factor_of = factor_of * jnp.repeat(jnp.exp(steps), shape[dim] // blocks).reshape((-1,) + (1,) * (len(shape) - 1 - dim))
    return factor_of


def scatter_about(key, shape, spread, reach, cuts=(), kind=jnp.bfloat16):
    loudness = level_of(key, shape, cuts, -0.22, 0.18) if cuts else 1.0
    values = jax.random.normal(key, shape, jnp.float32) * spread * loudness
    return jnp.minimum(jnp.maximum(values, -reach), reach).astype(kind)


def setup_inputs(seed: int = 0) -> dict:
    key_list = jax.random.split(jax.random.key(seed), 12)
    return {
        "x_in": scatter_about(key_list[0], (STREAMS, LEN, HEADS * P_SIZE), 1.0, 6.0, ((0, 2), (1, 4), (2, 4))),
        "z_in": scatter_about(key_list[1], (STREAMS, LEN, HEADS * P_SIZE), 1.0, 6.0, ((0, 2), (1, 4), (2, 4))),
        "b_in": scatter_about(key_list[2], (STREAMS, LEN, N), N ** -0.5, 0.5, ((0, 2), (1, 4))),
        "c_in": scatter_about(key_list[3], (STREAMS, LEN, N), 0.125, 0.75, ((0, 2), (1, 4))),
        "decay_log": draw_decay_log(jax.random.fold_in(key_list[11], 71), 0),
        "skip": jnp.clip(0.5 + 1.0 * jax.random.uniform(key_list[5], (HEADS,), jnp.float32) ** level_of(key_list[5], (HEADS,), ((0, 4),), -0.2, 0.2), 0.5, 1.5),
        "out_weight": draw_out_weight(jax.random.fold_in(key_list[11], 71), 0),
        "moe_gain": jnp.clip(jax.random.uniform(key_list[7], (D,), jnp.float32, 0.5, 1.5), 0.5, 1.5),
        "gate_up": scatter_about(key_list[8], (EXPERTS, 2, FF, D), D ** -0.5, 0.09375, ((0, 4), (2, 8))),
        "expert_ids": draw_expert_ids(jax.random.fold_in(key_list[11], 71), 0),
        "slot_ids": draw_slot_ids(jax.random.fold_in(key_list[11], 71), 0),
    }


def reference(x_in, z_in, b_in, c_in, decay_log, skip, out_weight, moe_gain, gate_up, expert_ids, slot_ids):
    highest = lax.Precision.HIGHEST
    x_float = x_in.astype(jnp.float32).reshape(STREAMS, LEN, HEADS, P_SIZE)
    b_float = b_in.astype(jnp.float32)
    c_float = c_in.astype(jnp.float32)
    decay = jnp.exp(decay_log)

    def advance(state, inputs):
        x_step, b_step, c_step, a_step = inputs
        state = a_step[:, :, None, None] * state + x_step[:, :, :, None] * b_step[:, None, None, :]
        produced = jnp.einsum('shpn,sn->shp', state, c_step, precision=highest)
        return (state, produced)
    start_state = jnp.zeros((STREAMS, HEADS, P_SIZE, N), jnp.float32)
    inputs = (jnp.moveaxis(x_float, 1, 0), jnp.moveaxis(b_float, 1, 0), jnp.moveaxis(c_float, 1, 0), jnp.moveaxis(decay, 1, 0))
    final_state, produced = lax.scan(advance, start_state, inputs)
    ssd = jnp.moveaxis(produced, 0, 1) + skip[None, None, :, None] * x_float
    gated = (ssd.reshape(STREAMS, LEN, HEADS * P_SIZE) * jax.nn.silu(z_in.astype(jnp.float32))).astype(jnp.bfloat16)
    mamba_flat = jnp.dot(gated.reshape(STREAMS * LEN, HEADS * P_SIZE), out_weight, preferred_element_type=jnp.float32).astype(jnp.bfloat16)
    flat = mamba_flat.astype(jnp.float32)
    normed = (flat * lax.rsqrt(lax.optimization_barrier(jnp.mean(flat * flat, axis=1, keepdims=True)) + 1e-05) * moe_gain).astype(jnp.bfloat16)
    stream_index = jnp.arange(STREAMS, dtype=jnp.int32)[:, None, None]
    place_index = jnp.arange(LEN, dtype=jnp.int32)[None, :, None]
    group = (stream_index // STREAMS_DEV * (LEN // CH) + place_index // CH) * (CH // PB) + place_index % CH // PB
    slot_index = (group * CAP + slot_ids).astype(jnp.int32)
    values = jnp.broadcast_to(normed.reshape(STREAMS, LEN, 1, D), (STREAMS, LEN, TOPK, D))
    dispatched = jnp.zeros((EXPERTS, SLOTS, D), jnp.bfloat16).at[expert_ids, slot_index].set(values)

    def per_expert(inputs):
        rows, weights = inputs
        both = jnp.einsum('gfd,qd->gfq', weights.astype(jnp.float32), rows.astype(jnp.float32), preferred_element_type=jnp.float32)
        return (jax.nn.silu(both[0]) * both[1]).astype(jnp.bfloat16)
    expert_hidden = lax.map(per_expert, (dispatched, gate_up))
    return (mamba_flat.reshape(STREAMS, LEN, D), expert_hidden)
```

```python
import jax
import jax.numpy as jnp
from jax import lax
from jax.sharding import PartitionSpec as P

P_SIZE = 64
ALL_AXES = ("dp", "ctx", "expert")


def mixer(x_in, b_in, c_in, decay_log, skip):
    highest = lax.Precision.HIGHEST
    seq_count, total_len, width_in = x_in.shape
    head_count = skip.shape[0]
    state_size = b_in.shape[2]
    chunk = total_len if total_len <= 128 else 64
    chunks = total_len // chunk
    x_float = x_in.astype(jnp.float32).reshape(seq_count, chunks, chunk, head_count, P_SIZE)
    b_float = b_in.astype(jnp.float32).reshape(seq_count, chunks, chunk, state_size)
    c_float = c_in.astype(jnp.float32).reshape(seq_count, chunks, chunk, state_size)
    cum_decay = jnp.cumsum(decay_log.reshape(seq_count, chunks, chunk, head_count), axis=2)
    scores = jnp.einsum("sktn,skun->sktu", c_float, b_float, precision=highest)
    causal = (jnp.arange(chunk)[:, None] >= jnp.arange(chunk)[None, :])[None, None, :, :, None]
    spans = cum_decay[:, :, :, None, :] - cum_decay[:, :, None, :, :]
    kernel = jnp.where(causal, jnp.exp(jnp.where(causal, spans, 0.0)), 0.0) * scores[..., None]
    ssd = jnp.einsum("sktuh,skuhp->skthp", kernel, x_float, precision=highest)
    if chunks > 1:
        final_decay = cum_decay[:, :, -1, :]
        tails = jnp.exp(final_decay[:, :, None, :] - cum_decay)
        states = jnp.einsum("skuh,skuhp,skun->skhpn", tails, x_float, b_float, precision=highest)

        def step(carry, inputs):
            decay_k, state_k = inputs
            return decay_k[:, :, None, None] * carry + state_k, carry

        _, incoming = lax.scan(
            step,
            jnp.zeros_like(states[:, 0]),
            (jnp.moveaxis(jnp.exp(final_decay), 1, 0), jnp.moveaxis(states, 1, 0)),
        )
        incoming = jnp.moveaxis(incoming, 0, 1)
        ssd = ssd + jnp.exp(cum_decay)[..., None] * jnp.einsum(
            "sktn,skhpn->skthp", c_float, incoming, precision=highest
        )
    ssd = ssd + skip[None, None, None, :, None] * x_float
    return ssd.reshape(seq_count, total_len, width_in)


def expert_ffn(gate_up, slot_rows):
    both = jnp.einsum("gfd,qd->gfq", gate_up[0], slot_rows, preferred_element_type=jnp.float32)
    return (jax.nn.silu(both[0]) * both[1]).astype(jnp.bfloat16)


def dispatch_routed(partial_value, moe_gain, gate_up, expert_ids, slot_ids, capacity):
    seq_count = partial_value.shape[0]
    model_width = moe_gain.shape[0]
    per_block = expert_ids.shape[1]
    pick_count = expert_ids.shape[2]
    row_count = seq_count * per_block
    ctx_count = lax.axis_size("ctx")
    group_count = lax.axis_size("expert")
    grouped = partial_value.reshape(
        seq_count, ctx_count, group_count, per_block, partial_value.shape[2]
    )
    reduced = lax.psum_scatter(grouped, "expert", scatter_dimension=2, tiled=True).astype(
        jnp.bfloat16
    )
    swapped = lax.all_to_all(reduced, "ctx", split_axis=1, concat_axis=4, tiled=True)
    mamba_out = swapped.reshape(seq_count, per_block, model_width)
    flat = mamba_out.reshape(row_count, model_width).astype(jnp.float32)
    scale = lax.rsqrt(jnp.mean(flat * flat, axis=1, keepdims=True) + 1e-05)
    normed = (flat * scale * moe_gain[None, :]).astype(jnp.bfloat16)
    chosen = expert_ids.reshape(row_count, pick_count)
    placed = slot_ids.reshape(row_count, pick_count)
    match_expert = chosen[:, :, None, None] == jnp.arange(group_count)[None, None, :, None]
    match_slot = placed[:, :, None, None] == jnp.arange(capacity)[None, None, None, :]
    selector = (match_expert & match_slot).astype(jnp.bfloat16)
    outgoing = jnp.einsum(
        "rkec,rd->ecd", selector, normed, preferred_element_type=jnp.float32
    ).astype(jnp.bfloat16)
    arrived = lax.all_to_all(outgoing, "expert", split_axis=0, concat_axis=0, tiled=True)
    piece = lax.all_gather(arrived[None], ("dp", "ctx"), axis=0, tiled=True)
    slot_rows = piece.reshape(-1, piece.shape[3])
    return (mamba_out, expert_ffn(gate_up, slot_rows)[None])


def local(
    x_in, z_in, b_in, c_in, decay_log, skip, out_weight, moe_gain, gate_up, expert_ids, slot_ids
):
    seq_count, block_len, width_in = x_in.shape
    state_size = b_in.shape[2]
    model_width = moe_gain.shape[0]
    col_width = out_weight.shape[1]
    per_block = expert_ids.shape[1]
    pick_count = expert_ids.shape[2]
    dp_count = lax.axis_size("dp")
    ctx_count = lax.axis_size("ctx")
    group_count = lax.axis_size("expert")
    device_count = dp_count * ctx_count * group_count
    row_count = seq_count * per_block
    capacity = max(2, 4 * row_count // group_count)

    packed = jnp.concatenate([x_in, z_in, b_in, c_in], axis=2)
    packed = lax.all_gather(packed, "ctx", axis=1, tiled=True)
    decay_all = lax.all_gather(decay_log, "ctx", axis=1, tiled=True)
    route = jnp.stack([expert_ids, slot_ids], axis=-1)
    routes = lax.all_gather(route[None], ALL_AXES, axis=0, tiled=True)

    x_all = packed[:, :, :width_in]
    z_all = packed[:, :, width_in : 2 * width_in]
    b_all = packed[:, :, 2 * width_in : 2 * width_in + state_size]
    c_all = packed[:, :, 2 * width_in + state_size :]
    ssd = mixer(x_all, b_all, c_all, decay_all, skip)
    gated = (ssd * jax.nn.silu(z_all.astype(jnp.float32))).astype(jnp.bfloat16)
    partial_value = jnp.einsum(
        "stk,kd->std", gated, out_weight, preferred_element_type=jnp.float32
    )
    if device_count * row_count * model_width * 2 > (8 << 20):
        return dispatch_routed(partial_value, moe_gain, gate_up, expert_ids, slot_ids, capacity)
    grouped = partial_value.reshape(seq_count, ctx_count, group_count, per_block, col_width)
    grouped = jnp.moveaxis(grouped, 2, 0)
    reduced = lax.psum_scatter(grouped, "expert", scatter_dimension=0, tiled=True)
    reduced = reduced.astype(jnp.bfloat16)
    gathered = lax.all_gather(reduced, ALL_AXES, axis=0, tiled=True)
    gathered = gathered.reshape(
        dp_count, ctx_count, group_count, seq_count, ctx_count, per_block, col_width
    )
    tokens = jnp.transpose(gathered, (0, 4, 2, 3, 5, 1, 6)).reshape(
        device_count, row_count, model_width
    )
    me = (lax.axis_index("dp") * ctx_count + lax.axis_index("ctx")) * group_count + lax.axis_index(
        "expert"
    )
    mamba_out = lax.dynamic_index_in_dim(tokens, me, axis=0, keepdims=False).reshape(
        seq_count, per_block, model_width
    )
    flat = tokens.reshape(device_count * row_count, model_width).astype(jnp.float32)
    scale = lax.rsqrt(jnp.mean(flat * flat, axis=1, keepdims=True) + 1e-05)
    normed = (flat * scale * moe_gain[None, :]).astype(jnp.bfloat16)

    chosen = routes[..., 0].reshape(device_count, row_count, pick_count)
    placed = routes[..., 1].reshape(device_count, row_count, pick_count)
    target = jnp.arange(device_count)[:, None, None] * capacity + placed
    mine = chosen == lax.axis_index("expert")
    slot_count = device_count * capacity
    hit = mine[..., None] & (target[..., None] == jnp.arange(slot_count))
    selector = jnp.any(hit, axis=2).reshape(device_count * row_count, slot_count)
    dispatched = jnp.einsum(
        "rq,rd->qd", selector.astype(jnp.bfloat16), normed, preferred_element_type=jnp.float32
    ).astype(jnp.bfloat16)
    hidden = expert_ffn(gate_up, dispatched)
    return (mamba_out, hidden[None])


def solution(mesh):
    in_specs = (
        P("dp", "ctx", "expert"),
        P("dp", "ctx", "expert"),
        P("dp", "ctx", None),
        P("dp", "ctx", None),
        P("dp", "ctx", "expert"),
        P("expert"),
        P("expert", "ctx"),
        P(),
        P("expert", None, ("dp", "ctx"), None),
        P("dp", ("ctx", "expert"), None),
        P("dp", ("ctx", "expert"), None),
    )
    out_specs = (P("dp", ("ctx", "expert"), None), P("expert", ("dp", "ctx"), None))
    return jax.shard_map(local, mesh=mesh, in_specs=in_specs, out_specs=out_specs, check_vma=False)
```

```python
import jax
import jax.numpy as jnp
from jax import lax
from jax.sharding import PartitionSpec as P

P_SIZE = 64
ALL_AXES = ("dp", "ctx", "expert")


def mixer(x_in, b_in, c_in, decay_log, skip):
    highest = lax.Precision.HIGHEST
    seq_count, total_len, width_in = x_in.shape
    head_count = skip.shape[0]
    state_size = b_in.shape[2]
    chunk = total_len if total_len <= 128 else 64
    chunks = total_len // chunk
    x_float = x_in.astype(jnp.float32).reshape(seq_count, chunks, chunk, head_count, P_SIZE)
    b_float = b_in.astype(jnp.float32).reshape(seq_count, chunks, chunk, state_size)
    c_float = c_in.astype(jnp.float32).reshape(seq_count, chunks, chunk, state_size)
    cum_decay = jnp.cumsum(decay_log.reshape(seq_count, chunks, chunk, head_count), axis=2)
    scores = jnp.einsum("sktn,skun->sktu", c_float, b_float, precision=highest)
    causal = (jnp.arange(chunk)[:, None] >= jnp.arange(chunk)[None, :])[None, None, :, :, None]
    spans = cum_decay[:, :, :, None, :] - cum_decay[:, :, None, :, :]
    kernel = jnp.where(causal, jnp.exp(jnp.where(causal, spans, 0.0)), 0.0) * scores[..., None]
    ssd = jnp.einsum("sktuh,skuhp->skthp", kernel, x_float, precision=highest)
    if chunks > 1:
        final_decay = cum_decay[:, :, -1, :]
        tails = jnp.exp(final_decay[:, :, None, :] - cum_decay)
        states = jnp.einsum("skuh,skuhp,skun->skhpn", tails, x_float, b_float, precision=highest)

        def step(carry, inputs):
            decay_k, state_k = inputs
            return decay_k[:, :, None, None] * carry + state_k, carry

        _, incoming = lax.scan(
            step,
            jnp.zeros_like(states[:, 0]),
            (jnp.moveaxis(jnp.exp(final_decay), 1, 0), jnp.moveaxis(states, 1, 0)),
        )
        incoming = jnp.moveaxis(incoming, 0, 1)
        ssd = ssd + jnp.exp(cum_decay)[..., None] * jnp.einsum(
            "sktn,skhpn->skthp", c_float, incoming, precision=highest
        )
    ssd = ssd + skip[None, None, None, :, None] * x_float
    return ssd.reshape(seq_count, total_len, width_in)


def expert_ffn(gate_up, slot_rows):
    both = jnp.einsum("gfd,qd->gfq", gate_up[0], slot_rows, preferred_element_type=jnp.float32)
    return (jax.nn.silu(both[0]) * both[1]).astype(jnp.bfloat16)


def dispatch_routed(partial_value, moe_gain, gate_up, expert_ids, slot_ids, capacity):
    seq_count = partial_value.shape[0]
    model_width = moe_gain.shape[0]
    per_block = expert_ids.shape[1]
    pick_count = expert_ids.shape[2]
    row_count = seq_count * per_block
    ctx_count = lax.axis_size("ctx")
    group_count = lax.axis_size("expert")
    grouped = partial_value.reshape(
        seq_count, ctx_count, group_count, per_block, partial_value.shape[2]
    )
    reduced = lax.psum_scatter(grouped, "expert", scatter_dimension=2, tiled=True).astype(
        jnp.bfloat16
    )
    swapped = lax.all_to_all(reduced, "ctx", split_axis=1, concat_axis=4, tiled=True)
    mamba_out = swapped.reshape(seq_count, per_block, model_width)
    flat = mamba_out.reshape(row_count, model_width).astype(jnp.float32)
    scale = lax.rsqrt(jnp.mean(flat * flat, axis=1, keepdims=True) + 1e-05)
    normed = (flat * scale * moe_gain[None, :]).astype(jnp.bfloat16)
    chosen = expert_ids.reshape(row_count, pick_count)
    placed = slot_ids.reshape(row_count, pick_count)
    match_expert = chosen[:, :, None, None] == jnp.arange(group_count)[None, None, :, None]
    match_slot = placed[:, :, None, None] == jnp.arange(capacity)[None, None, None, :]
    selector = (match_expert & match_slot).astype(jnp.bfloat16)
    outgoing = jnp.einsum(
        "rkec,rd->ecd", selector, normed, preferred_element_type=jnp.float32
    ).astype(jnp.bfloat16)
    arrived = lax.all_to_all(outgoing, "expert", split_axis=0, concat_axis=0, tiled=True)
    piece = lax.all_gather(arrived[None], ("dp", "ctx"), axis=0, tiled=True)
    slot_rows = piece.reshape(-1, piece.shape[3])
    return (mamba_out, expert_ffn(gate_up, slot_rows)[None])


def local(
    x_in, z_in, b_in, c_in, decay_log, skip, out_weight, moe_gain, gate_up, expert_ids, slot_ids
):
    seq_count, block_len, width_in = x_in.shape
    state_size = b_in.shape[2]
    model_width = moe_gain.shape[0]
    col_width = out_weight.shape[1]
    per_block = expert_ids.shape[1]
    pick_count = expert_ids.shape[2]
    dp_count = lax.axis_size("dp")
    ctx_count = lax.axis_size("ctx")
    group_count = lax.axis_size("expert")
    device_count = dp_count * ctx_count * group_count
    row_count = seq_count * per_block
    capacity = max(2, 4 * row_count // group_count)

    packed = jnp.concatenate([x_in, z_in, b_in, c_in], axis=2)
    packed = lax.all_gather(packed, "ctx", axis=1, tiled=True)
    decay_all = lax.all_gather(decay_log, "ctx", axis=1, tiled=True)
    route = jnp.stack([expert_ids, slot_ids], axis=-1)
    routes = lax.all_gather(route[None], ALL_AXES, axis=0, tiled=True)

    packed, decay_all, routes = lax.optimization_barrier((packed, decay_all, routes))
    x_all = packed[:, :, :width_in]
    z_all = packed[:, :, width_in : 2 * width_in]
    b_all = packed[:, :, 2 * width_in : 2 * width_in + state_size]
    c_all = packed[:, :, 2 * width_in + state_size :]
    ssd = mixer(x_all, b_all, c_all, decay_all, skip)
    gated = (ssd * jax.nn.silu(z_all.astype(jnp.float32))).astype(jnp.bfloat16)
    partial_value = jnp.einsum(
        "stk,kd->std", gated, out_weight, preferred_element_type=jnp.float32
    )
    if device_count * row_count * model_width * 2 > (8 << 20):
        return dispatch_routed(partial_value, moe_gain, gate_up, expert_ids, slot_ids, capacity)
    summed = lax.psum(partial_value, "expert").astype(jnp.bfloat16)
    gathered = lax.all_gather(summed[None], ("dp", "ctx"), axis=0, tiled=True)
    gathered = gathered.reshape(
        dp_count, ctx_count, seq_count, ctx_count, group_count, per_block, col_width
    )
    tokens = jnp.transpose(gathered, (0, 3, 4, 2, 5, 1, 6)).reshape(
        device_count, row_count, model_width
    )
    me = (lax.axis_index("dp") * ctx_count + lax.axis_index("ctx")) * group_count + lax.axis_index(
        "expert"
    )
    mamba_out = lax.dynamic_index_in_dim(tokens, me, axis=0, keepdims=False).reshape(
        seq_count, per_block, model_width
    )
    flat = tokens.reshape(device_count * row_count, model_width).astype(jnp.float32)
    scale = lax.rsqrt(jnp.mean(flat * flat, axis=1, keepdims=True) + 1e-05)
    normed = (flat * scale * moe_gain[None, :]).astype(jnp.bfloat16)

    chosen = routes[..., 0].reshape(device_count, row_count, pick_count)
    placed = routes[..., 1].reshape(device_count, row_count, pick_count)
    target = jnp.arange(device_count)[:, None, None] * capacity + placed
    mine = chosen == lax.axis_index("expert")
    slot_count = device_count * capacity
    hit = mine[..., None] & (target[..., None] == jnp.arange(slot_count))
    selector = jnp.any(hit, axis=2).reshape(device_count * row_count, slot_count)
    dispatched = jnp.einsum(
        "rq,rd->qd", selector.astype(jnp.bfloat16), normed, preferred_element_type=jnp.float32
    ).astype(jnp.bfloat16)
    hidden = expert_ffn(gate_up, dispatched)
    return (mamba_out, hidden[None])


def solution(mesh):
    in_specs = (
        P("dp", "ctx", "expert"),
        P("dp", "ctx", "expert"),
        P("dp", "ctx", None),
        P("dp", "ctx", None),
        P("dp", "ctx", "expert"),
        P("expert"),
        P("expert", "ctx"),
        P(),
        P("expert", None, ("dp", "ctx"), None),
        P("dp", ("ctx", "expert"), None),
        P("dp", ("ctx", "expert"), None),
    )
    out_specs = (P("dp", ("ctx", "expert"), None), P("expert", ("dp", "ctx"), None))
    return jax.shard_map(local, mesh=mesh, in_specs=in_specs, out_specs=out_specs, check_vma=False)
```

```python
import jax
import jax.numpy as jnp
from jax import lax
from jax.sharding import PartitionSpec as P

P_SIZE = 64
ALL_AXES = ("dp", "ctx", "expert")


def mixer(x_in, b_in, c_in, decay_log, skip):
    highest = lax.Precision.HIGHEST
    seq_count, total_len, width_in = x_in.shape
    head_count = skip.shape[0]
    state_size = b_in.shape[2]
    chunk = total_len if total_len <= 128 else 64
    chunks = total_len // chunk
    x_float = x_in.astype(jnp.float32).reshape(seq_count, chunks, chunk, head_count, P_SIZE)
    b_float = b_in.astype(jnp.float32).reshape(seq_count, chunks, chunk, state_size)
    c_float = c_in.astype(jnp.float32).reshape(seq_count, chunks, chunk, state_size)
    cum_decay = jnp.cumsum(decay_log.reshape(seq_count, chunks, chunk, head_count), axis=2)
    scores = jnp.einsum("sktn,skun->sktu", c_float, b_float, precision=highest)
    causal = (jnp.arange(chunk)[:, None] >= jnp.arange(chunk)[None, :])[None, None, :, :, None]
    spans = cum_decay[:, :, :, None, :] - cum_decay[:, :, None, :, :]
    kernel = jnp.where(causal, jnp.exp(jnp.where(causal, spans, 0.0)), 0.0) * scores[..., None]
    ssd = jnp.einsum("sktuh,skuhp->skthp", kernel, x_float, precision=highest)
    if chunks > 1:
        final_decay = cum_decay[:, :, -1, :]
        tails = jnp.exp(final_decay[:, :, None, :] - cum_decay)
        states = jnp.einsum("skuh,skuhp,skun->skhpn", tails, x_float, b_float, precision=highest)

        def step(carry, inputs):
            decay_k, state_k = inputs
            return decay_k[:, :, None, None] * carry + state_k, carry

        _, incoming = lax.scan(
            step,
            jnp.zeros_like(states[:, 0]),
            (jnp.moveaxis(jnp.exp(final_decay), 1, 0), jnp.moveaxis(states, 1, 0)),
        )
        incoming = jnp.moveaxis(incoming, 0, 1)
        ssd = ssd + jnp.exp(cum_decay)[..., None] * jnp.einsum(
            "sktn,skhpn->skthp", c_float, incoming, precision=highest
        )
    ssd = ssd + skip[None, None, None, :, None] * x_float
    return ssd.reshape(seq_count, total_len, width_in)


def expert_ffn(gate_up, slot_rows):
    both = jnp.einsum("gfd,qd->gfq", gate_up[0], slot_rows, preferred_element_type=jnp.float32)
    return (jax.nn.silu(both[0]) * both[1]).astype(jnp.bfloat16)


def dispatch_routed(partial_value, moe_gain, gate_up, expert_ids, slot_ids, capacity):
    seq_count = partial_value.shape[0]
    model_width = moe_gain.shape[0]
    per_block = expert_ids.shape[1]
    pick_count = expert_ids.shape[2]
    row_count = seq_count * per_block
    ctx_count = lax.axis_size("ctx")
    group_count = lax.axis_size("expert")
    grouped = partial_value.reshape(
        seq_count, ctx_count, group_count, per_block, partial_value.shape[2]
    )
    reduced = lax.psum_scatter(grouped, "expert", scatter_dimension=2, tiled=True).astype(
        jnp.bfloat16
    )
    swapped = lax.all_to_all(reduced, "ctx", split_axis=1, concat_axis=4, tiled=True)
    mamba_out = swapped.reshape(seq_count, per_block, model_width)
    flat = mamba_out.reshape(row_count, model_width).astype(jnp.float32)
    scale = lax.rsqrt(jnp.mean(flat * flat, axis=1, keepdims=True) + 1e-05)
    normed = (flat * scale * moe_gain[None, :]).astype(jnp.bfloat16)
    chosen = expert_ids.reshape(row_count, pick_count)
    placed = slot_ids.reshape(row_count, pick_count)
    match_expert = chosen[:, :, None, None] == jnp.arange(group_count)[None, None, :, None]
    match_slot = placed[:, :, None, None] == jnp.arange(capacity)[None, None, None, :]
    selector = (match_expert & match_slot).astype(jnp.bfloat16)
    outgoing = jnp.einsum(
        "rkec,rd->ecd", selector, normed, preferred_element_type=jnp.float32
    ).astype(jnp.bfloat16)
    arrived = lax.all_to_all(outgoing, "expert", split_axis=0, concat_axis=0, tiled=True)
    piece = lax.all_gather(arrived[None], ("dp", "ctx"), axis=0, tiled=True)
    slot_rows = piece.reshape(-1, piece.shape[3])
    return (mamba_out, expert_ffn(gate_up, slot_rows)[None])


def local(
    x_in, z_in, b_in, c_in, decay_log, skip, out_weight, moe_gain, gate_up, expert_ids, slot_ids
):
    seq_count, block_len, width_in = x_in.shape
    state_size = b_in.shape[2]
    model_width = moe_gain.shape[0]
    col_width = out_weight.shape[1]
    per_block = expert_ids.shape[1]
    pick_count = expert_ids.shape[2]
    dp_count = lax.axis_size("dp")
    ctx_count = lax.axis_size("ctx")
    group_count = lax.axis_size("expert")
    device_count = dp_count * ctx_count * group_count
    row_count = seq_count * per_block
    capacity = max(2, 4 * row_count // group_count)

    packed = jnp.concatenate([x_in, z_in, b_in, c_in], axis=2)
    packed = lax.all_gather(packed, "ctx", axis=1, tiled=True)
    decay_all = lax.all_gather(decay_log, "ctx", axis=1, tiled=True)
    packed, decay_all = lax.optimization_barrier((packed, decay_all))

    x_all = packed[:, :, :width_in]
    z_all = packed[:, :, width_in : 2 * width_in]
    b_all = packed[:, :, 2 * width_in : 2 * width_in + state_size]
    c_all = packed[:, :, 2 * width_in + state_size :]
    ssd = mixer(x_all, b_all, c_all, decay_all, skip)
    gated = (ssd * jax.nn.silu(z_all.astype(jnp.float32))).astype(jnp.bfloat16)
    partial_value = jnp.einsum(
        "stk,kd->std", gated, out_weight, preferred_element_type=jnp.float32
    )
    if device_count * row_count * model_width * 2 > (8 << 20):
        return dispatch_routed(partial_value, moe_gain, gate_up, expert_ids, slot_ids, capacity)
    total_len = partial_value.shape[1]
    route = jnp.stack([expert_ids, slot_ids], axis=-1).astype(jnp.float32).reshape(-1)
    route_len = route.shape[0]
    extra_rows = -(-(group_count * route_len) // col_width)
    route_row = jnp.zeros((extra_rows * col_width,), jnp.float32)
    route_row = lax.dynamic_update_slice(route_row, route, (lax.axis_index("expert") * route_len,))
    extended = jnp.concatenate(
        [partial_value.reshape(seq_count * total_len, col_width), route_row.reshape(extra_rows, col_width)],
        axis=0,
    )
    summed = lax.psum(extended, "expert").astype(jnp.bfloat16)
    gathered = lax.all_gather(summed[None], ("dp", "ctx"), axis=0, tiled=True)
    gathered = gathered.reshape(dp_count, ctx_count, seq_count * total_len + extra_rows, col_width)
    routes = gathered[:, :, seq_count * total_len :, :].reshape(dp_count, ctx_count, -1)
    routes = routes[:, :, : group_count * route_len].astype(jnp.int32)
    routes = routes.reshape(dp_count, ctx_count, group_count, seq_count, per_block, pick_count, 2)
    routes = jnp.transpose(routes, (0, 3, 1, 2, 4, 5, 6))
    tokens = gathered[:, :, : seq_count * total_len, :].reshape(
        dp_count, ctx_count, seq_count, total_len, col_width
    )
    tokens = jnp.transpose(tokens, (0, 2, 3, 1, 4))
    tok_blocks = tokens.reshape(dp_count, seq_count, ctx_count * group_count, per_block, model_width)
    mine_block = lax.axis_index("ctx") * group_count + lax.axis_index("expert")
    mamba_out = lax.dynamic_index_in_dim(
        lax.dynamic_index_in_dim(tok_blocks, lax.axis_index("dp"), axis=0, keepdims=False),
        mine_block,
        axis=1,
        keepdims=False,
    )
    token_count = dp_count * seq_count * total_len
    flat = tokens.reshape(token_count, model_width).astype(jnp.float32)
    scale = lax.rsqrt(jnp.mean(flat * flat, axis=1, keepdims=True) + 1e-05)
    normed = (flat * scale * moe_gain[None, :]).astype(jnp.bfloat16)

    group = (
        (jnp.arange(dp_count)[:, None, None, None, None] * ctx_count
         + jnp.arange(ctx_count)[None, None, :, None, None]) * group_count
        + jnp.arange(group_count)[None, None, None, :, None]
    )
    group = jnp.broadcast_to(group, (dp_count, seq_count, ctx_count, group_count, per_block))
    target = group.reshape(token_count, 1) * capacity + routes[..., 1].reshape(token_count, pick_count)
    mine = routes[..., 0].reshape(token_count, pick_count) == lax.axis_index("expert")
    slot_count = device_count * capacity
    hit = mine[..., None] & (target[..., None] == jnp.arange(slot_count))
    selector = jnp.any(hit, axis=1)
    dispatched = jnp.einsum(
        "rq,rd->qd", selector.astype(jnp.bfloat16), normed, preferred_element_type=jnp.float32
    ).astype(jnp.bfloat16)
    hidden = expert_ffn(gate_up, dispatched)
    return (mamba_out, hidden[None])


def solution(mesh):
    in_specs = (
        P("dp", "ctx", "expert"),
        P("dp", "ctx", "expert"),
        P("dp", "ctx", None),
        P("dp", "ctx", None),
        P("dp", "ctx", "expert"),
        P("expert"),
        P("expert", "ctx"),
        P(),
        P("expert", None, ("dp", "ctx"), None),
        P("dp", ("ctx", "expert"), None),
        P("dp", ("ctx", "expert"), None),
    )
    out_specs = (P("dp", ("ctx", "expert"), None), P("expert", ("dp", "ctx"), None))
    return jax.shard_map(local, mesh=mesh, in_specs=in_specs, out_specs=out_specs, check_vma=False)
```

```python
import jax
import jax.numpy as jnp
from jax import lax
from jax.sharding import PartitionSpec as P

P_SIZE = 64
ALL_AXES = ("dp", "ctx", "expert")


def mixer(x_in, b_in, c_in, decay_log, skip):
    highest = lax.Precision.HIGHEST
    seq_count, total_len, width_in = x_in.shape
    head_count = skip.shape[0]
    state_size = b_in.shape[2]
    chunk = total_len if total_len <= 128 else 64
    chunks = total_len // chunk
    x_float = x_in.astype(jnp.float32).reshape(seq_count, chunks, chunk, head_count, P_SIZE)
    b_float = b_in.astype(jnp.float32).reshape(seq_count, chunks, chunk, state_size)
    c_float = c_in.astype(jnp.float32).reshape(seq_count, chunks, chunk, state_size)
    cum_decay = jnp.cumsum(decay_log.reshape(seq_count, chunks, chunk, head_count), axis=2)
    scores = jnp.einsum("sktn,skun->sktu", c_float, b_float, precision=highest)
    causal = (jnp.arange(chunk)[:, None] >= jnp.arange(chunk)[None, :])[None, None, :, :, None]
    spans = cum_decay[:, :, :, None, :] - cum_decay[:, :, None, :, :]
    kernel = jnp.where(causal, jnp.exp(jnp.where(causal, spans, 0.0)), 0.0) * scores[..., None]
    ssd = jnp.einsum("sktuh,skuhp->skthp", kernel, x_float, precision=highest)
    if chunks > 1:
        final_decay = cum_decay[:, :, -1, :]
        tails = jnp.exp(final_decay[:, :, None, :] - cum_decay)
        states = jnp.einsum("skuh,skuhp,skun->skhpn", tails, x_float, b_float, precision=highest)

        def step(carry, inputs):
            decay_k, state_k = inputs
            return decay_k[:, :, None, None] * carry + state_k, carry

        _, incoming = lax.scan(
            step,
            jnp.zeros_like(states[:, 0]),
            (jnp.moveaxis(jnp.exp(final_decay), 1, 0), jnp.moveaxis(states, 1, 0)),
        )
        incoming = jnp.moveaxis(incoming, 0, 1)
        ssd = ssd + jnp.exp(cum_decay)[..., None] * jnp.einsum(
            "sktn,skhpn->skthp", c_float, incoming, precision=highest
        )
    ssd = ssd + skip[None, None, None, :, None] * x_float
    return ssd.reshape(seq_count, total_len, width_in)


def expert_ffn(gate_up, slot_rows):
    both = jnp.einsum("gfd,qd->gfq", gate_up[0], slot_rows, preferred_element_type=jnp.float32)
    return (jax.nn.silu(both[0]) * both[1]).astype(jnp.bfloat16)


def dispatch_routed(partial_value, moe_gain, gate_up, expert_ids, slot_ids, capacity):
    seq_count = partial_value.shape[0]
    model_width = moe_gain.shape[0]
    per_block = expert_ids.shape[1]
    pick_count = expert_ids.shape[2]
    row_count = seq_count * per_block
    ctx_count = lax.axis_size("ctx")
    group_count = lax.axis_size("expert")
    grouped = partial_value.reshape(
        seq_count, ctx_count, group_count, per_block, partial_value.shape[2]
    )
    reduced = lax.psum_scatter(grouped, "expert", scatter_dimension=2, tiled=True).astype(
        jnp.bfloat16
    )
    swapped = lax.all_to_all(reduced, "ctx", split_axis=1, concat_axis=4, tiled=True)
    mamba_out = swapped.reshape(seq_count, per_block, model_width)
    flat = mamba_out.reshape(row_count, model_width).astype(jnp.float32)
    scale = lax.rsqrt(jnp.mean(flat * flat, axis=1, keepdims=True) + 1e-05)
    normed = (flat * scale * moe_gain[None, :]).astype(jnp.bfloat16)
    chosen = expert_ids.reshape(row_count, pick_count)
    placed = slot_ids.reshape(row_count, pick_count)
    match_expert = chosen[:, :, None, None] == jnp.arange(group_count)[None, None, :, None]
    match_slot = placed[:, :, None, None] == jnp.arange(capacity)[None, None, None, :]
    selector = (match_expert & match_slot).astype(jnp.bfloat16)
    outgoing = jnp.einsum(
        "rkec,rd->ecd", selector, normed, preferred_element_type=jnp.float32
    ).astype(jnp.bfloat16)
    arrived = lax.all_to_all(outgoing, "expert", split_axis=0, concat_axis=0, tiled=True)
    piece = lax.all_gather(arrived[None], ("dp", "ctx"), axis=0, tiled=True)
    slot_rows = piece.reshape(-1, piece.shape[3])
    return (mamba_out, expert_ffn(gate_up, slot_rows)[None])


def local(
    x_in, z_in, b_in, c_in, decay_log, skip, out_weight, moe_gain, gate_up, expert_ids, slot_ids
):
    seq_count, block_len, width_in = x_in.shape
    state_size = b_in.shape[2]
    model_width = moe_gain.shape[0]
    col_width = out_weight.shape[1]
    per_block = expert_ids.shape[1]
    pick_count = expert_ids.shape[2]
    dp_count = lax.axis_size("dp")
    ctx_count = lax.axis_size("ctx")
    group_count = lax.axis_size("expert")
    device_count = dp_count * ctx_count * group_count
    row_count = seq_count * per_block
    capacity = max(2, 4 * row_count // group_count)

    packed = jnp.concatenate([x_in, z_in, b_in, c_in], axis=2)
    packed = lax.all_gather(packed, "ctx", axis=1, tiled=True)
    decay_all = lax.all_gather(decay_log, "ctx", axis=1, tiled=True)
    packed, decay_all = lax.optimization_barrier((packed, decay_all))

    x_all = packed[:, :, :width_in]
    z_all = packed[:, :, width_in : 2 * width_in]
    b_all = packed[:, :, 2 * width_in : 2 * width_in + state_size]
    c_all = packed[:, :, 2 * width_in + state_size :]
    ssd = mixer(x_all, b_all, c_all, decay_all, skip)
    gated = (ssd * jax.nn.silu(z_all.astype(jnp.float32))).astype(jnp.bfloat16)
    partial_value = jnp.einsum(
        "stk,kd->std", gated, out_weight, preferred_element_type=jnp.float32
    )
    if device_count * row_count * model_width * 2 > (8 << 20):
        return dispatch_routed(partial_value, moe_gain, gate_up, expert_ids, slot_ids, capacity)
    total_len = partial_value.shape[1]
    route = jnp.stack([expert_ids, slot_ids], axis=-1).astype(jnp.float32).reshape(-1)
    route_len = route.shape[0]
    extra_rows = -(-(group_count * route_len) // col_width)
    route_row = jnp.zeros((extra_rows * col_width,), jnp.float32)
    route_row = lax.dynamic_update_slice(route_row, route, (lax.axis_index("expert") * route_len,))
    extended = jnp.concatenate(
        [partial_value.reshape(seq_count * total_len, col_width), route_row.reshape(extra_rows, col_width)],
        axis=0,
    )
    summed = lax.psum(extended.astype(jnp.bfloat16), "expert")
    gathered = lax.all_gather(summed[None], ("dp", "ctx"), axis=0, tiled=True)
    gathered = gathered.reshape(dp_count, ctx_count, seq_count * total_len + extra_rows, col_width)
    routes = gathered[:, :, seq_count * total_len :, :].reshape(dp_count, ctx_count, -1)
    routes = routes[:, :, : group_count * route_len].astype(jnp.int32)
    routes = routes.reshape(dp_count, ctx_count, group_count, seq_count, per_block, pick_count, 2)
    routes = jnp.transpose(routes, (0, 3, 1, 2, 4, 5, 6))
    row_total = seq_count * total_len
    tokens = gathered[:, :, :row_total, :]
    mine_rows = lax.dynamic_index_in_dim(tokens, lax.axis_index("dp"), axis=0, keepdims=False)
    mine_rows = mine_rows.reshape(ctx_count, seq_count, ctx_count * group_count, per_block, col_width)
    mine_block = lax.axis_index("ctx") * group_count + lax.axis_index("expert")
    mine_rows = lax.dynamic_index_in_dim(mine_rows, mine_block, axis=2, keepdims=False)
    mamba_out = jnp.transpose(mine_rows, (1, 2, 0, 3)).reshape(seq_count, per_block, model_width)
    token_count = dp_count * row_total
    flat = tokens.astype(jnp.float32)
    square_sum = jnp.sum(flat * flat, axis=(1, 3), keepdims=True)
    scale = lax.rsqrt(square_sum / model_width + 1e-05)
    gain = moe_gain.reshape(1, ctx_count, 1, col_width)
    normed = (flat * scale * gain).astype(jnp.bfloat16)

    group = (
        (jnp.arange(dp_count)[:, None, None, None, None] * ctx_count
         + jnp.arange(ctx_count)[None, None, :, None, None]) * group_count
        + jnp.arange(group_count)[None, None, None, :, None]
    )
    group = jnp.broadcast_to(group, (dp_count, seq_count, ctx_count, group_count, per_block))
    target = group.reshape(token_count, 1) * capacity + routes[..., 1].reshape(token_count, pick_count)
    mine = routes[..., 0].reshape(token_count, pick_count) == lax.axis_index("expert")
    slot_count = device_count * capacity
    hit = mine[..., None] & (target[..., None] == jnp.arange(slot_count))
    selector = jnp.any(hit, axis=1).reshape(dp_count, row_total, slot_count)
    dispatched = jnp.einsum(
        "drq,dcrk->qck", selector.astype(jnp.bfloat16), normed, preferred_element_type=jnp.float32
    ).astype(jnp.bfloat16)
    hidden = expert_ffn(gate_up, dispatched.reshape(slot_count, model_width))
    return (mamba_out, hidden[None])


def solution(mesh):
    in_specs = (
        P("dp", "ctx", "expert"),
        P("dp", "ctx", "expert"),
        P("dp", "ctx", None),
        P("dp", "ctx", None),
        P("dp", "ctx", "expert"),
        P("expert"),
        P("expert", "ctx"),
        P(),
        P("expert", None, ("dp", "ctx"), None),
        P("dp", ("ctx", "expert"), None),
        P("dp", ("ctx", "expert"), None),
    )
    out_specs = (P("dp", ("ctx", "expert"), None), P("expert", ("dp", "ctx"), None))
    return jax.shard_map(local, mesh=mesh, in_specs=in_specs, out_specs=out_specs, check_vma=False)
```

```python
import jax
import jax.numpy as jnp
from jax import lax
from jax.sharding import PartitionSpec as P

P_SIZE = 64
ALL_AXES = ("dp", "ctx", "expert")


def mixer(x_in, b_in, c_in, decay_log, skip):
    highest = lax.Precision.HIGHEST
    seq_count, total_len, width_in = x_in.shape
    head_count = skip.shape[0]
    state_size = b_in.shape[2]
    chunk = total_len if total_len <= 128 else 64
    chunks = total_len // chunk
    x_float = x_in.astype(jnp.float32).reshape(seq_count, chunks, chunk, head_count, P_SIZE)
    b_float = b_in.astype(jnp.float32).reshape(seq_count, chunks, chunk, state_size)
    c_float = c_in.astype(jnp.float32).reshape(seq_count, chunks, chunk, state_size)
    cum_decay = jnp.cumsum(decay_log.reshape(seq_count, chunks, chunk, head_count), axis=2)
    scores = jnp.einsum("sktn,skun->sktu", c_float, b_float, precision=highest)
    causal = (jnp.arange(chunk)[:, None] >= jnp.arange(chunk)[None, :])[None, None, :, :, None]
    spans = cum_decay[:, :, :, None, :] - cum_decay[:, :, None, :, :]
    kernel = jnp.where(causal, jnp.exp(jnp.where(causal, spans, 0.0)), 0.0) * scores[..., None]
    ssd = jnp.einsum("sktuh,skuhp->skthp", kernel, x_float, precision=highest)
    if chunks > 1:
        final_decay = cum_decay[:, :, -1, :]
        tails = jnp.exp(final_decay[:, :, None, :] - cum_decay)
        states = jnp.einsum("skuh,skuhp,skun->skhpn", tails, x_float, b_float, precision=highest)

        def step(carry, inputs):
            decay_k, state_k = inputs
            return decay_k[:, :, None, None] * carry + state_k, carry

        _, incoming = lax.scan(
            step,
            jnp.zeros_like(states[:, 0]),
            (jnp.moveaxis(jnp.exp(final_decay), 1, 0), jnp.moveaxis(states, 1, 0)),
        )
        incoming = jnp.moveaxis(incoming, 0, 1)
        ssd = ssd + jnp.exp(cum_decay)[..., None] * jnp.einsum(
            "sktn,skhpn->skthp", c_float, incoming, precision=highest
        )
    ssd = ssd + skip[None, None, None, :, None] * x_float
    return ssd.reshape(seq_count, total_len, width_in)


def expert_ffn(gate_up, slot_rows):
    both = jnp.einsum("gfd,qd->gfq", gate_up[0], slot_rows, preferred_element_type=jnp.float32)
    return (jax.nn.silu(both[0]) * both[1]).astype(jnp.bfloat16)


def dispatch_routed(partial_value, moe_gain, gate_up, expert_ids, slot_ids, capacity):
    seq_count = partial_value.shape[0]
    model_width = moe_gain.shape[0]
    per_block = expert_ids.shape[1]
    pick_count = expert_ids.shape[2]
    row_count = seq_count * per_block
    ctx_count = lax.axis_size("ctx")
    group_count = lax.axis_size("expert")
    grouped = partial_value.reshape(
        seq_count, ctx_count, group_count, per_block, partial_value.shape[2]
    )
    reduced = lax.psum_scatter(grouped, "expert", scatter_dimension=2, tiled=True).astype(
        jnp.bfloat16
    )
    swapped = lax.all_to_all(reduced, "ctx", split_axis=1, concat_axis=4, tiled=True)
    mamba_out = swapped.reshape(seq_count, per_block, model_width)
    flat = mamba_out.reshape(row_count, model_width).astype(jnp.float32)
    scale = lax.rsqrt(jnp.mean(flat * flat, axis=1, keepdims=True) + 1e-05)
    normed = (flat * scale * moe_gain[None, :]).astype(jnp.bfloat16)
    chosen = expert_ids.reshape(row_count, pick_count)
    placed = slot_ids.reshape(row_count, pick_count)
    match_expert = chosen[:, :, None, None] == jnp.arange(group_count)[None, None, :, None]
    match_slot = placed[:, :, None, None] == jnp.arange(capacity)[None, None, None, :]
    selector = (match_expert & match_slot).astype(jnp.bfloat16)
    outgoing = jnp.einsum(
        "rkec,rd->ecd", selector, normed, preferred_element_type=jnp.float32
    ).astype(jnp.bfloat16)
    arrived = lax.all_to_all(outgoing, "expert", split_axis=0, concat_axis=0, tiled=True)
    piece = lax.all_gather(arrived[None], ("dp", "ctx"), axis=0, tiled=True)
    slot_rows = piece.reshape(-1, piece.shape[3])
    return (mamba_out, expert_ffn(gate_up, slot_rows)[None])


def local(
    x_in, z_in, b_in, c_in, decay_log, skip, out_weight, moe_gain, gate_up, expert_ids, slot_ids
):
    seq_count, block_len, width_in = x_in.shape
    state_size = b_in.shape[2]
    model_width = moe_gain.shape[0]
    col_width = out_weight.shape[1]
    per_block = expert_ids.shape[1]
    pick_count = expert_ids.shape[2]
    dp_count = lax.axis_size("dp")
    ctx_count = lax.axis_size("ctx")
    group_count = lax.axis_size("expert")
    device_count = dp_count * ctx_count * group_count
    row_count = seq_count * per_block
    capacity = max(2, 4 * row_count // group_count)

    packed = jnp.concatenate([x_in, z_in, b_in, c_in], axis=2)
    packed = lax.all_gather(packed, "ctx", axis=1, tiled=True)
    decay_all = lax.all_gather(decay_log, "ctx", axis=1, tiled=True)
    packed, decay_all = lax.optimization_barrier((packed, decay_all))

    x_all = packed[:, :, :width_in]
    z_all = packed[:, :, width_in : 2 * width_in]
    b_all = packed[:, :, 2 * width_in : 2 * width_in + state_size]
    c_all = packed[:, :, 2 * width_in + state_size :]
    ssd = mixer(x_all, b_all, c_all, decay_all, skip)
    gated = (ssd * jax.nn.silu(z_all.astype(jnp.float32))).astype(jnp.bfloat16)
    partial_value = jnp.einsum(
        "stk,kd->std", gated, out_weight, preferred_element_type=jnp.float32
    )
    if device_count * row_count * model_width * 2 > (8 << 20):
        return dispatch_routed(partial_value, moe_gain, gate_up, expert_ids, slot_ids, capacity)
    total_len = partial_value.shape[1]
    route = jnp.stack([expert_ids, slot_ids], axis=-1).astype(jnp.float32).reshape(-1)
    route_len = route.shape[0]
    extra_rows = -(-(group_count * route_len) // col_width)
    route_row = jnp.zeros((extra_rows * col_width,), jnp.float32)
    route_row = lax.dynamic_update_slice(route_row, route, (lax.axis_index("expert") * route_len,))
    extended = jnp.concatenate(
        [partial_value.reshape(seq_count * total_len, col_width), route_row.reshape(extra_rows, col_width)],
        axis=0,
    )
    summed = lax.psum(extended, "expert").astype(jnp.bfloat16)
    gathered = lax.all_gather(summed[None], ("dp", "ctx"), axis=0, tiled=True)
    gathered = gathered.reshape(dp_count, ctx_count, seq_count * total_len + extra_rows, col_width)
    routes = gathered[:, :, seq_count * total_len :, :].reshape(dp_count, ctx_count, -1)
    routes = routes[:, :, : group_count * route_len].astype(jnp.int32)
    routes = routes.reshape(dp_count, ctx_count, group_count, seq_count, per_block, pick_count, 2)
    routes = jnp.transpose(routes, (0, 3, 1, 2, 4, 5, 6))
    row_total = seq_count * total_len
    tokens = gathered[:, :, :row_total, :]
    mine_rows = lax.dynamic_index_in_dim(tokens, lax.axis_index("dp"), axis=0, keepdims=False)
    mine_rows = mine_rows.reshape(ctx_count, seq_count, ctx_count * group_count, per_block, col_width)
    mine_block = lax.axis_index("ctx") * group_count + lax.axis_index("expert")
    mine_rows = lax.dynamic_index_in_dim(mine_rows, mine_block, axis=2, keepdims=False)
    mamba_out = jnp.transpose(mine_rows, (1, 2, 0, 3)).reshape(seq_count, per_block, model_width)
    token_count = dp_count * row_total
    flat = tokens.astype(jnp.float32)
    square_sum = jnp.sum(flat * flat, axis=(1, 3), keepdims=True)
    scale = lax.rsqrt(square_sum / model_width + 1e-05)
    gain = moe_gain.reshape(1, ctx_count, 1, col_width)
    normed = (flat * scale * gain).astype(jnp.bfloat16)

    group = (
        (jnp.arange(dp_count)[:, None, None, None, None] * ctx_count
         + jnp.arange(ctx_count)[None, None, :, None, None]) * group_count
        + jnp.arange(group_count)[None, None, None, :, None]
    )
    group = jnp.broadcast_to(group, (dp_count, seq_count, ctx_count, group_count, per_block))
    target = group.reshape(token_count, 1) * capacity + routes[..., 1].reshape(token_count, pick_count)
    mine = routes[..., 0].reshape(token_count, pick_count) == lax.axis_index("expert")
    slot_count = device_count * capacity
    hit = mine[..., None] & (target[..., None] == jnp.arange(slot_count))
    selector = jnp.any(hit, axis=1).reshape(dp_count, row_total, slot_count)
    dispatched = jnp.einsum(
        "drq,dcrk->qck", selector.astype(jnp.bfloat16), normed, preferred_element_type=jnp.float32
    ).astype(jnp.bfloat16)
    hidden = expert_ffn(gate_up, dispatched.reshape(slot_count, model_width))
    return (mamba_out, hidden[None])


def solution(mesh):
    in_specs = (
        P("dp", "ctx", "expert"),
        P("dp", "ctx", "expert"),
        P("dp", "ctx", None),
        P("dp", "ctx", None),
        P("dp", "ctx", "expert"),
        P("expert"),
        P("expert", "ctx"),
        P(),
        P("expert", None, ("dp", "ctx"), None),
        P("dp", ("ctx", "expert"), None),
        P("dp", ("ctx", "expert"), None),
    )
    out_specs = (P("dp", ("ctx", "expert"), None), P("expert", ("dp", "ctx"), None))
    return jax.shard_map(local, mesh=mesh, in_specs=in_specs, out_specs=out_specs, check_vma=False)
```

```python
import jax
import jax.numpy as jnp
from jax import lax
from jax.sharding import PartitionSpec as P

P_SIZE = 64
ALL_AXES = ("dp", "ctx", "expert")


def gather_blocks(value, axis_name, count):
    me = lax.axis_index(axis_name)
    received = [value]
    for shift in range(1, count):
        perm = [(i, (i + shift) % count) for i in range(count)]
        received.append(lax.ppermute(value, axis_name, perm))
    order = (me - jnp.arange(count)) % count
    return jnp.take(jnp.stack(received), order, axis=0)


def sum_over(value, axis_name, count):
    if count & (count - 1) or value.shape[-1] % count:
        return lax.psum(value, axis_name).astype(jnp.bfloat16)
    me = lax.axis_index(axis_name)
    masks = []
    mask = 1
    while mask < count:
        masks.append(mask)
        mask *= 2
    data = value
    for mask in masks:
        bit = (me // mask) % 2
        halves = data.reshape(data.shape[:-1] + (2, data.shape[-1] // 2))
        keep = lax.dynamic_index_in_dim(halves, bit, axis=-2, keepdims=False)
        send = lax.dynamic_index_in_dim(halves, 1 - bit, axis=-2, keepdims=False)
        perm = [(i, i ^ mask) for i in range(count)]
        data = keep + lax.ppermute(send, axis_name, perm)
    data = data.astype(jnp.bfloat16)
    for mask in reversed(masks):
        bit = (me // mask) % 2
        perm = [(i, i ^ mask) for i in range(count)]
        other = lax.ppermute(data, axis_name, perm)
        low = jnp.where(bit == 0, data, other)
        high = jnp.where(bit == 0, other, data)
        data = jnp.concatenate([low, high], axis=-1)
    return data


def mixer(x_in, b_in, c_in, decay_log, skip):
    highest = lax.Precision.HIGHEST
    seq_count, total_len, width_in = x_in.shape
    head_count = skip.shape[0]
    state_size = b_in.shape[2]
    chunk = total_len if total_len <= 128 else 64
    chunks = total_len // chunk
    x_float = x_in.astype(jnp.float32).reshape(seq_count, chunks, chunk, head_count, P_SIZE)
    b_float = b_in.astype(jnp.float32).reshape(seq_count, chunks, chunk, state_size)
    c_float = c_in.astype(jnp.float32).reshape(seq_count, chunks, chunk, state_size)
    cum_decay = jnp.cumsum(decay_log.reshape(seq_count, chunks, chunk, head_count), axis=2)
    scores = jnp.einsum("sktn,skun->sktu", c_float, b_float, precision=highest)
    causal = (jnp.arange(chunk)[:, None] >= jnp.arange(chunk)[None, :])[None, None, :, :, None]
    spans = cum_decay[:, :, :, None, :] - cum_decay[:, :, None, :, :]
    kernel = jnp.where(causal, jnp.exp(jnp.where(causal, spans, 0.0)), 0.0) * scores[..., None]
    ssd = jnp.einsum("sktuh,skuhp->skthp", kernel, x_float, precision=highest)
    if chunks > 1:
        final_decay = cum_decay[:, :, -1, :]
        tails = jnp.exp(final_decay[:, :, None, :] - cum_decay)
        states = jnp.einsum("skuh,skuhp,skun->skhpn", tails, x_float, b_float, precision=highest)

        def step(carry, inputs):
            decay_k, state_k = inputs
            return decay_k[:, :, None, None] * carry + state_k, carry

        _, incoming = lax.scan(
            step,
            jnp.zeros_like(states[:, 0]),
            (jnp.moveaxis(jnp.exp(final_decay), 1, 0), jnp.moveaxis(states, 1, 0)),
        )
        incoming = jnp.moveaxis(incoming, 0, 1)
        ssd = ssd + jnp.exp(cum_decay)[..., None] * jnp.einsum(
            "sktn,skhpn->skthp", c_float, incoming, precision=highest
        )
    ssd = ssd + skip[None, None, None, :, None] * x_float
    return ssd.reshape(seq_count, total_len, width_in)


def expert_ffn(gate_up, slot_rows):
    both = jnp.einsum("gfd,qd->gfq", gate_up[0], slot_rows, preferred_element_type=jnp.float32)
    return (jax.nn.silu(both[0]) * both[1]).astype(jnp.bfloat16)


def dispatch_routed(partial_value, moe_gain, gate_up, expert_ids, slot_ids, capacity):
    seq_count = partial_value.shape[0]
    model_width = moe_gain.shape[0]
    per_block = expert_ids.shape[1]
    pick_count = expert_ids.shape[2]
    row_count = seq_count * per_block
    ctx_count = lax.axis_size("ctx")
    group_count = lax.axis_size("expert")
    grouped = partial_value.reshape(
        seq_count, ctx_count, group_count, per_block, partial_value.shape[2]
    )
    reduced = lax.psum_scatter(grouped, "expert", scatter_dimension=2, tiled=True).astype(
        jnp.bfloat16
    )
    swapped = lax.all_to_all(reduced, "ctx", split_axis=1, concat_axis=4, tiled=True)
    mamba_out = swapped.reshape(seq_count, per_block, model_width)
    flat = mamba_out.reshape(row_count, model_width).astype(jnp.float32)
    scale = lax.rsqrt(jnp.mean(flat * flat, axis=1, keepdims=True) + 1e-05)
    normed = (flat * scale * moe_gain[None, :]).astype(jnp.bfloat16)
    chosen = expert_ids.reshape(row_count, pick_count)
    placed = slot_ids.reshape(row_count, pick_count)
    match_expert = chosen[:, :, None, None] == jnp.arange(group_count)[None, None, :, None]
    match_slot = placed[:, :, None, None] == jnp.arange(capacity)[None, None, None, :]
    selector = (match_expert & match_slot).astype(jnp.bfloat16)
    outgoing = jnp.einsum(
        "rkec,rd->ecd", selector, normed, preferred_element_type=jnp.float32
    ).astype(jnp.bfloat16)
    arrived = lax.all_to_all(outgoing, "expert", split_axis=0, concat_axis=0, tiled=True)
    piece = lax.all_gather(arrived[None], ("dp", "ctx"), axis=0, tiled=True)
    slot_rows = piece.reshape(-1, piece.shape[3])
    return (mamba_out, expert_ffn(gate_up, slot_rows)[None])


def local(
    x_in, z_in, b_in, c_in, decay_log, skip, out_weight, moe_gain, gate_up, expert_ids, slot_ids
):
    seq_count, block_len, width_in = x_in.shape
    state_size = b_in.shape[2]
    model_width = moe_gain.shape[0]
    col_width = out_weight.shape[1]
    per_block = expert_ids.shape[1]
    pick_count = expert_ids.shape[2]
    dp_count = lax.axis_size("dp")
    ctx_count = lax.axis_size("ctx")
    group_count = lax.axis_size("expert")
    device_count = dp_count * ctx_count * group_count
    row_count = seq_count * per_block
    capacity = max(2, 4 * row_count // group_count)

    packed = jnp.concatenate([x_in, z_in, b_in, c_in], axis=2)
    packed = jnp.moveaxis(gather_blocks(packed, "ctx", ctx_count), 0, 1).reshape(
        seq_count, ctx_count * block_len, packed.shape[2]
    )
    decay_all = jnp.moveaxis(gather_blocks(decay_log, "ctx", ctx_count), 0, 1).reshape(
        seq_count, ctx_count * block_len, decay_log.shape[2]
    )
    packed, decay_all = lax.optimization_barrier((packed, decay_all))

    x_all = packed[:, :, :width_in]
    z_all = packed[:, :, width_in : 2 * width_in]
    b_all = packed[:, :, 2 * width_in : 2 * width_in + state_size]
    c_all = packed[:, :, 2 * width_in + state_size :]
    ssd = mixer(x_all, b_all, c_all, decay_all, skip)
    gated = (ssd * jax.nn.silu(z_all.astype(jnp.float32))).astype(jnp.bfloat16)
    partial_value = jnp.einsum(
        "stk,kd->std", gated, out_weight, preferred_element_type=jnp.float32
    )
    if device_count * row_count * model_width * 2 > (8 << 20):
        return dispatch_routed(partial_value, moe_gain, gate_up, expert_ids, slot_ids, capacity)
    total_len = partial_value.shape[1]
    route = jnp.stack([expert_ids, slot_ids], axis=-1).astype(jnp.float32).reshape(-1)
    route_len = route.shape[0]
    extra_rows = -(-(group_count * route_len) // col_width)
    route_row = jnp.zeros((extra_rows * col_width,), jnp.float32)
    route_row = lax.dynamic_update_slice(route_row, route, (lax.axis_index("expert") * route_len,))
    extended = jnp.concatenate(
        [partial_value.reshape(seq_count * total_len, col_width), route_row.reshape(extra_rows, col_width)],
        axis=0,
    )
    summed = sum_over(extended, "expert", group_count)
    gathered = gather_blocks(gather_blocks(summed, "ctx", ctx_count), "dp", dp_count)
    gathered = gathered.reshape(dp_count, ctx_count, seq_count * total_len + extra_rows, col_width)
    routes = gathered[:, :, seq_count * total_len :, :].reshape(dp_count, ctx_count, -1)
    routes = routes[:, :, : group_count * route_len].astype(jnp.int32)
    routes = routes.reshape(dp_count, ctx_count, group_count, seq_count, per_block, pick_count, 2)
    routes = jnp.transpose(routes, (0, 3, 1, 2, 4, 5, 6))
    row_total = seq_count * total_len
    tokens = gathered[:, :, :row_total, :]
    mine_rows = lax.dynamic_index_in_dim(tokens, lax.axis_index("dp"), axis=0, keepdims=False)
    mine_rows = mine_rows.reshape(ctx_count, seq_count, ctx_count * group_count, per_block, col_width)
    mine_block = lax.axis_index("ctx") * group_count + lax.axis_index("expert")
    mine_rows = lax.dynamic_index_in_dim(mine_rows, mine_block, axis=2, keepdims=False)
    mamba_out = jnp.transpose(mine_rows, (1, 2, 0, 3)).reshape(seq_count, per_block, model_width)
    token_count = dp_count * row_total
    flat = tokens.astype(jnp.float32)
    square_sum = jnp.sum(flat * flat, axis=(1, 3), keepdims=True)
    scale = lax.rsqrt(square_sum / model_width + 1e-05)
    gain = moe_gain.reshape(1, ctx_count, 1, col_width)
    normed = (flat * scale * gain).astype(jnp.bfloat16)

    group = (
        (jnp.arange(dp_count)[:, None, None, None, None] * ctx_count
         + jnp.arange(ctx_count)[None, None, :, None, None]) * group_count
        + jnp.arange(group_count)[None, None, None, :, None]
    )
    group = jnp.broadcast_to(group, (dp_count, seq_count, ctx_count, group_count, per_block))
    target = group.reshape(token_count, 1) * capacity + routes[..., 1].reshape(token_count, pick_count)
    mine = routes[..., 0].reshape(token_count, pick_count) == lax.axis_index("expert")
    slot_count = device_count * capacity
    hit = mine[..., None] & (target[..., None] == jnp.arange(slot_count))
    selector = jnp.any(hit, axis=1).reshape(dp_count, row_total, slot_count)
    dispatched = jnp.einsum(
        "drq,dcrk->qck", selector.astype(jnp.bfloat16), normed, preferred_element_type=jnp.float32
    ).astype(jnp.bfloat16)
    hidden = expert_ffn(gate_up, dispatched.reshape(slot_count, model_width))
    return (mamba_out, hidden[None])


def solution(mesh):
    in_specs = (
        P("dp", "ctx", "expert"),
        P("dp", "ctx", "expert"),
        P("dp", "ctx", None),
        P("dp", "ctx", None),
        P("dp", "ctx", "expert"),
        P("expert"),
        P("expert", "ctx"),
        P(),
        P("expert", None, ("dp", "ctx"), None),
        P("dp", ("ctx", "expert"), None),
        P("dp", ("ctx", "expert"), None),
    )
    out_specs = (P("dp", ("ctx", "expert"), None), P("expert", ("dp", "ctx"), None))
    return jax.shard_map(local, mesh=mesh, in_specs=in_specs, out_specs=out_specs, check_vma=False)
```

```python
import jax
import jax.numpy as jnp
from jax import lax
from jax.sharding import PartitionSpec as P

P_SIZE = 64
ALL_AXES = ("dp", "ctx", "expert")


def gather_blocks(value, axis_name, count):
    me = lax.axis_index(axis_name)
    received = [value]
    for shift in range(1, count):
        perm = [(i, (i + shift) % count) for i in range(count)]
        received.append(lax.ppermute(value, axis_name, perm))
    order = (me - jnp.arange(count)) % count
    return jnp.take(jnp.stack(received), order, axis=0)


def sum_over(value, axis_name, count):
    if count & (count - 1) or value.shape[-1] % count:
        return lax.psum(value, axis_name).astype(jnp.bfloat16)
    me = lax.axis_index(axis_name)
    pieces = value.reshape(value.shape[:-1] + (count, value.shape[-1] // count))
    total = lax.dynamic_index_in_dim(pieces, me, axis=-2, keepdims=False)
    for shift in range(1, count):
        perm = [(i, i ^ shift) for i in range(count)]
        send = lax.dynamic_index_in_dim(pieces, me ^ shift, axis=-2, keepdims=False)
        total = total + lax.ppermute(send, axis_name, perm)
    total = total.astype(jnp.bfloat16)
    received = [total]
    for shift in range(1, count):
        perm = [(i, i ^ shift) for i in range(count)]
        received.append(lax.ppermute(total, axis_name, perm))
    ordered = jnp.take(jnp.stack(received, axis=-2), me ^ jnp.arange(count), axis=-2)
    return ordered.reshape(value.shape)


def split_exact(value):
    high = value.astype(jnp.bfloat16)
    rest = value - lax.optimization_barrier(high).astype(jnp.float32)
    middle = rest.astype(jnp.bfloat16)
    low = (rest - lax.optimization_barrier(middle).astype(jnp.float32)).astype(jnp.bfloat16)
    return [high, middle, low]


def join_exact(parts):
    high, middle, low = (part.astype(jnp.float32) for part in parts)
    return (high + middle) + low


def mixer(x_in, b_in, c_in, decay_log, skip):
    highest = lax.Precision.HIGHEST
    seq_count, total_len, width_in = x_in.shape
    head_count = skip.shape[0]
    state_size = b_in.shape[2]
    chunk = total_len if total_len <= 128 else 64
    chunks = total_len // chunk
    x_float = x_in.astype(jnp.float32).reshape(seq_count, chunks, chunk, head_count, P_SIZE)
    b_float = b_in.astype(jnp.float32).reshape(seq_count, chunks, chunk, state_size)
    c_float = c_in.astype(jnp.float32).reshape(seq_count, chunks, chunk, state_size)
    cum_decay = jnp.cumsum(decay_log.reshape(seq_count, chunks, chunk, head_count), axis=2)
    scores = jnp.einsum("sktn,skun->sktu", c_float, b_float, precision=highest)
    causal = (jnp.arange(chunk)[:, None] >= jnp.arange(chunk)[None, :])[None, None, :, :, None]
    spans = cum_decay[:, :, :, None, :] - cum_decay[:, :, None, :, :]
    kernel = jnp.where(causal, jnp.exp(jnp.where(causal, spans, 0.0)), 0.0) * scores[..., None]
    ssd = jnp.einsum("sktuh,skuhp->skthp", kernel, x_float, precision=highest)
    if chunks > 1:
        final_decay = cum_decay[:, :, -1, :]
        tails = jnp.exp(final_decay[:, :, None, :] - cum_decay)
        states = jnp.einsum("skuh,skuhp,skun->skhpn", tails, x_float, b_float, precision=highest)

        def step(carry, inputs):
            decay_k, state_k = inputs
            return decay_k[:, :, None, None] * carry + state_k, carry

        _, incoming = lax.scan(
            step,
            jnp.zeros_like(states[:, 0]),
            (jnp.moveaxis(jnp.exp(final_decay), 1, 0), jnp.moveaxis(states, 1, 0)),
        )
        incoming = jnp.moveaxis(incoming, 0, 1)
        ssd = ssd + jnp.exp(cum_decay)[..., None] * jnp.einsum(
            "sktn,skhpn->skthp", c_float, incoming, precision=highest
        )
    ssd = ssd + skip[None, None, None, :, None] * x_float
    return ssd.reshape(seq_count, total_len, width_in)


def expert_ffn(gate_up, slot_rows):
    both = jnp.einsum("gfd,qd->gfq", gate_up[0], slot_rows, preferred_element_type=jnp.float32)
    return (jax.nn.silu(both[0]) * both[1]).astype(jnp.bfloat16)


def dispatch_routed(partial_value, moe_gain, gate_up, expert_ids, slot_ids, capacity):
    seq_count = partial_value.shape[0]
    model_width = moe_gain.shape[0]
    per_block = expert_ids.shape[1]
    pick_count = expert_ids.shape[2]
    row_count = seq_count * per_block
    ctx_count = lax.axis_size("ctx")
    group_count = lax.axis_size("expert")
    grouped = partial_value.reshape(
        seq_count, ctx_count, group_count, per_block, partial_value.shape[2]
    )
    reduced = lax.psum_scatter(grouped, "expert", scatter_dimension=2, tiled=True).astype(
        jnp.bfloat16
    )
    swapped = lax.all_to_all(reduced, "ctx", split_axis=1, concat_axis=4, tiled=True)
    mamba_out = swapped.reshape(seq_count, per_block, model_width)
    flat = mamba_out.reshape(row_count, model_width).astype(jnp.float32)
    scale = lax.rsqrt(jnp.mean(flat * flat, axis=1, keepdims=True) + 1e-05)
    normed = (flat * scale * moe_gain[None, :]).astype(jnp.bfloat16)
    chosen = expert_ids.reshape(row_count, pick_count)
    placed = slot_ids.reshape(row_count, pick_count)
    match_expert = chosen[:, :, None, None] == jnp.arange(group_count)[None, None, :, None]
    match_slot = placed[:, :, None, None] == jnp.arange(capacity)[None, None, None, :]
    selector = (match_expert & match_slot).astype(jnp.bfloat16)
    outgoing = jnp.einsum(
        "rkec,rd->ecd", selector, normed, preferred_element_type=jnp.float32
    ).astype(jnp.bfloat16)
    arrived = lax.all_to_all(outgoing, "expert", split_axis=0, concat_axis=0, tiled=True)
    piece = lax.all_gather(arrived[None], ("dp", "ctx"), axis=0, tiled=True)
    slot_rows = piece.reshape(-1, piece.shape[3])
    return (mamba_out, expert_ffn(gate_up, slot_rows)[None])


def local(
    x_in, z_in, b_in, c_in, decay_log, skip, out_weight, moe_gain, gate_up, expert_ids, slot_ids
):
    seq_count, block_len, width_in = x_in.shape
    state_size = b_in.shape[2]
    model_width = moe_gain.shape[0]
    col_width = out_weight.shape[1]
    per_block = expert_ids.shape[1]
    pick_count = expert_ids.shape[2]
    dp_count = lax.axis_size("dp")
    ctx_count = lax.axis_size("ctx")
    group_count = lax.axis_size("expert")
    device_count = dp_count * ctx_count * group_count
    row_count = seq_count * per_block
    capacity = max(2, 4 * row_count // group_count)

    head_count = decay_log.shape[2]
    packed = jnp.concatenate([x_in, z_in, b_in, c_in] + split_exact(decay_log), axis=2)
    packed = jnp.moveaxis(gather_blocks(packed, "ctx", ctx_count), 0, 1).reshape(
        seq_count, ctx_count * block_len, packed.shape[2]
    )
    decay_base = 2 * width_in + 2 * state_size
    decay_all = join_exact(
        [packed[:, :, decay_base + i * head_count : decay_base + (i + 1) * head_count] for i in range(3)]
    )

    x_all = packed[:, :, :width_in]
    z_all = packed[:, :, width_in : 2 * width_in]
    b_all = packed[:, :, 2 * width_in : 2 * width_in + state_size]
    c_all = packed[:, :, 2 * width_in + state_size : decay_base]
    ssd = mixer(x_all, b_all, c_all, decay_all, skip)
    gated = (ssd * jax.nn.silu(z_all.astype(jnp.float32))).astype(jnp.bfloat16)
    partial_value = jnp.einsum(
        "stk,kd->std", gated, out_weight, preferred_element_type=jnp.float32
    )
    if device_count * row_count * model_width * 2 > (8 << 20):
        return dispatch_routed(partial_value, moe_gain, gate_up, expert_ids, slot_ids, capacity)
    total_len = partial_value.shape[1]
    route = jnp.stack([expert_ids, slot_ids], axis=-1).astype(jnp.float32).reshape(-1)
    route_len = route.shape[0]
    extra_rows = -(-(group_count * route_len) // col_width)
    route_row = jnp.zeros((extra_rows * col_width,), jnp.float32)
    route_row = lax.dynamic_update_slice(route_row, route, (lax.axis_index("expert") * route_len,))
    extended = jnp.concatenate(
        [partial_value.reshape(seq_count * total_len, col_width), route_row.reshape(extra_rows, col_width)],
        axis=0,
    )
    summed = sum_over(extended, "expert", group_count)
    gathered = gather_blocks(gather_blocks(summed, "ctx", ctx_count), "dp", dp_count)
    gathered = gathered.reshape(dp_count, ctx_count, seq_count * total_len + extra_rows, col_width)
    routes = gathered[:, :, seq_count * total_len :, :].reshape(dp_count, ctx_count, -1)
    routes = routes[:, :, : group_count * route_len].astype(jnp.int32)
    routes = routes.reshape(dp_count, ctx_count, group_count, seq_count, per_block, pick_count, 2)
    routes = jnp.transpose(routes, (0, 3, 1, 2, 4, 5, 6))
    row_total = seq_count * total_len
    tokens = gathered[:, :, :row_total, :]
    mine_rows = lax.dynamic_index_in_dim(tokens, lax.axis_index("dp"), axis=0, keepdims=False)
    mine_rows = mine_rows.reshape(ctx_count, seq_count, ctx_count * group_count, per_block, col_width)
    mine_block = lax.axis_index("ctx") * group_count + lax.axis_index("expert")
    mine_rows = lax.dynamic_index_in_dim(mine_rows, mine_block, axis=2, keepdims=False)
    mamba_out = jnp.transpose(mine_rows, (1, 2, 0, 3)).reshape(seq_count, per_block, model_width)
    token_count = dp_count * row_total
    flat = tokens.astype(jnp.float32)
    square_sum = jnp.sum(flat * flat, axis=(1, 3), keepdims=True)
    scale = lax.rsqrt(square_sum / model_width + 1e-05)
    gain = moe_gain.reshape(1, ctx_count, 1, col_width)
    normed = (flat * scale * gain).astype(jnp.bfloat16)

    group = (
        (jnp.arange(dp_count)[:, None, None, None, None] * ctx_count
         + jnp.arange(ctx_count)[None, None, :, None, None]) * group_count
        + jnp.arange(group_count)[None, None, None, :, None]
    )
    group = jnp.broadcast_to(group, (dp_count, seq_count, ctx_count, group_count, per_block))
    target = group.reshape(token_count, 1) * capacity + routes[..., 1].reshape(token_count, pick_count)
    mine = routes[..., 0].reshape(token_count, pick_count) == lax.axis_index("expert")
    slot_count = device_count * capacity
    hit = mine[..., None] & (target[..., None] == jnp.arange(slot_count))
    selector = jnp.any(hit, axis=1).reshape(dp_count, row_total, slot_count)
    dispatched = jnp.einsum(
        "drq,dcrk->qck", selector.astype(jnp.bfloat16), normed, preferred_element_type=jnp.float32
    ).astype(jnp.bfloat16)
    hidden = expert_ffn(gate_up, dispatched.reshape(slot_count, model_width))
    return (mamba_out, hidden[None])


def solution(mesh):
    in_specs = (
        P("dp", "ctx", "expert"),
        P("dp", "ctx", "expert"),
        P("dp", "ctx", None),
        P("dp", "ctx", None),
        P("dp", "ctx", "expert"),
        P("expert"),
        P("expert", "ctx"),
        P(),
        P("expert", None, ("dp", "ctx"), None),
        P("dp", ("ctx", "expert"), None),
        P("dp", ("ctx", "expert"), None),
    )
    out_specs = (P("dp", ("ctx", "expert"), None), P("expert", ("dp", "ctx"), None))
    return jax.shard_map(local, mesh=mesh, in_specs=in_specs, out_specs=out_specs, check_vma=False)
```

```python
import jax
import jax.numpy as jnp
from jax import lax
from jax.sharding import PartitionSpec as P

P_SIZE = 64
ALL_AXES = ("dp", "ctx", "expert")


def place(received, sources, count):
    out = jnp.zeros((count,) + received[0].shape, received[0].dtype)
    for block, source in zip(received, sources):
        out = lax.dynamic_update_index_in_dim(out, block, source, axis=0)
    return out


def gather_blocks(value, axis_name, count):
    me = lax.axis_index(axis_name)
    received = [value]
    sources = [me]
    for shift in range(1, count):
        perm = [(i, (i + shift) % count) for i in range(count)]
        received.append(lax.ppermute(value, axis_name, perm))
        sources.append((me - shift) % count)
    return place(received, sources, count)


def gather_xor(value, axis_name, count):
    me = lax.axis_index(axis_name)
    received = [value]
    sources = [me]
    for shift in range(1, count):
        perm = [(i, i ^ shift) for i in range(count)]
        received.append(lax.ppermute(value, axis_name, perm))
        sources.append(me ^ shift)
    return place(received, sources, count)


def sum_scatter(value, axis_name, count):
    me = lax.axis_index(axis_name)
    pieces = value.reshape(value.shape[:-1] + (count, value.shape[-1] // count))
    total = lax.dynamic_index_in_dim(pieces, me, axis=-2, keepdims=False)
    for shift in range(1, count):
        perm = [(i, i ^ shift) for i in range(count)]
        send = lax.dynamic_index_in_dim(pieces, me ^ shift, axis=-2, keepdims=False)
        total = total + lax.ppermute(send, axis_name, perm)
    return total.astype(jnp.bfloat16)


def split_exact(value):
    high = value.astype(jnp.bfloat16)
    rest = value - lax.optimization_barrier(high).astype(jnp.float32)
    middle = rest.astype(jnp.bfloat16)
    low = (rest - lax.optimization_barrier(middle).astype(jnp.float32)).astype(jnp.bfloat16)
    return [high, middle, low]


def join_exact(parts):
    high, middle, low = (part.astype(jnp.float32) for part in parts)
    return (high + middle) + low


def mixer(x_in, b_in, c_in, decay_log, skip):
    highest = lax.Precision.HIGHEST
    seq_count, total_len, width_in = x_in.shape
    head_count = skip.shape[0]
    state_size = b_in.shape[2]
    chunk = total_len if total_len <= 128 else 64
    chunks = total_len // chunk
    x_float = x_in.astype(jnp.float32).reshape(seq_count, chunks, chunk, head_count, P_SIZE)
    b_float = b_in.astype(jnp.float32).reshape(seq_count, chunks, chunk, state_size)
    c_float = c_in.astype(jnp.float32).reshape(seq_count, chunks, chunk, state_size)
    cum_decay = jnp.cumsum(decay_log.reshape(seq_count, chunks, chunk, head_count), axis=2)
    scores = jnp.einsum("sktn,skun->sktu", c_float, b_float, precision=highest)
    causal = (jnp.arange(chunk)[:, None] >= jnp.arange(chunk)[None, :])[None, None, :, :, None]
    spans = cum_decay[:, :, :, None, :] - cum_decay[:, :, None, :, :]
    kernel = jnp.where(causal, jnp.exp(jnp.where(causal, spans, 0.0)), 0.0) * scores[..., None]
    ssd = jnp.einsum("sktuh,skuhp->skthp", kernel, x_float, precision=highest)
    if chunks > 1:
        final_decay = cum_decay[:, :, -1, :]
        tails = jnp.exp(final_decay[:, :, None, :] - cum_decay)
        states = jnp.einsum("skuh,skuhp,skun->skhpn", tails, x_float, b_float, precision=highest)

        def step(carry, inputs):
            decay_k, state_k = inputs
            return decay_k[:, :, None, None] * carry + state_k, carry

        _, incoming = lax.scan(
            step,
            jnp.zeros_like(states[:, 0]),
            (jnp.moveaxis(jnp.exp(final_decay), 1, 0), jnp.moveaxis(states, 1, 0)),
        )
        incoming = jnp.moveaxis(incoming, 0, 1)
        ssd = ssd + jnp.exp(cum_decay)[..., None] * jnp.einsum(
            "sktn,skhpn->skthp", c_float, incoming, precision=highest
        )
    ssd = ssd + skip[None, None, None, :, None] * x_float
    return ssd.reshape(seq_count, total_len, width_in)


def expert_ffn(gate_up, slot_rows):
    both = jnp.einsum("gfd,qd->gfq", gate_up[0], slot_rows, preferred_element_type=jnp.float32)
    return (jax.nn.silu(both[0]) * both[1]).astype(jnp.bfloat16)


def dispatch_routed(partial_value, moe_gain, gate_up, expert_ids, slot_ids, capacity):
    seq_count = partial_value.shape[0]
    model_width = moe_gain.shape[0]
    per_block = expert_ids.shape[1]
    pick_count = expert_ids.shape[2]
    row_count = seq_count * per_block
    ctx_count = lax.axis_size("ctx")
    group_count = lax.axis_size("expert")
    grouped = partial_value.reshape(
        seq_count, ctx_count, group_count, per_block, partial_value.shape[2]
    )
    reduced = lax.psum_scatter(grouped, "expert", scatter_dimension=2, tiled=True).astype(
        jnp.bfloat16
    )
    swapped = lax.all_to_all(reduced, "ctx", split_axis=1, concat_axis=4, tiled=True)
    mamba_out = swapped.reshape(seq_count, per_block, model_width)
    flat = mamba_out.reshape(row_count, model_width).astype(jnp.float32)
    scale = lax.rsqrt(jnp.mean(flat * flat, axis=1, keepdims=True) + 1e-05)
    normed = (flat * scale * moe_gain[None, :]).astype(jnp.bfloat16)
    chosen = expert_ids.reshape(row_count, pick_count)
    placed = slot_ids.reshape(row_count, pick_count)
    match_expert = chosen[:, :, None, None] == jnp.arange(group_count)[None, None, :, None]
    match_slot = placed[:, :, None, None] == jnp.arange(capacity)[None, None, None, :]
    selector = (match_expert & match_slot).astype(jnp.bfloat16)
    outgoing = jnp.einsum(
        "rkec,rd->ecd", selector, normed, preferred_element_type=jnp.float32
    ).astype(jnp.bfloat16)
    arrived = lax.all_to_all(outgoing, "expert", split_axis=0, concat_axis=0, tiled=True)
    piece = lax.all_gather(arrived[None], ("dp", "ctx"), axis=0, tiled=True)
    slot_rows = piece.reshape(-1, piece.shape[3])
    return (mamba_out, expert_ffn(gate_up, slot_rows)[None])


def local(
    x_in, z_in, b_in, c_in, decay_log, skip, out_weight, moe_gain, gate_up, expert_ids, slot_ids
):
    seq_count, block_len, width_in = x_in.shape
    state_size = b_in.shape[2]
    model_width = moe_gain.shape[0]
    col_width = out_weight.shape[1]
    per_block = expert_ids.shape[1]
    pick_count = expert_ids.shape[2]
    dp_count = lax.axis_size("dp")
    ctx_count = lax.axis_size("ctx")
    group_count = lax.axis_size("expert")
    device_count = dp_count * ctx_count * group_count
    row_count = seq_count * per_block
    capacity = max(2, 4 * row_count // group_count)

    head_count = decay_log.shape[2]
    packed = jnp.concatenate([x_in, z_in, b_in, c_in] + split_exact(decay_log), axis=2)
    packed = jnp.moveaxis(gather_blocks(packed, "ctx", ctx_count), 0, 1).reshape(
        seq_count, ctx_count * block_len, packed.shape[2]
    )
    decay_base = 2 * width_in + 2 * state_size
    decay_all = join_exact(
        [packed[:, :, decay_base + i * head_count : decay_base + (i + 1) * head_count] for i in range(3)]
    )

    x_all = packed[:, :, :width_in]
    z_all = packed[:, :, width_in : 2 * width_in]
    b_all = packed[:, :, 2 * width_in : 2 * width_in + state_size]
    c_all = packed[:, :, 2 * width_in + state_size : decay_base]
    ssd = mixer(x_all, b_all, c_all, decay_all, skip)
    gated = (ssd * jax.nn.silu(z_all.astype(jnp.float32))).astype(jnp.bfloat16)
    partial_value = jnp.einsum(
        "stk,kd->std", gated, out_weight, preferred_element_type=jnp.float32
    )
    if device_count * row_count * model_width * 2 > (8 << 20):
        return dispatch_routed(partial_value, moe_gain, gate_up, expert_ids, slot_ids, capacity)
    total_len = partial_value.shape[1]
    route = jnp.stack([expert_ids, slot_ids], axis=-1).astype(jnp.float32).reshape(-1)
    route_len = route.shape[0]
    extra_rows = -(-(group_count * route_len) // col_width)
    route_row = jnp.zeros((extra_rows * col_width,), jnp.float32)
    route_row = lax.dynamic_update_slice(route_row, route, (lax.axis_index("expert") * route_len,))
    extended = jnp.concatenate(
        [partial_value.reshape(seq_count * total_len, col_width), route_row.reshape(extra_rows, col_width)],
        axis=0,
    )
    piece_width = col_width // group_count
    piece = sum_scatter(extended, "expert", group_count)
    gathered = gather_blocks(piece, "ctx", ctx_count)
    gathered = gather_xor(gathered, "expert", group_count)
    gathered = gather_blocks(gathered, "dp", dp_count)
    row_total = seq_count * total_len
    extra = jnp.transpose(gathered[:, :, :, row_total:, :], (0, 2, 3, 1, 4))
    routes = extra.reshape(dp_count, ctx_count, -1)[:, :, : group_count * route_len]
    routes = routes.astype(jnp.int32)
    routes = routes.reshape(dp_count, ctx_count, group_count, seq_count, per_block, pick_count, 2)
    routes = jnp.transpose(routes, (0, 3, 1, 2, 4, 5, 6))
    tokens = gathered[:, :, :, :row_total, :]
    mine_rows = lax.dynamic_index_in_dim(tokens, lax.axis_index("dp"), axis=0, keepdims=False)
    mine_rows = mine_rows.reshape(
        group_count, ctx_count, seq_count, ctx_count * group_count, per_block, piece_width
    )
    mine_block = lax.axis_index("ctx") * group_count + lax.axis_index("expert")
    mine_rows = lax.dynamic_index_in_dim(mine_rows, mine_block, axis=3, keepdims=False)
    mamba_out = jnp.transpose(mine_rows, (2, 3, 1, 0, 4)).reshape(seq_count, per_block, model_width)
    token_count = dp_count * row_total
    flat = tokens.astype(jnp.float32)
    square_sum = jnp.sum(flat * flat, axis=(1, 2, 4), keepdims=True)
    scale = lax.rsqrt(square_sum / model_width + 1e-05)
    gain = jnp.transpose(moe_gain.reshape(ctx_count, group_count, piece_width), (1, 0, 2))
    normed = (flat * scale * gain[None, :, :, None, :]).astype(jnp.bfloat16)

    group = (
        (jnp.arange(dp_count)[:, None, None, None, None] * ctx_count
         + jnp.arange(ctx_count)[None, None, :, None, None]) * group_count
        + jnp.arange(group_count)[None, None, None, :, None]
    )
    group = jnp.broadcast_to(group, (dp_count, seq_count, ctx_count, group_count, per_block))
    target = group.reshape(token_count, 1) * capacity + routes[..., 1].reshape(token_count, pick_count)
    mine = routes[..., 0].reshape(token_count, pick_count) == lax.axis_index("expert")
    slot_count = device_count * capacity
    hit = mine[..., None] & (target[..., None] == jnp.arange(slot_count))
    selector = jnp.any(hit, axis=1).reshape(dp_count, row_total, slot_count)
    dispatched = jnp.einsum(
        "drq,decrk->qcek", selector.astype(jnp.bfloat16), normed, preferred_element_type=jnp.float32
    ).astype(jnp.bfloat16)
    hidden = expert_ffn(gate_up, dispatched.reshape(slot_count, model_width))
    return (mamba_out, hidden[None])


def solution(mesh):
    in_specs = (
        P("dp", "ctx", "expert"),
        P("dp", "ctx", "expert"),
        P("dp", "ctx", None),
        P("dp", "ctx", None),
        P("dp", "ctx", "expert"),
        P("expert"),
        P("expert", "ctx"),
        P(),
        P("expert", None, ("dp", "ctx"), None),
        P("dp", ("ctx", "expert"), None),
        P("dp", ("ctx", "expert"), None),
    )
    out_specs = (P("dp", ("ctx", "expert"), None), P("expert", ("dp", "ctx"), None))
    return jax.shard_map(local, mesh=mesh, in_specs=in_specs, out_specs=out_specs, check_vma=False)
```

```python
import jax
import jax.numpy as jnp
from jax import lax
from jax.sharding import PartitionSpec as P

P_SIZE = 64
ALL_AXES = ("dp", "ctx", "expert")


def place(received, sources, count):
    slots = []
    for slot in range(count):
        block = received[0]
        for other, source in zip(received[1:], sources[1:]):
            block = jnp.where(source == slot, other, block)
        slots.append(block)
    return jnp.stack(slots)


def gather_blocks(value, axis_name, count):
    me = lax.axis_index(axis_name)
    received = [value]
    sources = [me]
    for shift in range(1, count):
        perm = [(i, (i + shift) % count) for i in range(count)]
        received.append(lax.ppermute(value, axis_name, perm))
        sources.append((me - shift) % count)
    return place(received, sources, count)


def gather_xor(value, axis_name, count):
    me = lax.axis_index(axis_name)
    received = [value]
    sources = [me]
    for shift in range(1, count):
        perm = [(i, i ^ shift) for i in range(count)]
        received.append(lax.ppermute(value, axis_name, perm))
        sources.append(me ^ shift)
    return place(received, sources, count)


def sum_scatter(value, axis_name, count):
    me = lax.axis_index(axis_name)
    pieces = value.reshape(value.shape[:-1] + (count, value.shape[-1] // count))
    total = lax.dynamic_index_in_dim(pieces, me, axis=-2, keepdims=False)
    for shift in range(1, count):
        perm = [(i, i ^ shift) for i in range(count)]
        send = lax.dynamic_index_in_dim(pieces, me ^ shift, axis=-2, keepdims=False)
        total = total + lax.ppermute(send, axis_name, perm)
    return total.astype(jnp.bfloat16)


def split_exact(value):
    high = value.astype(jnp.bfloat16)
    rest = value - lax.optimization_barrier(high).astype(jnp.float32)
    middle = rest.astype(jnp.bfloat16)
    low = (rest - lax.optimization_barrier(middle).astype(jnp.float32)).astype(jnp.bfloat16)
    return [high, middle, low]


def join_exact(parts):
    high, middle, low = (part.astype(jnp.float32) for part in parts)
    return (high + middle) + low


def mixer(x_in, b_in, c_in, decay_log, skip):
    highest = lax.Precision.HIGHEST
    seq_count, total_len, width_in = x_in.shape
    head_count = skip.shape[0]
    state_size = b_in.shape[2]
    chunk = total_len if total_len <= 128 else 64
    chunks = total_len // chunk
    x_float = x_in.astype(jnp.float32).reshape(seq_count, chunks, chunk, head_count, P_SIZE)
    b_float = b_in.astype(jnp.float32).reshape(seq_count, chunks, chunk, state_size)
    c_float = c_in.astype(jnp.float32).reshape(seq_count, chunks, chunk, state_size)
    cum_decay = jnp.cumsum(decay_log.reshape(seq_count, chunks, chunk, head_count), axis=2)
    scores = jnp.einsum("sktn,skun->sktu", c_float, b_float, precision=highest)
    causal = (jnp.arange(chunk)[:, None] >= jnp.arange(chunk)[None, :])[None, None, :, :, None]
    spans = cum_decay[:, :, :, None, :] - cum_decay[:, :, None, :, :]
    kernel = jnp.where(causal, jnp.exp(jnp.where(causal, spans, 0.0)), 0.0) * scores[..., None]
    ssd = jnp.einsum("sktuh,skuhp->skthp", kernel, x_float, precision=highest)
    if chunks > 1:
        final_decay = cum_decay[:, :, -1, :]
        tails = jnp.exp(final_decay[:, :, None, :] - cum_decay)
        states = jnp.einsum("skuh,skuhp,skun->skhpn", tails, x_float, b_float, precision=highest)

        def step(carry, inputs):
            decay_k, state_k = inputs
            return decay_k[:, :, None, None] * carry + state_k, carry

        _, incoming = lax.scan(
            step,
            jnp.zeros_like(states[:, 0]),
            (jnp.moveaxis(jnp.exp(final_decay), 1, 0), jnp.moveaxis(states, 1, 0)),
        )
        incoming = jnp.moveaxis(incoming, 0, 1)
        ssd = ssd + jnp.exp(cum_decay)[..., None] * jnp.einsum(
            "sktn,skhpn->skthp", c_float, incoming, precision=highest
        )
    ssd = ssd + skip[None, None, None, :, None] * x_float
    return ssd.reshape(seq_count, total_len, width_in)


def expert_ffn(gate_up, slot_rows):
    both = jnp.einsum("gfd,qd->gfq", gate_up[0], slot_rows, preferred_element_type=jnp.float32)
    return (jax.nn.silu(both[0]) * both[1]).astype(jnp.bfloat16)


def dispatch_routed(partial_value, moe_gain, gate_up, expert_ids, slot_ids, capacity):
    seq_count = partial_value.shape[0]
    model_width = moe_gain.shape[0]
    per_block = expert_ids.shape[1]
    pick_count = expert_ids.shape[2]
    row_count = seq_count * per_block
    ctx_count = lax.axis_size("ctx")
    group_count = lax.axis_size("expert")
    grouped = partial_value.reshape(
        seq_count, ctx_count, group_count, per_block, partial_value.shape[2]
    )
    reduced = lax.psum_scatter(grouped, "expert", scatter_dimension=2, tiled=True).astype(
        jnp.bfloat16
    )
    swapped = lax.all_to_all(reduced, "ctx", split_axis=1, concat_axis=4, tiled=True)
    mamba_out = swapped.reshape(seq_count, per_block, model_width)
    flat = mamba_out.reshape(row_count, model_width).astype(jnp.float32)
    scale = lax.rsqrt(jnp.mean(flat * flat, axis=1, keepdims=True) + 1e-05)
    normed = (flat * scale * moe_gain[None, :]).astype(jnp.bfloat16)
    chosen = expert_ids.reshape(row_count, pick_count)
    placed = slot_ids.reshape(row_count, pick_count)
    match_expert = chosen[:, :, None, None] == jnp.arange(group_count)[None, None, :, None]
    match_slot = placed[:, :, None, None] == jnp.arange(capacity)[None, None, None, :]
    selector = (match_expert & match_slot).astype(jnp.bfloat16)
    outgoing = jnp.einsum(
        "rkec,rd->ecd", selector, normed, preferred_element_type=jnp.float32
    ).astype(jnp.bfloat16)
    arrived = lax.all_to_all(outgoing, "expert", split_axis=0, concat_axis=0, tiled=True)
    piece = lax.all_gather(arrived[None], ("dp", "ctx"), axis=0, tiled=True)
    slot_rows = piece.reshape(-1, piece.shape[3])
    return (mamba_out, expert_ffn(gate_up, slot_rows)[None])


def local(
    x_in, z_in, b_in, c_in, decay_log, skip, out_weight, moe_gain, gate_up, expert_ids, slot_ids
):
    seq_count, block_len, width_in = x_in.shape
    state_size = b_in.shape[2]
    model_width = moe_gain.shape[0]
    col_width = out_weight.shape[1]
    per_block = expert_ids.shape[1]
    pick_count = expert_ids.shape[2]
    dp_count = lax.axis_size("dp")
    ctx_count = lax.axis_size("ctx")
    group_count = lax.axis_size("expert")
    device_count = dp_count * ctx_count * group_count
    row_count = seq_count * per_block
    capacity = max(2, 4 * row_count // group_count)

    head_count = decay_log.shape[2]
    packed = jnp.concatenate([x_in, z_in, b_in, c_in] + split_exact(decay_log), axis=2)
    packed = jnp.moveaxis(gather_blocks(packed, "ctx", ctx_count), 0, 1).reshape(
        seq_count, ctx_count * block_len, packed.shape[2]
    )
    decay_base = 2 * width_in + 2 * state_size
    decay_all = join_exact(
        [packed[:, :, decay_base + i * head_count : decay_base + (i + 1) * head_count] for i in range(3)]
    )

    x_all = packed[:, :, :width_in]
    z_all = packed[:, :, width_in : 2 * width_in]
    b_all = packed[:, :, 2 * width_in : 2 * width_in + state_size]
    c_all = packed[:, :, 2 * width_in + state_size : decay_base]
    ssd = mixer(x_all, b_all, c_all, decay_all, skip)
    gated = (ssd * jax.nn.silu(z_all.astype(jnp.float32))).astype(jnp.bfloat16)
    partial_value = jnp.einsum(
        "stk,kd->std", gated, out_weight, preferred_element_type=jnp.float32
    )
    if device_count * row_count * model_width * 2 > (8 << 20):
        return dispatch_routed(partial_value, moe_gain, gate_up, expert_ids, slot_ids, capacity)
    total_len = partial_value.shape[1]
    route = jnp.stack([expert_ids, slot_ids], axis=-1).astype(jnp.float32).reshape(-1)
    route_len = route.shape[0]
    extra_rows = -(-(group_count * route_len) // col_width)
    route_row = jnp.zeros((extra_rows * col_width,), jnp.float32)
    route_row = lax.dynamic_update_slice(route_row, route, (lax.axis_index("expert") * route_len,))
    extended = jnp.concatenate(
        [partial_value.reshape(seq_count * total_len, col_width), route_row.reshape(extra_rows, col_width)],
        axis=0,
    )
    piece_width = col_width // group_count
    piece = sum_scatter(extended, "expert", group_count)
    gathered = gather_blocks(piece, "ctx", ctx_count)
    gathered = gather_xor(gathered, "expert", group_count)
    gathered = gather_blocks(gathered, "dp", dp_count)
    row_total = seq_count * total_len
    extra = jnp.transpose(gathered[:, :, :, row_total:, :], (0, 2, 3, 1, 4))
    routes = extra.reshape(dp_count, ctx_count, -1)[:, :, : group_count * route_len]
    routes = routes.astype(jnp.int32)
    routes = routes.reshape(dp_count, ctx_count, group_count, seq_count, per_block, pick_count, 2)
    routes = jnp.transpose(routes, (0, 3, 1, 2, 4, 5, 6))
    tokens = gathered[:, :, :, :row_total, :]
    mine_rows = lax.dynamic_index_in_dim(tokens, lax.axis_index("dp"), axis=0, keepdims=False)
    mine_rows = mine_rows.reshape(
        group_count, ctx_count, seq_count, ctx_count * group_count, per_block, piece_width
    )
    mine_block = lax.axis_index("ctx") * group_count + lax.axis_index("expert")
    mine_rows = lax.dynamic_index_in_dim(mine_rows, mine_block, axis=3, keepdims=False)
    mamba_out = jnp.transpose(mine_rows, (2, 3, 1, 0, 4)).reshape(seq_count, per_block, model_width)
    token_count = dp_count * row_total
    flat = tokens.astype(jnp.float32)
    square_sum = jnp.sum(flat * flat, axis=(1, 2, 4), keepdims=True)
    scale = lax.rsqrt(square_sum / model_width + 1e-05)
    gain = jnp.transpose(moe_gain.reshape(ctx_count, group_count, piece_width), (1, 0, 2))
    normed = (flat * scale * gain[None, :, :, None, :]).astype(jnp.bfloat16)

    group = (
        (jnp.arange(dp_count)[:, None, None, None, None] * ctx_count
         + jnp.arange(ctx_count)[None, None, :, None, None]) * group_count
        + jnp.arange(group_count)[None, None, None, :, None]
    )
    group = jnp.broadcast_to(group, (dp_count, seq_count, ctx_count, group_count, per_block))
    target = group.reshape(token_count, 1) * capacity + routes[..., 1].reshape(token_count, pick_count)
    mine = routes[..., 0].reshape(token_count, pick_count) == lax.axis_index("expert")
    slot_count = device_count * capacity
    hit = mine[..., None] & (target[..., None] == jnp.arange(slot_count))
    selector = jnp.any(hit, axis=1).reshape(dp_count, row_total, slot_count)
    dispatched = jnp.einsum(
        "drq,decrk->qcek", selector.astype(jnp.bfloat16), normed, preferred_element_type=jnp.float32
    ).astype(jnp.bfloat16)
    hidden = expert_ffn(gate_up, dispatched.reshape(slot_count, model_width))
    return (mamba_out, hidden[None])


def solution(mesh):
    in_specs = (
        P("dp", "ctx", "expert"),
        P("dp", "ctx", "expert"),
        P("dp", "ctx", None),
        P("dp", "ctx", None),
        P("dp", "ctx", "expert"),
        P("expert"),
        P("expert", "ctx"),
        P(),
        P("expert", None, ("dp", "ctx"), None),
        P("dp", ("ctx", "expert"), None),
        P("dp", ("ctx", "expert"), None),
    )
    out_specs = (P("dp", ("ctx", "expert"), None), P("expert", ("dp", "ctx"), None))
    return jax.shard_map(local, mesh=mesh, in_specs=in_specs, out_specs=out_specs, check_vma=False)
```

```python
import jax
import jax.numpy as jnp
from jax import lax
from jax.sharding import PartitionSpec as P

P_SIZE = 64
ALL_AXES = ("dp", "ctx", "expert")


def place(received, sources, count):
    slots = []
    for slot in range(count):
        block = received[0]
        for other, source in zip(received[1:], sources[1:]):
            block = jnp.where(source == slot, other, block)
        slots.append(block)
    return jnp.stack(slots)


def gather_blocks(value, axis_name, count):
    me = lax.axis_index(axis_name)
    received = [value]
    sources = [me]
    for shift in range(1, count):
        perm = [(i, (i + shift) % count) for i in range(count)]
        received.append(lax.ppermute(value, axis_name, perm))
        sources.append((me - shift) % count)
    return place(received, sources, count)


def gather_xor(value, axis_name, count):
    me = lax.axis_index(axis_name)
    received = [value]
    sources = [me]
    for shift in range(1, count):
        perm = [(i, i ^ shift) for i in range(count)]
        received.append(lax.ppermute(value, axis_name, perm))
        sources.append(me ^ shift)
    return place(received, sources, count)


def sum_scatter(value, axis_name, count):
    me = lax.axis_index(axis_name)
    pieces = value.reshape(value.shape[:-1] + (count, value.shape[-1] // count))
    total = lax.dynamic_index_in_dim(pieces, me, axis=-2, keepdims=False)
    for shift in range(1, count):
        perm = [(i, i ^ shift) for i in range(count)]
        send = lax.dynamic_index_in_dim(pieces, me ^ shift, axis=-2, keepdims=False)
        total = total + lax.ppermute(send, axis_name, perm)
    return total.astype(jnp.bfloat16)


def split_exact(value):
    high = value.astype(jnp.bfloat16)
    rest = value - lax.optimization_barrier(high).astype(jnp.float32)
    middle = rest.astype(jnp.bfloat16)
    low = (rest - lax.optimization_barrier(middle).astype(jnp.float32)).astype(jnp.bfloat16)
    return [high, middle, low]


def join_exact(parts):
    high, middle, low = (part.astype(jnp.float32) for part in parts)
    return (high + middle) + low


def mixer(x_in, b_in, c_in, decay_log, skip):
    highest = lax.Precision.HIGHEST
    seq_count, total_len, width_in = x_in.shape
    head_count = skip.shape[0]
    state_size = b_in.shape[2]
    chunk = total_len if total_len <= 128 else 64
    chunks = total_len // chunk
    x_float = x_in.astype(jnp.float32).reshape(seq_count, chunks, chunk, head_count, P_SIZE)
    b_float = b_in.astype(jnp.float32).reshape(seq_count, chunks, chunk, state_size)
    c_float = c_in.astype(jnp.float32).reshape(seq_count, chunks, chunk, state_size)
    cum_decay = jnp.cumsum(decay_log.reshape(seq_count, chunks, chunk, head_count), axis=2)
    scores = jnp.einsum("sktn,skun->sktu", c_float, b_float, precision=highest)
    causal = (jnp.arange(chunk)[:, None] >= jnp.arange(chunk)[None, :])[None, None, :, :, None]
    spans = cum_decay[:, :, :, None, :] - cum_decay[:, :, None, :, :]
    kernel = jnp.where(causal, jnp.exp(jnp.where(causal, spans, 0.0)), 0.0) * scores[..., None]
    ssd = jnp.einsum("sktuh,skuhp->skthp", kernel, x_float, precision=highest)
    if chunks > 1:
        final_decay = cum_decay[:, :, -1, :]
        tails = jnp.exp(final_decay[:, :, None, :] - cum_decay)
        states = jnp.einsum("skuh,skuhp,skun->skhpn", tails, x_float, b_float, precision=highest)

        def step(carry, inputs):
            decay_k, state_k = inputs
            return decay_k[:, :, None, None] * carry + state_k, carry

        _, incoming = lax.scan(
            step,
            jnp.zeros_like(states[:, 0]),
            (jnp.moveaxis(jnp.exp(final_decay), 1, 0), jnp.moveaxis(states, 1, 0)),
        )
        incoming = jnp.moveaxis(incoming, 0, 1)
        ssd = ssd + jnp.exp(cum_decay)[..., None] * jnp.einsum(
            "sktn,skhpn->skthp", c_float, incoming, precision=highest
        )
    ssd = ssd + skip[None, None, None, :, None] * x_float
    return ssd.reshape(seq_count, total_len, width_in)


def expert_ffn(gate_up, slot_rows):
    both = jnp.einsum("gfd,qd->gfq", gate_up[0], slot_rows, preferred_element_type=jnp.float32)
    return (jax.nn.silu(both[0]) * both[1]).astype(jnp.bfloat16)


def dispatch_routed(partial_value, moe_gain, gate_up, expert_ids, slot_ids, capacity):
    seq_count = partial_value.shape[0]
    model_width = moe_gain.shape[0]
    per_block = expert_ids.shape[1]
    pick_count = expert_ids.shape[2]
    row_count = seq_count * per_block
    ctx_count = lax.axis_size("ctx")
    group_count = lax.axis_size("expert")
    grouped = partial_value.reshape(
        seq_count, ctx_count, group_count, per_block, partial_value.shape[2]
    )
    reduced = lax.psum_scatter(grouped, "expert", scatter_dimension=2, tiled=True).astype(
        jnp.bfloat16
    )
    swapped = lax.all_to_all(reduced, "ctx", split_axis=1, concat_axis=4, tiled=True)
    mamba_out = swapped.reshape(seq_count, per_block, model_width)
    flat = mamba_out.reshape(row_count, model_width).astype(jnp.float32)
    scale = lax.rsqrt(jnp.mean(flat * flat, axis=1, keepdims=True) + 1e-05)
    normed = (flat * scale * moe_gain[None, :]).astype(jnp.bfloat16)
    chosen = expert_ids.reshape(row_count, pick_count)
    placed = slot_ids.reshape(row_count, pick_count)
    match_expert = chosen[:, :, None, None] == jnp.arange(group_count)[None, None, :, None]
    match_slot = placed[:, :, None, None] == jnp.arange(capacity)[None, None, None, :]
    selector = (match_expert & match_slot).astype(jnp.bfloat16)
    outgoing = jnp.einsum(
        "rkec,rd->ecd", selector, normed, preferred_element_type=jnp.float32
    ).astype(jnp.bfloat16)
    arrived = lax.all_to_all(outgoing, "expert", split_axis=0, concat_axis=0, tiled=True)
    piece = lax.all_gather(arrived[None], ("dp", "ctx"), axis=0, tiled=True)
    slot_rows = piece.reshape(-1, piece.shape[3])
    return (mamba_out, expert_ffn(gate_up, slot_rows)[None])


def local(
    x_in, z_in, b_in, c_in, decay_log, skip, out_weight, moe_gain, gate_up, expert_ids, slot_ids
):
    seq_count, block_len, width_in = x_in.shape
    state_size = b_in.shape[2]
    model_width = moe_gain.shape[0]
    col_width = out_weight.shape[1]
    per_block = expert_ids.shape[1]
    pick_count = expert_ids.shape[2]
    dp_count = lax.axis_size("dp")
    ctx_count = lax.axis_size("ctx")
    group_count = lax.axis_size("expert")
    device_count = dp_count * ctx_count * group_count
    row_count = seq_count * per_block
    capacity = max(2, 4 * row_count // group_count)

    head_count = decay_log.shape[2]
    decay_base = 2 * width_in + 2 * state_size

    def front(x_part, z_part, b_part, c_part, decay_part):
        part_count = x_part.shape[0]
        packed = jnp.concatenate([x_part, z_part, b_part, c_part] + split_exact(decay_part), axis=2)
        packed = jnp.moveaxis(gather_blocks(packed, "ctx", ctx_count), 0, 1).reshape(
            part_count, ctx_count * block_len, packed.shape[2]
        )
        decay_all = join_exact(
            [packed[:, :, decay_base + i * head_count : decay_base + (i + 1) * head_count] for i in range(3)]
        )
        x_all = packed[:, :, :width_in]
        z_all = packed[:, :, width_in : 2 * width_in]
        b_all = packed[:, :, 2 * width_in : 2 * width_in + state_size]
        c_all = packed[:, :, 2 * width_in + state_size : decay_base]
        ssd = mixer(x_all, b_all, c_all, decay_all, skip)
        gated = (ssd * jax.nn.silu(z_all.astype(jnp.float32))).astype(jnp.bfloat16)
        return jnp.einsum("stk,kd->std", gated, out_weight, preferred_element_type=jnp.float32)

    if device_count * row_count * model_width * 2 > (8 << 20):
        partial_value = front(x_in, z_in, b_in, c_in, decay_log)
        return dispatch_routed(partial_value, moe_gain, gate_up, expert_ids, slot_ids, capacity)
    total_len = ctx_count * block_len
    route = jnp.stack([expert_ids, slot_ids], axis=-1).astype(jnp.float32).reshape(-1)
    route_len = route.shape[0]
    extra_rows = -(-(group_count * route_len) // col_width)
    route_row = jnp.zeros((extra_rows * col_width,), jnp.float32)
    route_row = lax.dynamic_update_slice(route_row, route, (lax.axis_index("expert") * route_len,))
    piece_width = col_width // group_count
    split = 2 if seq_count % 2 == 0 else 1
    part_len = seq_count // split
    token_parts = []
    for part in range(split):
        streams = slice(part * part_len, (part + 1) * part_len)
        partial_value = front(
            x_in[streams], z_in[streams], b_in[streams], c_in[streams], decay_log[streams]
        )
        rows = partial_value.reshape(part_len * total_len, col_width)
        if part == 0:
            rows = jnp.concatenate([rows, route_row.reshape(extra_rows, col_width)], axis=0)
        piece = sum_scatter(rows, "expert", group_count)
        gathered = gather_blocks(piece, "ctx", ctx_count)
        gathered = gather_xor(gathered, "expert", group_count)
        gathered = gather_blocks(gathered, "dp", dp_count)
        token_parts.append(gathered)
    part_rows = part_len * total_len
    extra = token_parts[0][:, :, :, part_rows:, :]
    token_parts[0] = token_parts[0][:, :, :, :part_rows, :]
    gathered = jnp.concatenate(token_parts + [extra], axis=3)
    row_total = seq_count * total_len
    extra = jnp.transpose(gathered[:, :, :, row_total:, :], (0, 2, 3, 1, 4))
    routes = extra.reshape(dp_count, ctx_count, -1)[:, :, : group_count * route_len]
    routes = routes.astype(jnp.int32)
    routes = routes.reshape(dp_count, ctx_count, group_count, seq_count, per_block, pick_count, 2)
    routes = jnp.transpose(routes, (0, 3, 1, 2, 4, 5, 6))
    tokens = gathered[:, :, :, :row_total, :]
    mine_rows = lax.dynamic_index_in_dim(tokens, lax.axis_index("dp"), axis=0, keepdims=False)
    mine_rows = mine_rows.reshape(
        group_count, ctx_count, seq_count, ctx_count * group_count, per_block, piece_width
    )
    mine_block = lax.axis_index("ctx") * group_count + lax.axis_index("expert")
    mine_rows = lax.dynamic_index_in_dim(mine_rows, mine_block, axis=3, keepdims=False)
    mamba_out = jnp.transpose(mine_rows, (2, 3, 1, 0, 4)).reshape(seq_count, per_block, model_width)
    token_count = dp_count * row_total
    flat = tokens.astype(jnp.float32)
    square_sum = jnp.sum(flat * flat, axis=(1, 2, 4), keepdims=True)
    scale = lax.rsqrt(square_sum / model_width + 1e-05)
    gain = jnp.transpose(moe_gain.reshape(ctx_count, group_count, piece_width), (1, 0, 2))
    normed = (flat * scale * gain[None, :, :, None, :]).astype(jnp.bfloat16)

    group = (
        (jnp.arange(dp_count)[:, None, None, None, None] * ctx_count
         + jnp.arange(ctx_count)[None, None, :, None, None]) * group_count
        + jnp.arange(group_count)[None, None, None, :, None]
    )
    group = jnp.broadcast_to(group, (dp_count, seq_count, ctx_count, group_count, per_block))
    target = group.reshape(token_count, 1) * capacity + routes[..., 1].reshape(token_count, pick_count)
    mine = routes[..., 0].reshape(token_count, pick_count) == lax.axis_index("expert")
    slot_count = device_count * capacity
    hit = mine[..., None] & (target[..., None] == jnp.arange(slot_count))
    selector = jnp.any(hit, axis=1).reshape(dp_count, row_total, slot_count)
    dispatched = jnp.einsum(
        "drq,decrk->qcek", selector.astype(jnp.bfloat16), normed, preferred_element_type=jnp.float32
    ).astype(jnp.bfloat16)
    hidden = expert_ffn(gate_up, dispatched.reshape(slot_count, model_width))
    return (mamba_out, hidden[None])


def solution(mesh):
    in_specs = (
        P("dp", "ctx", "expert"),
        P("dp", "ctx", "expert"),
        P("dp", "ctx", None),
        P("dp", "ctx", None),
        P("dp", "ctx", "expert"),
        P("expert"),
        P("expert", "ctx"),
        P(),
        P("expert", None, ("dp", "ctx"), None),
        P("dp", ("ctx", "expert"), None),
        P("dp", ("ctx", "expert"), None),
    )
    out_specs = (P("dp", ("ctx", "expert"), None), P("expert", ("dp", "ctx"), None))
    return jax.shard_map(local, mesh=mesh, in_specs=in_specs, out_specs=out_specs, check_vma=False)
```

```python
import jax
import jax.numpy as jnp
from jax import lax
from jax.sharding import PartitionSpec as P

P_SIZE = 64
ALL_AXES = ("dp", "ctx", "expert")


def place(received, sources, count):
    slots = []
    for slot in range(count):
        block = received[0]
        for other, source in zip(received[1:], sources[1:]):
            block = jnp.where(source == slot, other, block)
        slots.append(block)
    return jnp.stack(slots)


def gather_blocks(value, axis_name, count):
    me = lax.axis_index(axis_name)
    received = [value]
    sources = [me]
    for shift in range(1, count):
        perm = [(i, (i + shift) % count) for i in range(count)]
        received.append(lax.ppermute(value, axis_name, perm))
        sources.append((me - shift) % count)
    return place(received, sources, count)


def gather_xor(value, axis_name, count):
    me = lax.axis_index(axis_name)
    received = [value]
    sources = [me]
    for shift in range(1, count):
        perm = [(i, i ^ shift) for i in range(count)]
        received.append(lax.ppermute(value, axis_name, perm))
        sources.append(me ^ shift)
    return place(received, sources, count)


def sum_scatter(value, axis_name, count):
    me = lax.axis_index(axis_name)
    pieces = value.reshape(value.shape[:-1] + (count, value.shape[-1] // count))
    total = lax.dynamic_index_in_dim(pieces, me, axis=-2, keepdims=False)
    for shift in range(1, count):
        perm = [(i, i ^ shift) for i in range(count)]
        send = lax.dynamic_index_in_dim(pieces, me ^ shift, axis=-2, keepdims=False)
        total = total + lax.ppermute(send, axis_name, perm)
    return total.astype(jnp.bfloat16)


def split_exact(value):
    high = value.astype(jnp.bfloat16)
    rest = value - lax.optimization_barrier(high).astype(jnp.float32)
    middle = rest.astype(jnp.bfloat16)
    low = (rest - lax.optimization_barrier(middle).astype(jnp.float32)).astype(jnp.bfloat16)
    return [high, middle, low]


def join_exact(parts):
    high, middle, low = (part.astype(jnp.float32) for part in parts)
    return (high + middle) + low


def mixer(x_in, b_in, c_in, decay_log, skip):
    highest = lax.Precision.HIGHEST
    seq_count, total_len, width_in = x_in.shape
    head_count = skip.shape[0]
    state_size = b_in.shape[2]
    chunk = total_len if total_len <= 128 else 64
    chunks = total_len // chunk
    x_float = x_in.astype(jnp.float32).reshape(seq_count, chunks, chunk, head_count, P_SIZE)
    b_float = b_in.astype(jnp.float32).reshape(seq_count, chunks, chunk, state_size)
    c_float = c_in.astype(jnp.float32).reshape(seq_count, chunks, chunk, state_size)
    cum_decay = jnp.cumsum(decay_log.reshape(seq_count, chunks, chunk, head_count), axis=2)
    scores = jnp.einsum(
        "sktn,skun->sktu",
        c_in.reshape(seq_count, chunks, chunk, state_size),
        b_in.reshape(seq_count, chunks, chunk, state_size),
        preferred_element_type=jnp.float32,
    )
    causal = (jnp.arange(chunk)[:, None] >= jnp.arange(chunk)[None, :])[None, None, :, :, None]
    spans = cum_decay[:, :, :, None, :] - cum_decay[:, :, None, :, :]
    kernel = jnp.where(causal, jnp.exp(jnp.where(causal, spans, 0.0)), 0.0) * scores[..., None]
    x_parts = x_in.reshape(seq_count, chunks, chunk, head_count, P_SIZE)
    ssd = jnp.einsum(
        "sktuh,skuhp->skthp",
        jnp.concatenate(split_exact(kernel), axis=3),
        jnp.concatenate([x_parts] * 3, axis=2),
        preferred_element_type=jnp.float32,
    )
    if chunks > 1:
        final_decay = cum_decay[:, :, -1, :]
        tails = jnp.exp(final_decay[:, :, None, :] - cum_decay)
        states = jnp.einsum("skuh,skuhp,skun->skhpn", tails, x_float, b_float, precision=highest)

        def step(carry, inputs):
            decay_k, state_k = inputs
            return decay_k[:, :, None, None] * carry + state_k, carry

        _, incoming = lax.scan(
            step,
            jnp.zeros_like(states[:, 0]),
            (jnp.moveaxis(jnp.exp(final_decay), 1, 0), jnp.moveaxis(states, 1, 0)),
        )
        incoming = jnp.moveaxis(incoming, 0, 1)
        ssd = ssd + jnp.exp(cum_decay)[..., None] * jnp.einsum(
            "sktn,skhpn->skthp", c_float, incoming, precision=highest
        )
    ssd = ssd + skip[None, None, None, :, None] * x_float
    return ssd.reshape(seq_count, total_len, width_in)


def expert_ffn(gate_up, slot_rows):
    both = jnp.einsum("gfd,qd->gfq", gate_up[0], slot_rows, preferred_element_type=jnp.float32)
    return (jax.nn.silu(both[0]) * both[1]).astype(jnp.bfloat16)


def dispatch_routed(partial_value, moe_gain, gate_up, expert_ids, slot_ids, capacity):
    seq_count = partial_value.shape[0]
    model_width = moe_gain.shape[0]
    per_block = expert_ids.shape[1]
    pick_count = expert_ids.shape[2]
    row_count = seq_count * per_block
    ctx_count = lax.axis_size("ctx")
    group_count = lax.axis_size("expert")
    grouped = partial_value.reshape(
        seq_count, ctx_count, group_count, per_block, partial_value.shape[2]
    )
    reduced = lax.psum_scatter(grouped, "expert", scatter_dimension=2, tiled=True).astype(
        jnp.bfloat16
    )
    swapped = lax.all_to_all(reduced, "ctx", split_axis=1, concat_axis=4, tiled=True)
    mamba_out = swapped.reshape(seq_count, per_block, model_width)
    flat = mamba_out.reshape(row_count, model_width).astype(jnp.float32)
    scale = lax.rsqrt(jnp.mean(flat * flat, axis=1, keepdims=True) + 1e-05)
    normed = (flat * scale * moe_gain[None, :]).astype(jnp.bfloat16)
    chosen = expert_ids.reshape(row_count, pick_count)
    placed = slot_ids.reshape(row_count, pick_count)
    match_expert = chosen[:, :, None, None] == jnp.arange(group_count)[None, None, :, None]
    match_slot = placed[:, :, None, None] == jnp.arange(capacity)[None, None, None, :]
    selector = (match_expert & match_slot).astype(jnp.bfloat16)
    outgoing = jnp.einsum(
        "rkec,rd->ecd", selector, normed, preferred_element_type=jnp.float32
    ).astype(jnp.bfloat16)
    arrived = lax.all_to_all(outgoing, "expert", split_axis=0, concat_axis=0, tiled=True)
    piece = lax.all_gather(arrived[None], ("dp", "ctx"), axis=0, tiled=True)
    slot_rows = piece.reshape(-1, piece.shape[3])
    return (mamba_out, expert_ffn(gate_up, slot_rows)[None])


def local(
    x_in, z_in, b_in, c_in, decay_log, skip, out_weight, moe_gain, gate_up, expert_ids, slot_ids
):
    seq_count, block_len, width_in = x_in.shape
    state_size = b_in.shape[2]
    model_width = moe_gain.shape[0]
    col_width = out_weight.shape[1]
    per_block = expert_ids.shape[1]
    pick_count = expert_ids.shape[2]
    dp_count = lax.axis_size("dp")
    ctx_count = lax.axis_size("ctx")
    group_count = lax.axis_size("expert")
    device_count = dp_count * ctx_count * group_count
    row_count = seq_count * per_block
    capacity = max(2, 4 * row_count // group_count)

    head_count = decay_log.shape[2]
    packed = jnp.concatenate([x_in, z_in, b_in, c_in] + split_exact(decay_log), axis=2)
    packed = jnp.moveaxis(gather_blocks(packed, "ctx", ctx_count), 0, 1).reshape(
        seq_count, ctx_count * block_len, packed.shape[2]
    )
    decay_base = 2 * width_in + 2 * state_size
    decay_all = join_exact(
        [packed[:, :, decay_base + i * head_count : decay_base + (i + 1) * head_count] for i in range(3)]
    )

    x_all = packed[:, :, :width_in]
    z_all = packed[:, :, width_in : 2 * width_in]
    b_all = packed[:, :, 2 * width_in : 2 * width_in + state_size]
    c_all = packed[:, :, 2 * width_in + state_size : decay_base]
    ssd = mixer(x_all, b_all, c_all, decay_all, skip)
    gated = (ssd * jax.nn.silu(z_all.astype(jnp.float32))).astype(jnp.bfloat16)
    partial_value = jnp.einsum(
        "stk,kd->std", gated, out_weight, preferred_element_type=jnp.float32
    )
    if device_count * row_count * model_width * 2 > (8 << 20):
        return dispatch_routed(partial_value, moe_gain, gate_up, expert_ids, slot_ids, capacity)
    total_len = partial_value.shape[1]
    route = jnp.stack([expert_ids, slot_ids], axis=-1).astype(jnp.float32).reshape(-1)
    route_len = route.shape[0]
    extra_rows = -(-(group_count * route_len) // col_width)
    route_row = jnp.zeros((extra_rows * col_width,), jnp.float32)
    route_row = lax.dynamic_update_slice(route_row, route, (lax.axis_index("expert") * route_len,))
    extended = jnp.concatenate(
        [partial_value.reshape(seq_count * total_len, col_width), route_row.reshape(extra_rows, col_width)],
        axis=0,
    )
    piece_width = col_width // group_count
    piece = sum_scatter(extended, "expert", group_count)
    gathered = gather_blocks(piece, "ctx", ctx_count)
    gathered = gather_xor(gathered, "expert", group_count)
    gathered = gather_blocks(gathered, "dp", dp_count)
    row_total = seq_count * total_len
    extra = jnp.transpose(gathered[:, :, :, row_total:, :], (0, 2, 3, 1, 4))
    routes = extra.reshape(dp_count, ctx_count, -1)[:, :, : group_count * route_len]
    routes = routes.astype(jnp.int32)
    routes = routes.reshape(dp_count, ctx_count, group_count, seq_count, per_block, pick_count, 2)
    routes = jnp.transpose(routes, (0, 3, 1, 2, 4, 5, 6))
    tokens = gathered[:, :, :, :row_total, :]
    mine_rows = lax.dynamic_index_in_dim(tokens, lax.axis_index("dp"), axis=0, keepdims=False)
    mine_rows = mine_rows.reshape(
        group_count, ctx_count, seq_count, ctx_count * group_count, per_block, piece_width
    )
    mine_block = lax.axis_index("ctx") * group_count + lax.axis_index("expert")
    mine_rows = lax.dynamic_index_in_dim(mine_rows, mine_block, axis=3, keepdims=False)
    mamba_out = jnp.transpose(mine_rows, (2, 3, 1, 0, 4)).reshape(seq_count, per_block, model_width)
    token_count = dp_count * row_total
    flat = tokens.astype(jnp.float32)
    square_sum = jnp.sum(flat * flat, axis=(1, 2, 4), keepdims=True)
    scale = lax.rsqrt(square_sum / model_width + 1e-05)
    gain = jnp.transpose(moe_gain.reshape(ctx_count, group_count, piece_width), (1, 0, 2))
    normed = (flat * scale * gain[None, :, :, None, :]).astype(jnp.bfloat16)

    group = (
        (jnp.arange(dp_count)[:, None, None, None, None] * ctx_count
         + jnp.arange(ctx_count)[None, None, :, None, None]) * group_count
        + jnp.arange(group_count)[None, None, None, :, None]
    )
    group = jnp.broadcast_to(group, (dp_count, seq_count, ctx_count, group_count, per_block))
    target = group.reshape(token_count, 1) * capacity + routes[..., 1].reshape(token_count, pick_count)
    mine = routes[..., 0].reshape(token_count, pick_count) == lax.axis_index("expert")
    slot_count = device_count * capacity
    hit = mine[..., None] & (target[..., None] == jnp.arange(slot_count))
    selector = jnp.any(hit, axis=1).reshape(dp_count, row_total, slot_count)
    dispatched = jnp.einsum(
        "drq,decrk->qcek", selector.astype(jnp.bfloat16), normed, preferred_element_type=jnp.float32
    ).astype(jnp.bfloat16)
    hidden = expert_ffn(gate_up, dispatched.reshape(slot_count, model_width))
    return (mamba_out, hidden[None])


def solution(mesh):
    in_specs = (
        P("dp", "ctx", "expert"),
        P("dp", "ctx", "expert"),
        P("dp", "ctx", None),
        P("dp", "ctx", None),
        P("dp", "ctx", "expert"),
        P("expert"),
        P("expert", "ctx"),
        P(),
        P("expert", None, ("dp", "ctx"), None),
        P("dp", ("ctx", "expert"), None),
        P("dp", ("ctx", "expert"), None),
    )
    out_specs = (P("dp", ("ctx", "expert"), None), P("expert", ("dp", "ctx"), None))
    return jax.shard_map(local, mesh=mesh, in_specs=in_specs, out_specs=out_specs, check_vma=False)
```

```python
import jax
import jax.numpy as jnp
from jax import lax
from jax.sharding import PartitionSpec as P

P_SIZE = 64
ALL_AXES = ("dp", "ctx", "expert")


def place(received, sources, count):
    slots = []
    for slot in range(count):
        block = received[0]
        for other, source in zip(received[1:], sources[1:]):
            block = jnp.where(source == slot, other, block)
        slots.append(block)
    return jnp.stack(slots)


def gather_blocks(value, axis_name, count):
    me = lax.axis_index(axis_name)
    received = [value]
    sources = [me]
    for shift in range(1, count):
        perm = [(i, (i + shift) % count) for i in range(count)]
        received.append(lax.ppermute(value, axis_name, perm))
        sources.append((me - shift) % count)
    return place(received, sources, count)


def gather_xor(value, axis_name, count):
    me = lax.axis_index(axis_name)
    received = [value]
    sources = [me]
    for shift in range(1, count):
        perm = [(i, i ^ shift) for i in range(count)]
        received.append(lax.ppermute(value, axis_name, perm))
        sources.append(me ^ shift)
    return place(received, sources, count)


def sum_scatter(value, axis_name, count):
    me = lax.axis_index(axis_name)
    pieces = value.reshape(value.shape[:-1] + (count, value.shape[-1] // count))
    total = lax.dynamic_index_in_dim(pieces, me, axis=-2, keepdims=False)
    for shift in range(1, count):
        perm = [(i, i ^ shift) for i in range(count)]
        send = lax.dynamic_index_in_dim(pieces, me ^ shift, axis=-2, keepdims=False)
        total = total + lax.ppermute(send, axis_name, perm)
    return total.astype(jnp.bfloat16)


def split_exact(value):
    high = value.astype(jnp.bfloat16)
    rest = value - lax.optimization_barrier(high).astype(jnp.float32)
    middle = rest.astype(jnp.bfloat16)
    low = (rest - lax.optimization_barrier(middle).astype(jnp.float32)).astype(jnp.bfloat16)
    return [high, middle, low]


def join_exact(parts):
    high, middle, low = (part.astype(jnp.float32) for part in parts)
    return (high + middle) + low


def mixer(x_in, b_in, c_in, decay_log, skip):
    highest = lax.Precision.HIGHEST
    seq_count, total_len, width_in = x_in.shape
    head_count = skip.shape[0]
    state_size = b_in.shape[2]
    chunk = total_len if total_len <= 128 else 64
    chunks = total_len // chunk
    x_float = x_in.astype(jnp.float32).reshape(seq_count, chunks, chunk, head_count, P_SIZE)
    b_float = b_in.astype(jnp.float32).reshape(seq_count, chunks, chunk, state_size)
    c_float = c_in.astype(jnp.float32).reshape(seq_count, chunks, chunk, state_size)
    cum_decay = jnp.cumsum(decay_log.reshape(seq_count, chunks, chunk, head_count), axis=2)
    scores = jnp.einsum("sktn,skun->sktu", c_float, b_float, precision=highest)
    causal = (jnp.arange(chunk)[:, None] >= jnp.arange(chunk)[None, :])[None, None, :, :, None]
    spans = cum_decay[:, :, :, None, :] - cum_decay[:, :, None, :, :]
    kernel = jnp.where(causal, jnp.exp(jnp.where(causal, spans, 0.0)), 0.0) * scores[..., None]
    ssd = jnp.einsum("sktuh,skuhp->skthp", kernel, x_float, precision=highest)
    if chunks > 1:
        final_decay = cum_decay[:, :, -1, :]
        tails = jnp.exp(final_decay[:, :, None, :] - cum_decay)
        states = jnp.einsum("skuh,skuhp,skun->skhpn", tails, x_float, b_float, precision=highest)

        def step(carry, inputs):
            decay_k, state_k = inputs
            return decay_k[:, :, None, None] * carry + state_k, carry

        _, incoming = lax.scan(
            step,
            jnp.zeros_like(states[:, 0]),
            (jnp.moveaxis(jnp.exp(final_decay), 1, 0), jnp.moveaxis(states, 1, 0)),
        )
        incoming = jnp.moveaxis(incoming, 0, 1)
        ssd = ssd + jnp.exp(cum_decay)[..., None] * jnp.einsum(
            "sktn,skhpn->skthp", c_float, incoming, precision=highest
        )
    ssd = ssd + skip[None, None, None, :, None] * x_float
    return ssd.reshape(seq_count, total_len, width_in)


def expert_ffn(gate_up, slot_rows):
    both = jnp.einsum("gfd,qd->gfq", gate_up[0], slot_rows, preferred_element_type=jnp.float32)
    return (jax.nn.silu(both[0]) * both[1]).astype(jnp.bfloat16)


def dispatch_routed(partial_value, moe_gain, gate_up, expert_ids, slot_ids, capacity):
    seq_count = partial_value.shape[0]
    model_width = moe_gain.shape[0]
    per_block = expert_ids.shape[1]
    pick_count = expert_ids.shape[2]
    row_count = seq_count * per_block
    ctx_count = lax.axis_size("ctx")
    group_count = lax.axis_size("expert")
    grouped = partial_value.reshape(
        seq_count, ctx_count, group_count, per_block, partial_value.shape[2]
    )
    reduced = lax.psum_scatter(grouped, "expert", scatter_dimension=2, tiled=True).astype(
        jnp.bfloat16
    )
    swapped = lax.all_to_all(reduced, "ctx", split_axis=1, concat_axis=4, tiled=True)
    mamba_out = swapped.reshape(seq_count, per_block, model_width)
    flat = mamba_out.reshape(row_count, model_width).astype(jnp.float32)
    scale = lax.rsqrt(jnp.mean(flat * flat, axis=1, keepdims=True) + 1e-05)
    normed = (flat * scale * moe_gain[None, :]).astype(jnp.bfloat16)
    chosen = expert_ids.reshape(row_count, pick_count)
    placed = slot_ids.reshape(row_count, pick_count)
    match_expert = chosen[:, :, None, None] == jnp.arange(group_count)[None, None, :, None]
    match_slot = placed[:, :, None, None] == jnp.arange(capacity)[None, None, None, :]
    selector = (match_expert & match_slot).astype(jnp.bfloat16)
    outgoing = jnp.einsum(
        "rkec,rd->ecd", selector, normed, preferred_element_type=jnp.float32
    ).astype(jnp.bfloat16)
    arrived = lax.all_to_all(outgoing, "expert", split_axis=0, concat_axis=0, tiled=True)
    piece = lax.all_gather(arrived[None], ("dp", "ctx"), axis=0, tiled=True)
    slot_rows = piece.reshape(-1, piece.shape[3])
    return (mamba_out, expert_ffn(gate_up, slot_rows)[None])


def local(
    x_in, z_in, b_in, c_in, decay_log, skip, out_weight, moe_gain, gate_up, expert_ids, slot_ids
):
    seq_count, block_len, width_in = x_in.shape
    state_size = b_in.shape[2]
    model_width = moe_gain.shape[0]
    col_width = out_weight.shape[1]
    per_block = expert_ids.shape[1]
    pick_count = expert_ids.shape[2]
    dp_count = lax.axis_size("dp")
    ctx_count = lax.axis_size("ctx")
    group_count = lax.axis_size("expert")
    device_count = dp_count * ctx_count * group_count
    row_count = seq_count * per_block
    capacity = max(2, 4 * row_count // group_count)

    head_count = decay_log.shape[2]
    decay_base = 2 * width_in + 2 * state_size

    def front(x_part, z_part, b_part, c_part, decay_part, after=None):
        part_count = x_part.shape[0]
        packed = jnp.concatenate([x_part, z_part, b_part, c_part] + split_exact(decay_part), axis=2)
        if after is not None:
            _, packed = lax.optimization_barrier((after, packed))
        packed = jnp.moveaxis(gather_blocks(packed, "ctx", ctx_count), 0, 1).reshape(
            part_count, ctx_count * block_len, packed.shape[2]
        )
        decay_all = join_exact(
            [packed[:, :, decay_base + i * head_count : decay_base + (i + 1) * head_count] for i in range(3)]
        )
        x_all = packed[:, :, :width_in]
        z_all = packed[:, :, width_in : 2 * width_in]
        b_all = packed[:, :, 2 * width_in : 2 * width_in + state_size]
        c_all = packed[:, :, 2 * width_in + state_size : decay_base]
        ssd = mixer(x_all, b_all, c_all, decay_all, skip)
        gated = (ssd * jax.nn.silu(z_all.astype(jnp.float32))).astype(jnp.bfloat16)
        return jnp.einsum("stk,kd->std", gated, out_weight, preferred_element_type=jnp.float32), packed

    if device_count * row_count * model_width * 2 > (8 << 20):
        partial_value = front(x_in, z_in, b_in, c_in, decay_log)[0]
        return dispatch_routed(partial_value, moe_gain, gate_up, expert_ids, slot_ids, capacity)
    total_len = ctx_count * block_len
    route = jnp.stack([expert_ids, slot_ids], axis=-1).astype(jnp.float32).reshape(-1)
    route_len = route.shape[0]
    extra_rows = -(-(group_count * route_len) // col_width)
    route_row = jnp.zeros((extra_rows * col_width,), jnp.float32)
    route_row = lax.dynamic_update_slice(route_row, route, (lax.axis_index("expert") * route_len,))
    piece_width = col_width // group_count
    split = 2 if seq_count % 2 == 0 else 1
    part_len = seq_count // split
    token_parts = []
    arrived = None
    for part in range(split):
        streams = slice(part * part_len, (part + 1) * part_len)
        partial_value, arrived = front(
            x_in[streams], z_in[streams], b_in[streams], c_in[streams], decay_log[streams], arrived
        )
        rows = partial_value.reshape(part_len * total_len, col_width)
        if part == 0:
            rows = jnp.concatenate([rows, route_row.reshape(extra_rows, col_width)], axis=0)
        piece = sum_scatter(rows, "expert", group_count)
        gathered = gather_blocks(piece, "ctx", ctx_count)
        gathered = gather_xor(gathered, "expert", group_count)
        gathered = gather_blocks(gathered, "dp", dp_count)
        token_parts.append(gathered)
    part_rows = part_len * total_len
    extra = token_parts[0][:, :, :, part_rows:, :]
    token_parts[0] = token_parts[0][:, :, :, :part_rows, :]
    gathered = jnp.concatenate(token_parts + [extra], axis=3)
    row_total = seq_count * total_len
    extra = jnp.transpose(gathered[:, :, :, row_total:, :], (0, 2, 3, 1, 4))
    routes = extra.reshape(dp_count, ctx_count, -1)[:, :, : group_count * route_len]
    routes = routes.astype(jnp.int32)
    routes = routes.reshape(dp_count, ctx_count, group_count, seq_count, per_block, pick_count, 2)
    routes = jnp.transpose(routes, (0, 3, 1, 2, 4, 5, 6))
    tokens = gathered[:, :, :, :row_total, :]
    mine_rows = lax.dynamic_index_in_dim(tokens, lax.axis_index("dp"), axis=0, keepdims=False)
    mine_rows = mine_rows.reshape(
        group_count, ctx_count, seq_count, ctx_count * group_count, per_block, piece_width
    )
    mine_block = lax.axis_index("ctx") * group_count + lax.axis_index("expert")
    mine_rows = lax.dynamic_index_in_dim(mine_rows, mine_block, axis=3, keepdims=False)
    mamba_out = jnp.transpose(mine_rows, (2, 3, 1, 0, 4)).reshape(seq_count, per_block, model_width)
    token_count = dp_count * row_total
    flat = tokens.astype(jnp.float32)
    square_sum = jnp.sum(flat * flat, axis=(1, 2, 4), keepdims=True)
    scale = lax.rsqrt(square_sum / model_width + 1e-05)
    gain = jnp.transpose(moe_gain.reshape(ctx_count, group_count, piece_width), (1, 0, 2))
    normed = (flat * scale * gain[None, :, :, None, :]).astype(jnp.bfloat16)

    group = (
        (jnp.arange(dp_count)[:, None, None, None, None] * ctx_count
         + jnp.arange(ctx_count)[None, None, :, None, None]) * group_count
        + jnp.arange(group_count)[None, None, None, :, None]
    )
    group = jnp.broadcast_to(group, (dp_count, seq_count, ctx_count, group_count, per_block))
    target = group.reshape(token_count, 1) * capacity + routes[..., 1].reshape(token_count, pick_count)
    mine = routes[..., 0].reshape(token_count, pick_count) == lax.axis_index("expert")
    slot_count = device_count * capacity
    hit = mine[..., None] & (target[..., None] == jnp.arange(slot_count))
    selector = jnp.any(hit, axis=1).reshape(dp_count, row_total, slot_count)
    dispatched = jnp.einsum(
        "drq,decrk->qcek", selector.astype(jnp.bfloat16), normed, preferred_element_type=jnp.float32
    ).astype(jnp.bfloat16)
    hidden = expert_ffn(gate_up, dispatched.reshape(slot_count, model_width))
    return (mamba_out, hidden[None])


def solution(mesh):
    in_specs = (
        P("dp", "ctx", "expert"),
        P("dp", "ctx", "expert"),
        P("dp", "ctx", None),
        P("dp", "ctx", None),
        P("dp", "ctx", "expert"),
        P("expert"),
        P("expert", "ctx"),
        P(),
        P("expert", None, ("dp", "ctx"), None),
        P("dp", ("ctx", "expert"), None),
        P("dp", ("ctx", "expert"), None),
    )
    out_specs = (P("dp", ("ctx", "expert"), None), P("expert", ("dp", "ctx"), None))
    return jax.shard_map(local, mesh=mesh, in_specs=in_specs, out_specs=out_specs, check_vma=False)
```

```python
import jax
import jax.numpy as jnp
from jax import lax
from jax.sharding import PartitionSpec as P


P_SIZE = 64


def place(received, sources, count):
    slots = []
    for slot in range(count):
        block = received[0]
        for other, source in zip(received[1:], sources[1:]):
            block = jnp.where(source == slot, other, block)
        slots.append(block)
    return jnp.stack(slots)


def gather_blocks(value, axis_name, count):
    me = lax.axis_index(axis_name)
    received = [value]
    sources = [me]
    for shift in range(1, count):
        perm = [(i, (i + shift) % count) for i in range(count)]
        received.append(lax.ppermute(value, axis_name, perm))
        sources.append((me - shift) % count)
    return place(received, sources, count)


def gather_xor(value, axis_name, count):
    me = lax.axis_index(axis_name)
    received = [value]
    sources = [me]
    for shift in range(1, count):
        perm = [(i, i ^ shift) for i in range(count)]
        received.append(lax.ppermute(value, axis_name, perm))
        sources.append(me ^ shift)
    return place(received, sources, count)


def sum_scatter(value, axis_name, count):
    me = lax.axis_index(axis_name)
    pieces = value.reshape(value.shape[:-1] + (count, value.shape[-1] // count))
    total = lax.dynamic_index_in_dim(pieces, me, axis=-2, keepdims=False)
    for shift in range(1, count):
        perm = [(i, i ^ shift) for i in range(count)]
        send = lax.dynamic_index_in_dim(pieces, me ^ shift, axis=-2, keepdims=False)
        total = total + lax.ppermute(send, axis_name, perm)
    return total.astype(jnp.bfloat16)


def split_exact(value):
    high = value.astype(jnp.bfloat16)
    rest = value - lax.optimization_barrier(high).astype(jnp.float32)
    middle = rest.astype(jnp.bfloat16)
    low = (rest - lax.optimization_barrier(middle).astype(jnp.float32)).astype(jnp.bfloat16)
    return [high, middle, low]


def join_exact(parts):
    high, middle, low = (part.astype(jnp.float32) for part in parts)
    return (high + middle) + low


def mixer(x_in, b_in, c_in, decay_log, skip):
    highest = lax.Precision.HIGHEST
    seq_count, total_len, width_in = x_in.shape
    head_count = skip.shape[0]
    state_size = b_in.shape[2]
    chunk = total_len if total_len <= 128 else 64
    chunks = total_len // chunk
    x_float = x_in.astype(jnp.float32).reshape(seq_count, chunks, chunk, head_count, P_SIZE)
    b_float = b_in.astype(jnp.float32).reshape(seq_count, chunks, chunk, state_size)
    c_float = c_in.astype(jnp.float32).reshape(seq_count, chunks, chunk, state_size)
    cum_decay = jnp.cumsum(decay_log.reshape(seq_count, chunks, chunk, head_count), axis=2)
    scores = jnp.einsum("sktn,skun->sktu", c_float, b_float, precision=highest)
    causal = (jnp.arange(chunk)[:, None] >= jnp.arange(chunk)[None, :])[None, None, :, :, None]
    spans = cum_decay[:, :, :, None, :] - cum_decay[:, :, None, :, :]
    kernel = jnp.where(causal, jnp.exp(jnp.where(causal, spans, 0.0)), 0.0) * scores[..., None]
    ssd = jnp.einsum("sktuh,skuhp->skthp", kernel, x_float, precision=highest)
    if chunks > 1:
        final_decay = cum_decay[:, :, -1, :]
        tails = jnp.exp(final_decay[:, :, None, :] - cum_decay)
        states = jnp.einsum("skuh,skuhp,skun->skhpn", tails, x_float, b_float, precision=highest)

        def step(carry, inputs):
            decay_k, state_k = inputs
            return decay_k[:, :, None, None] * carry + state_k, carry

        _, incoming = lax.scan(
            step,
            jnp.zeros_like(states[:, 0]),
            (jnp.moveaxis(jnp.exp(final_decay), 1, 0), jnp.moveaxis(states, 1, 0)),
        )
        incoming = jnp.moveaxis(incoming, 0, 1)
        ssd = ssd + jnp.exp(cum_decay)[..., None] * jnp.einsum(
            "sktn,skhpn->skthp", c_float, incoming, precision=highest
        )
    ssd = ssd + skip[None, None, None, :, None] * x_float
    return ssd.reshape(seq_count, total_len, width_in)


def expert_ffn(gate_up, slot_rows):
    both = jnp.einsum("gfd,qd->gfq", gate_up[0], slot_rows, preferred_element_type=jnp.float32)
    return (jax.nn.silu(both[0]) * both[1]).astype(jnp.bfloat16)


def dispatch_routed(partial_value, moe_gain, gate_up, expert_ids, slot_ids, capacity):
    seq_count = partial_value.shape[0]
    model_width = moe_gain.shape[0]
    per_block = expert_ids.shape[1]
    pick_count = expert_ids.shape[2]
    row_count = seq_count * per_block
    ctx_count = lax.axis_size("ctx")
    group_count = lax.axis_size("expert")
    grouped = partial_value.reshape(
        seq_count, ctx_count, group_count, per_block, partial_value.shape[2]
    )
    reduced = lax.psum_scatter(grouped, "expert", scatter_dimension=2, tiled=True).astype(
        jnp.bfloat16
    )
    swapped = lax.all_to_all(reduced, "ctx", split_axis=1, concat_axis=4, tiled=True)
    mamba_out = swapped.reshape(seq_count, per_block, model_width)
    flat = mamba_out.reshape(row_count, model_width).astype(jnp.float32)
    scale = lax.rsqrt(jnp.mean(flat * flat, axis=1, keepdims=True) + 1e-05)
    normed = (flat * scale * moe_gain[None, :]).astype(jnp.bfloat16)
    chosen = expert_ids.reshape(row_count, pick_count)
    placed = slot_ids.reshape(row_count, pick_count)
    match_expert = chosen[:, :, None, None] == jnp.arange(group_count)[None, None, :, None]
    match_slot = placed[:, :, None, None] == jnp.arange(capacity)[None, None, None, :]
    selector = (match_expert & match_slot).astype(jnp.bfloat16)
    outgoing = jnp.einsum(
        "rkec,rd->ecd", selector, normed, preferred_element_type=jnp.float32
    ).astype(jnp.bfloat16)
    arrived = lax.all_to_all(outgoing, "expert", split_axis=0, concat_axis=0, tiled=True)
    piece = lax.all_gather(arrived[None], ("dp", "ctx"), axis=0, tiled=True)
    slot_rows = piece.reshape(-1, piece.shape[3])
    return (mamba_out, expert_ffn(gate_up, slot_rows)[None])


def local(
    x_in, z_in, b_in, c_in, decay_log, skip, out_weight, moe_gain, gate_up, expert_ids, slot_ids
):
    seq_count, block_len, width_in = x_in.shape
    state_size = b_in.shape[2]
    model_width = moe_gain.shape[0]
    col_width = out_weight.shape[1]
    per_block = expert_ids.shape[1]
    pick_count = expert_ids.shape[2]
    dp_count = lax.axis_size("dp")
    ctx_count = lax.axis_size("ctx")
    group_count = lax.axis_size("expert")
    device_count = dp_count * ctx_count * group_count
    row_count = seq_count * per_block
    capacity = max(2, 4 * row_count // group_count)

    head_count = decay_log.shape[2]
    decay_base = 2 * width_in + 2 * state_size

    def front(x_part, z_part, b_part, c_part, decay_part, after=None):
        part_count = x_part.shape[0]
        packed = jnp.concatenate([x_part, z_part, b_part, c_part] + split_exact(decay_part), axis=2)
        if after is not None:
            _, packed = lax.optimization_barrier((after, packed))
        packed = gather_blocks(packed, "ctx", ctx_count)
        packed = jnp.moveaxis(packed, 0, 1).reshape(
            part_count, ctx_count * block_len, packed.shape[3]
        )
        decay_all = join_exact(
            [packed[:, :, decay_base + i * head_count : decay_base + (i + 1) * head_count] for i in range(3)]
        )
        x_all = packed[:, :, :width_in]
        z_all = packed[:, :, width_in : 2 * width_in]
        b_all = packed[:, :, 2 * width_in : 2 * width_in + state_size]
        c_all = packed[:, :, 2 * width_in + state_size : decay_base]
        ssd = mixer(x_all, b_all, c_all, decay_all, skip)
        gated = (ssd * jax.nn.silu(z_all.astype(jnp.float32))).astype(jnp.bfloat16)
        projected = jnp.einsum("stk,kd->std", gated, out_weight, preferred_element_type=jnp.float32)
        return projected, packed

    if device_count * row_count * model_width * 2 > (8 << 20):
        partial_value = front(x_in, z_in, b_in, c_in, decay_log)[0]
        return dispatch_routed(partial_value, moe_gain, gate_up, expert_ids, slot_ids, capacity)
    total_len = ctx_count * block_len
    route = jnp.stack([expert_ids, slot_ids], axis=-1).astype(jnp.float32).reshape(-1)
    route_len = route.shape[0]
    extra_rows = -(-(group_count * route_len) // col_width)
    route_row = jnp.zeros((extra_rows * col_width,), jnp.float32)
    route_row = lax.dynamic_update_slice(route_row, route, (lax.axis_index("expert") * route_len,))
    piece_width = col_width // group_count
    split = 2 if seq_count % 2 == 0 else 1
    part_len = seq_count // split
    token_parts = []
    arrived = None
    for part in range(split):
        streams = slice(part * part_len, (part + 1) * part_len)
        partial_value, arrived = front(
            x_in[streams], z_in[streams], b_in[streams], c_in[streams], decay_log[streams], arrived
        )
        rows = partial_value.reshape(part_len * total_len, col_width)
        if part == 0:
            rows = jnp.concatenate([rows, route_row.reshape(extra_rows, col_width)], axis=0)
        piece = sum_scatter(rows, "expert", group_count)
        gathered = gather_blocks(piece, "ctx", ctx_count)
        gathered = gather_xor(gathered, "expert", group_count)
        gathered = gather_blocks(gathered, "dp", dp_count)
        token_parts.append(gathered)
    part_rows = part_len * total_len
    extra = token_parts[0][:, :, :, part_rows:, :]
    token_parts[0] = token_parts[0][:, :, :, :part_rows, :]
    gathered = jnp.concatenate(token_parts + [extra], axis=3)
    row_total = seq_count * total_len
    extra = jnp.transpose(gathered[:, :, :, row_total:, :], (0, 2, 3, 1, 4))
    routes = extra.reshape(dp_count, ctx_count, -1)[:, :, : group_count * route_len]
    routes = routes.astype(jnp.int32)
    routes = routes.reshape(dp_count, ctx_count, group_count, seq_count, per_block, pick_count, 2)
    routes = jnp.transpose(routes, (0, 3, 1, 2, 4, 5, 6))
    tokens = gathered[:, :, :, :row_total, :]
    mine_rows = lax.dynamic_index_in_dim(tokens, lax.axis_index("dp"), axis=0, keepdims=False)
    mine_rows = mine_rows.reshape(
        group_count, ctx_count, seq_count, ctx_count * group_count, per_block, piece_width
    )
    mine_block = lax.axis_index("ctx") * group_count + lax.axis_index("expert")
    mine_rows = lax.dynamic_index_in_dim(mine_rows, mine_block, axis=3, keepdims=False)
    mamba_out = jnp.transpose(mine_rows, (2, 3, 1, 0, 4)).reshape(seq_count, per_block, model_width)
    token_count = dp_count * row_total
    flat = tokens.astype(jnp.float32)
    square_sum = jnp.sum(flat * flat, axis=(1, 2, 4), keepdims=True)
    scale = lax.rsqrt(square_sum / model_width + 1e-05)
    gain = jnp.transpose(moe_gain.reshape(ctx_count, group_count, piece_width), (1, 0, 2))
    normed = (flat * scale * gain[None, :, :, None, :]).astype(jnp.bfloat16)

    group = (
        (jnp.arange(dp_count)[:, None, None, None, None] * ctx_count
         + jnp.arange(ctx_count)[None, None, :, None, None]) * group_count
        + jnp.arange(group_count)[None, None, None, :, None]
    )
    group = jnp.broadcast_to(group, (dp_count, seq_count, ctx_count, group_count, per_block))
    target = group.reshape(token_count, 1) * capacity + routes[..., 1].reshape(token_count, pick_count)
    mine = routes[..., 0].reshape(token_count, pick_count) == lax.axis_index("expert")
    slot_count = device_count * capacity
    hit = mine[..., None] & (target[..., None] == jnp.arange(slot_count))
    selector = jnp.any(hit, axis=1).reshape(dp_count, row_total, slot_count)
    dispatched = jnp.einsum(
        "drq,decrk->qcek", selector.astype(jnp.bfloat16), normed, preferred_element_type=jnp.float32
    ).astype(jnp.bfloat16)
    hidden = expert_ffn(gate_up, dispatched.reshape(slot_count, model_width))
    return (mamba_out, hidden[None])


def solution(mesh):
    in_specs = (
        P("dp", "ctx", "expert"),
        P("dp", "ctx", "expert"),
        P("dp", "ctx", None),
        P("dp", "ctx", None),
        P("dp", "ctx", "expert"),
        P("expert"),
        P("expert", "ctx"),
        P(),
        P("expert", None, ("dp", "ctx"), None),
        P("dp", ("ctx", "expert"), None),
        P("dp", ("ctx", "expert"), None),
    )
    out_specs = (P("dp", ("ctx", "expert"), None), P("expert", ("dp", "ctx"), None))

    return jax.shard_map(local, mesh=mesh, in_specs=in_specs, out_specs=out_specs, check_vma=False)
```

```python
import jax
import jax.numpy as jnp
from jax import lax
from jax.sharding import PartitionSpec as P


P_SIZE = 64


def place(received, sources, count):
    slots = []
    for slot in range(count):
        block = received[0]
        for other, source in zip(received[1:], sources[1:]):
            block = jnp.where(source == slot, other, block)
        slots.append(block)
    return jnp.stack(slots)


def gather_blocks(value, axis_name, count):
    me = lax.axis_index(axis_name)
    received = [value]
    sources = [me]
    for shift in range(1, count):
        perm = [(i, (i + shift) % count) for i in range(count)]
        received.append(lax.ppermute(value, axis_name, perm))
        sources.append((me - shift) % count)
    return place(received, sources, count)


def gather_xor(value, axis_name, count):
    me = lax.axis_index(axis_name)
    received = [value]
    sources = [me]
    for shift in range(1, count):
        perm = [(i, i ^ shift) for i in range(count)]
        received.append(lax.ppermute(value, axis_name, perm))
        sources.append(me ^ shift)
    return place(received, sources, count)


def sum_scatter(value, axis_name, count):
    me = lax.axis_index(axis_name)
    pieces = value.reshape(value.shape[:-1] + (count, value.shape[-1] // count))
    total = lax.dynamic_index_in_dim(pieces, me, axis=-2, keepdims=False)
    for shift in range(1, count):
        perm = [(i, i ^ shift) for i in range(count)]
        send = lax.dynamic_index_in_dim(pieces, me ^ shift, axis=-2, keepdims=False)
        total = total + lax.ppermute(send, axis_name, perm)
    return total.astype(jnp.bfloat16)


def split_exact(value):
    high = value.astype(jnp.bfloat16)
    rest = value - lax.optimization_barrier(high).astype(jnp.float32)
    middle = rest.astype(jnp.bfloat16)
    low = (rest - lax.optimization_barrier(middle).astype(jnp.float32)).astype(jnp.bfloat16)
    return [high, middle, low]


def join_exact(parts):
    high, middle, low = (part.astype(jnp.float32) for part in parts)
    return (high + middle) + low


def mixer(x_in, b_in, c_in, decay_log, skip):
    highest = lax.Precision.HIGHEST
    seq_count, total_len, width_in = x_in.shape
    head_count = skip.shape[0]
    state_size = b_in.shape[2]
    chunk = total_len if total_len <= 128 else 64
    chunks = total_len // chunk
    x_float = x_in.astype(jnp.float32).reshape(seq_count, chunks, chunk, head_count, P_SIZE)
    b_float = b_in.astype(jnp.float32).reshape(seq_count, chunks, chunk, state_size)
    c_float = c_in.astype(jnp.float32).reshape(seq_count, chunks, chunk, state_size)
    cum_decay = jnp.cumsum(decay_log.reshape(seq_count, chunks, chunk, head_count), axis=2)
    scores = jnp.einsum("sktn,skun->sktu", c_float, b_float, precision=highest)
    causal = (jnp.arange(chunk)[:, None] >= jnp.arange(chunk)[None, :])[None, None, :, :, None]
    spans = cum_decay[:, :, :, None, :] - cum_decay[:, :, None, :, :]
    kernel = jnp.where(causal, jnp.exp(jnp.where(causal, spans, 0.0)), 0.0) * scores[..., None]
    ssd = jnp.einsum("sktuh,skuhp->skthp", kernel, x_float, precision=highest)
    if chunks > 1:
        final_decay = cum_decay[:, :, -1, :]
        tails = jnp.exp(final_decay[:, :, None, :] - cum_decay)
        states = jnp.einsum("skuh,skuhp,skun->skhpn", tails, x_float, b_float, precision=highest)

        def step(carry, inputs):
            decay_k, state_k = inputs
            return decay_k[:, :, None, None] * carry + state_k, carry

        _, incoming = lax.scan(
            step,
            jnp.zeros_like(states[:, 0]),
            (jnp.moveaxis(jnp.exp(final_decay), 1, 0), jnp.moveaxis(states, 1, 0)),
        )
        incoming = jnp.moveaxis(incoming, 0, 1)
        ssd = ssd + jnp.exp(cum_decay)[..., None] * jnp.einsum(
            "sktn,skhpn->skthp", c_float, incoming, precision=highest
        )
    ssd = ssd + skip[None, None, None, :, None] * x_float
    return ssd.reshape(seq_count, total_len, width_in)


def expert_ffn(gate_up, slot_rows):
    both = jnp.einsum("gfd,qd->gfq", gate_up[0], slot_rows, preferred_element_type=jnp.float32)
    return (jax.nn.silu(both[0]) * both[1]).astype(jnp.bfloat16)


def dispatch_routed(partial_value, moe_gain, gate_up, expert_ids, slot_ids, capacity):
    seq_count = partial_value.shape[0]
    model_width = moe_gain.shape[0]
    per_block = expert_ids.shape[1]
    pick_count = expert_ids.shape[2]
    row_count = seq_count * per_block
    ctx_count = lax.axis_size("ctx")
    group_count = lax.axis_size("expert")
    grouped = partial_value.reshape(
        seq_count, ctx_count, group_count, per_block, partial_value.shape[2]
    )
    reduced = lax.psum_scatter(grouped, "expert", scatter_dimension=2, tiled=True).astype(
        jnp.bfloat16
    )
    swapped = lax.all_to_all(reduced, "ctx", split_axis=1, concat_axis=4, tiled=True)
    mamba_out = swapped.reshape(seq_count, per_block, model_width)
    flat = mamba_out.reshape(row_count, model_width).astype(jnp.float32)
    scale = lax.rsqrt(jnp.mean(flat * flat, axis=1, keepdims=True) + 1e-05)
    normed = (flat * scale * moe_gain[None, :]).astype(jnp.bfloat16)
    chosen = expert_ids.reshape(row_count, pick_count)
    placed = slot_ids.reshape(row_count, pick_count)
    match_expert = chosen[:, :, None, None] == jnp.arange(group_count)[None, None, :, None]
    match_slot = placed[:, :, None, None] == jnp.arange(capacity)[None, None, None, :]
    selector = (match_expert & match_slot).astype(jnp.bfloat16)
    outgoing = jnp.einsum(
        "rkec,rd->ecd", selector, normed, preferred_element_type=jnp.float32
    ).astype(jnp.bfloat16)
    arrived = lax.all_to_all(outgoing, "expert", split_axis=0, concat_axis=0, tiled=True)
    piece = lax.all_gather(arrived[None], ("dp", "ctx"), axis=0, tiled=True)
    slot_rows = piece.reshape(-1, piece.shape[3])
    return (mamba_out, expert_ffn(gate_up, slot_rows)[None])


def local(
    x_in, z_in, b_in, c_in, decay_log, skip, out_weight, moe_gain, gate_up, expert_ids, slot_ids
):
    seq_count, block_len, width_in = x_in.shape
    state_size = b_in.shape[2]
    model_width = moe_gain.shape[0]
    col_width = out_weight.shape[1]
    per_block = expert_ids.shape[1]
    pick_count = expert_ids.shape[2]
    dp_count = lax.axis_size("dp")
    ctx_count = lax.axis_size("ctx")
    group_count = lax.axis_size("expert")
    device_count = dp_count * ctx_count * group_count
    row_count = seq_count * per_block
    capacity = max(2, 4 * row_count // group_count)

    head_count = decay_log.shape[2]
    decay_base = 2 * width_in + 2 * state_size

    def front(x_part, z_part, b_part, c_part, decay_part, after=None):
        part_count = x_part.shape[0]
        packed = jnp.concatenate([x_part, z_part, b_part, c_part] + split_exact(decay_part), axis=2)
        if after is not None:
            _, packed = lax.optimization_barrier((after, packed))
        packed = gather_blocks(packed, "ctx", ctx_count)
        packed = jnp.moveaxis(packed, 0, 1).reshape(
            part_count, ctx_count * block_len, packed.shape[3]
        )
        decay_all = join_exact(
            [packed[:, :, decay_base + i * head_count : decay_base + (i + 1) * head_count] for i in range(3)]
        )
        x_all = packed[:, :, :width_in]
        z_all = packed[:, :, width_in : 2 * width_in]
        b_all = packed[:, :, 2 * width_in : 2 * width_in + state_size]
        c_all = packed[:, :, 2 * width_in + state_size : decay_base]
        ssd = mixer(x_all, b_all, c_all, decay_all, skip)
        gated = (ssd * jax.nn.silu(z_all.astype(jnp.float32))).astype(jnp.bfloat16)
        projected = jnp.einsum("stk,kd->std", gated, out_weight, preferred_element_type=jnp.float32)
        return projected, packed

    if device_count * row_count * model_width * 2 > (8 << 20):
        partial_value = front(x_in, z_in, b_in, c_in, decay_log)[0]
        return dispatch_routed(partial_value, moe_gain, gate_up, expert_ids, slot_ids, capacity)
    total_len = ctx_count * block_len
    route = jnp.stack([expert_ids, slot_ids], axis=-1).astype(jnp.float32).reshape(-1)
    route_len = route.shape[0]
    extra_rows = -(-(group_count * route_len) // col_width)
    route_row = jnp.zeros((extra_rows * col_width,), jnp.float32)
    route_row = lax.dynamic_update_slice(route_row, route, (lax.axis_index("expert") * route_len,))
    piece_width = col_width // group_count
    split = 2 if seq_count % 2 == 0 else 1
    part_len = seq_count // split
    token_parts = []
    arrived = None
    for part in range(split):
        streams = slice(part * part_len, (part + 1) * part_len)
        partial_value, arrived = front(
            x_in[streams], z_in[streams], b_in[streams], c_in[streams], decay_log[streams], arrived
        )
        rows = partial_value.reshape(part_len * total_len, col_width)
        if part == split - 1:
            rows = jnp.concatenate([rows, route_row.reshape(extra_rows, col_width)], axis=0)
        piece = sum_scatter(rows, "expert", group_count)
        token_parts.append(gather_blocks(piece, "ctx", ctx_count))
    gathered = jnp.concatenate(token_parts, axis=1)
    gathered = gather_xor(gathered, "expert", group_count)
    gathered = gather_blocks(gathered, "dp", dp_count)
    row_total = seq_count * total_len
    extra = jnp.transpose(gathered[:, :, :, row_total:, :], (0, 2, 3, 1, 4))
    routes = extra.reshape(dp_count, ctx_count, -1)[:, :, : group_count * route_len]
    routes = routes.astype(jnp.int32)
    routes = routes.reshape(dp_count, ctx_count, group_count, seq_count, per_block, pick_count, 2)
    routes = jnp.transpose(routes, (0, 3, 1, 2, 4, 5, 6))
    tokens = gathered[:, :, :, :row_total, :]
    mine_rows = lax.dynamic_index_in_dim(tokens, lax.axis_index("dp"), axis=0, keepdims=False)
    mine_rows = mine_rows.reshape(
        group_count, ctx_count, seq_count, ctx_count * group_count, per_block, piece_width
    )
    mine_block = lax.axis_index("ctx") * group_count + lax.axis_index("expert")
    mine_rows = lax.dynamic_index_in_dim(mine_rows, mine_block, axis=3, keepdims=False)
    mamba_out = jnp.transpose(mine_rows, (2, 3, 1, 0, 4)).reshape(seq_count, per_block, model_width)
    token_count = dp_count * row_total
    flat = tokens.astype(jnp.float32)
    square_sum = jnp.sum(flat * flat, axis=(1, 2, 4), keepdims=True)
    scale = lax.rsqrt(square_sum / model_width + 1e-05)
    gain = jnp.transpose(moe_gain.reshape(ctx_count, group_count, piece_width), (1, 0, 2))
    normed = (flat * scale * gain[None, :, :, None, :]).astype(jnp.bfloat16)

    group = (
        (jnp.arange(dp_count)[:, None, None, None, None] * ctx_count
         + jnp.arange(ctx_count)[None, None, :, None, None]) * group_count
        + jnp.arange(group_count)[None, None, None, :, None]
    )
    group = jnp.broadcast_to(group, (dp_count, seq_count, ctx_count, group_count, per_block))
    target = group.reshape(token_count, 1) * capacity + routes[..., 1].reshape(token_count, pick_count)
    mine = routes[..., 0].reshape(token_count, pick_count) == lax.axis_index("expert")
    slot_count = device_count * capacity
    hit = mine[..., None] & (target[..., None] == jnp.arange(slot_count))
    selector = jnp.any(hit, axis=1).reshape(dp_count, row_total, slot_count)
    dispatched = jnp.einsum(
        "drq,decrk->qcek", selector.astype(jnp.bfloat16), normed, preferred_element_type=jnp.float32
    ).astype(jnp.bfloat16)
    hidden = expert_ffn(gate_up, dispatched.reshape(slot_count, model_width))
    return (mamba_out, hidden[None])


def solution(mesh):
    in_specs = (
        P("dp", "ctx", "expert"),
        P("dp", "ctx", "expert"),
        P("dp", "ctx", None),
        P("dp", "ctx", None),
        P("dp", "ctx", "expert"),
        P("expert"),
        P("expert", "ctx"),
        P(),
        P("expert", None, ("dp", "ctx"), None),
        P("dp", ("ctx", "expert"), None),
        P("dp", ("ctx", "expert"), None),
    )
    out_specs = (P("dp", ("ctx", "expert"), None), P("expert", ("dp", "ctx"), None))

    return jax.shard_map(local, mesh=mesh, in_specs=in_specs, out_specs=out_specs, check_vma=False)
```

```python
import jax
import jax.numpy as jnp
from jax import lax
from jax.sharding import PartitionSpec as P


P_SIZE = 64


def place(received, sources, count):
    slots = []
    for slot in range(count):
        block = received[0]
        for other, source in zip(received[1:], sources[1:]):
            block = jnp.where(source == slot, other, block)
        slots.append(block)
    return jnp.stack(slots)


def gather_blocks(value, axis_name, count):
    me = lax.axis_index(axis_name)
    received = [value]
    sources = [me]
    for shift in range(1, count):
        perm = [(i, (i + shift) % count) for i in range(count)]
        received.append(lax.ppermute(value, axis_name, perm))
        sources.append((me - shift) % count)
    return place(received, sources, count)


def gather_xor(value, axis_name, count):
    me = lax.axis_index(axis_name)
    received = [value]
    sources = [me]
    for shift in range(1, count):
        perm = [(i, i ^ shift) for i in range(count)]
        received.append(lax.ppermute(value, axis_name, perm))
        sources.append(me ^ shift)
    return place(received, sources, count)


def sum_scatter(value, axis_name, count):
    me = lax.axis_index(axis_name)
    pieces = value.reshape(value.shape[:-1] + (count, value.shape[-1] // count))
    total = lax.dynamic_index_in_dim(pieces, me, axis=-2, keepdims=False)
    for shift in range(1, count):
        perm = [(i, i ^ shift) for i in range(count)]
        send = lax.dynamic_index_in_dim(pieces, me ^ shift, axis=-2, keepdims=False)
        total = total + lax.ppermute(send, axis_name, perm)
    return total.astype(jnp.bfloat16)


def split_exact(value):
    high = value.astype(jnp.bfloat16)
    rest = value - lax.optimization_barrier(high).astype(jnp.float32)
    middle = rest.astype(jnp.bfloat16)
    low = (rest - lax.optimization_barrier(middle).astype(jnp.float32)).astype(jnp.bfloat16)
    return [high, middle, low]


def join_exact(parts):
    high, middle, low = (part.astype(jnp.float32) for part in parts)
    return (high + middle) + low


def mixer(x_in, b_in, c_in, decay_log, skip):
    highest = lax.Precision.HIGHEST
    seq_count, total_len, width_in = x_in.shape
    head_count = skip.shape[0]
    state_size = b_in.shape[2]
    chunk = total_len if total_len <= 128 else 64
    chunks = total_len // chunk
    x_float = x_in.astype(jnp.float32).reshape(seq_count, chunks, chunk, head_count, P_SIZE)
    b_float = b_in.astype(jnp.float32).reshape(seq_count, chunks, chunk, state_size)
    c_float = c_in.astype(jnp.float32).reshape(seq_count, chunks, chunk, state_size)
    cum_decay = jnp.cumsum(decay_log.reshape(seq_count, chunks, chunk, head_count), axis=2)
    scores = jnp.einsum("sktn,skun->sktu", c_float, b_float, precision=highest)
    causal = (jnp.arange(chunk)[:, None] >= jnp.arange(chunk)[None, :])[None, None, :, :, None]
    spans = cum_decay[:, :, :, None, :] - cum_decay[:, :, None, :, :]
    kernel = jnp.where(causal, jnp.exp(jnp.where(causal, spans, 0.0)), 0.0) * scores[..., None]
    ssd = jnp.einsum("sktuh,skuhp->skthp", kernel, x_float, precision=highest)
    if chunks > 1:
        final_decay = cum_decay[:, :, -1, :]
        tails = jnp.exp(final_decay[:, :, None, :] - cum_decay)
        states = jnp.einsum("skuh,skuhp,skun->skhpn", tails, x_float, b_float, precision=highest)

        def step(carry, inputs):
            decay_k, state_k = inputs
            return decay_k[:, :, None, None] * carry + state_k, carry

        _, incoming = lax.scan(
            step,
            jnp.zeros_like(states[:, 0]),
            (jnp.moveaxis(jnp.exp(final_decay), 1, 0), jnp.moveaxis(states, 1, 0)),
        )
        incoming = jnp.moveaxis(incoming, 0, 1)
        ssd = ssd + jnp.exp(cum_decay)[..., None] * jnp.einsum(
            "sktn,skhpn->skthp", c_float, incoming, precision=highest
        )
    ssd = ssd + skip[None, None, None, :, None] * x_float
    return ssd.reshape(seq_count, total_len, width_in)


def expert_ffn(gate_up, slot_rows):
    both = jnp.einsum("gfd,qd->gfq", gate_up[0], slot_rows, preferred_element_type=jnp.float32)
    return (jax.nn.silu(both[0]) * both[1]).astype(jnp.bfloat16)


def dispatch_routed(partial_value, moe_gain, gate_up, expert_ids, slot_ids, capacity):
    seq_count = partial_value.shape[0]
    model_width = moe_gain.shape[0]
    per_block = expert_ids.shape[1]
    pick_count = expert_ids.shape[2]
    row_count = seq_count * per_block
    ctx_count = lax.axis_size("ctx")
    group_count = lax.axis_size("expert")
    grouped = partial_value.reshape(
        seq_count, ctx_count, group_count, per_block, partial_value.shape[2]
    )
    reduced = lax.psum_scatter(grouped, "expert", scatter_dimension=2, tiled=True).astype(
        jnp.bfloat16
    )
    swapped = lax.all_to_all(reduced, "ctx", split_axis=1, concat_axis=4, tiled=True)
    mamba_out = swapped.reshape(seq_count, per_block, model_width)
    flat = mamba_out.reshape(row_count, model_width).astype(jnp.float32)
    scale = lax.rsqrt(jnp.mean(flat * flat, axis=1, keepdims=True) + 1e-05)
    normed = (flat * scale * moe_gain[None, :]).astype(jnp.bfloat16)
    chosen = expert_ids.reshape(row_count, pick_count)
    placed = slot_ids.reshape(row_count, pick_count)
    match_expert = chosen[:, :, None, None] == jnp.arange(group_count)[None, None, :, None]
    match_slot = placed[:, :, None, None] == jnp.arange(capacity)[None, None, None, :]
    selector = (match_expert & match_slot).astype(jnp.bfloat16)
    outgoing = jnp.einsum(
        "rkec,rd->ecd", selector, normed, preferred_element_type=jnp.float32
    ).astype(jnp.bfloat16)
    arrived = lax.all_to_all(outgoing, "expert", split_axis=0, concat_axis=0, tiled=True)
    piece = lax.all_gather(arrived[None], ("dp", "ctx"), axis=0, tiled=True)
    slot_rows = piece.reshape(-1, piece.shape[3])
    return (mamba_out, expert_ffn(gate_up, slot_rows)[None])


def local(
    x_in, z_in, b_in, c_in, decay_log, skip, out_weight, moe_gain, gate_up, expert_ids, slot_ids
):
    seq_count, block_len, width_in = x_in.shape
    state_size = b_in.shape[2]
    model_width = moe_gain.shape[0]
    col_width = out_weight.shape[1]
    per_block = expert_ids.shape[1]
    pick_count = expert_ids.shape[2]
    dp_count = lax.axis_size("dp")
    ctx_count = lax.axis_size("ctx")
    group_count = lax.axis_size("expert")
    device_count = dp_count * ctx_count * group_count
    row_count = seq_count * per_block
    capacity = max(2, 4 * row_count // group_count)

    head_count = decay_log.shape[2]
    decay_base = 2 * width_in + 2 * state_size

    def front(packed, after=None):
        part_count = packed.shape[0]
        if after is not None:
            _, packed = lax.optimization_barrier((after, packed))
        packed = gather_blocks(packed, "ctx", ctx_count)
        packed = jnp.moveaxis(packed, 0, 1).reshape(
            part_count, ctx_count * block_len, packed.shape[3]
        )
        decay_all = join_exact(
            [packed[:, :, decay_base + i * head_count : decay_base + (i + 1) * head_count] for i in range(3)]
        )
        x_all = packed[:, :, :width_in]
        z_all = packed[:, :, width_in : 2 * width_in]
        b_all = packed[:, :, 2 * width_in : 2 * width_in + state_size]
        c_all = packed[:, :, 2 * width_in + state_size : decay_base]
        ssd = mixer(x_all, b_all, c_all, decay_all, skip)
        gated = (ssd * jax.nn.silu(z_all.astype(jnp.float32))).astype(jnp.bfloat16)
        projected = jnp.einsum("stk,kd->std", gated, out_weight, preferred_element_type=jnp.float32)
        return projected, packed

    if device_count * row_count * model_width * 2 > (8 << 20):
        packed = jnp.concatenate([x_in, z_in, b_in, c_in] + split_exact(decay_log), axis=2)
        partial_value = front(packed)[0]
        return dispatch_routed(partial_value, moe_gain, gate_up, expert_ids, slot_ids, capacity)
    total_len = ctx_count * block_len
    route = jnp.stack([expert_ids, slot_ids], axis=-1).astype(jnp.float32).reshape(-1)
    route_len = route.shape[0]
    extra_rows = -(-(group_count * route_len) // col_width)
    route_row = jnp.zeros((extra_rows * col_width,), jnp.float32)
    route_row = lax.dynamic_update_slice(route_row, route, (lax.axis_index("expert") * route_len,))
    piece_width = col_width // group_count
    split = 2 if seq_count % 2 == 0 else 1
    part_len = seq_count // split
    token_parts = []
    arrived = None
    packed_all = jnp.concatenate([x_in, z_in, b_in, c_in] + split_exact(decay_log), axis=2)
    for part in range(split):
        streams = slice(part * part_len, (part + 1) * part_len)
        partial_value, arrived = front(packed_all[streams], arrived)
        rows = partial_value.reshape(part_len * total_len, col_width)
        if part == split - 1:
            rows = jnp.concatenate([rows, route_row.reshape(extra_rows, col_width)], axis=0)
        piece = sum_scatter(rows, "expert", group_count)
        token_parts.append(gather_blocks(piece, "ctx", ctx_count))
    gathered = jnp.concatenate(token_parts, axis=1)
    gathered = gather_xor(gathered, "expert", group_count)
    gathered = gather_blocks(gathered, "dp", dp_count)
    row_total = seq_count * total_len
    extra = jnp.transpose(gathered[:, :, :, row_total:, :], (0, 2, 3, 1, 4))
    routes = extra.reshape(dp_count, ctx_count, -1)[:, :, : group_count * route_len]
    routes = routes.astype(jnp.int32)
    routes = routes.reshape(dp_count, ctx_count, group_count, seq_count, per_block, pick_count, 2)
    routes = jnp.transpose(routes, (0, 3, 1, 2, 4, 5, 6))
    tokens = gathered[:, :, :, :row_total, :]
    mine_rows = lax.dynamic_index_in_dim(tokens, lax.axis_index("dp"), axis=0, keepdims=False)
    mine_rows = mine_rows.reshape(
        group_count, ctx_count, seq_count, ctx_count * group_count, per_block, piece_width
    )
    mine_block = lax.axis_index("ctx") * group_count + lax.axis_index("expert")
    mine_rows = lax.dynamic_index_in_dim(mine_rows, mine_block, axis=3, keepdims=False)
    mamba_out = jnp.transpose(mine_rows, (2, 3, 1, 0, 4)).reshape(seq_count, per_block, model_width)
    token_count = dp_count * row_total
    flat = tokens.astype(jnp.float32)
    square_sum = jnp.sum(flat * flat, axis=(1, 2, 4), keepdims=True)
    scale = lax.rsqrt(square_sum / model_width + 1e-05)
    gain = jnp.transpose(moe_gain.reshape(ctx_count, group_count, piece_width), (1, 0, 2))
    normed = (flat * scale * gain[None, :, :, None, :]).astype(jnp.bfloat16)

    group = (
        (jnp.arange(dp_count)[:, None, None, None, None] * ctx_count
         + jnp.arange(ctx_count)[None, None, :, None, None]) * group_count
        + jnp.arange(group_count)[None, None, None, :, None]
    )
    group = jnp.broadcast_to(group, (dp_count, seq_count, ctx_count, group_count, per_block))
    target = group.reshape(token_count, 1) * capacity + routes[..., 1].reshape(token_count, pick_count)
    mine = routes[..., 0].reshape(token_count, pick_count) == lax.axis_index("expert")
    slot_count = device_count * capacity
    hit = mine[..., None] & (target[..., None] == jnp.arange(slot_count))
    selector = jnp.any(hit, axis=1).reshape(dp_count, row_total, slot_count)
    dispatched = jnp.einsum(
        "drq,decrk->qcek", selector.astype(jnp.bfloat16), normed, preferred_element_type=jnp.float32
    ).astype(jnp.bfloat16)
    hidden = expert_ffn(gate_up, dispatched.reshape(slot_count, model_width))
    return (mamba_out, hidden[None])


def solution(mesh):
    in_specs = (
        P("dp", "ctx", "expert"),
        P("dp", "ctx", "expert"),
        P("dp", "ctx", None),
        P("dp", "ctx", None),
        P("dp", "ctx", "expert"),
        P("expert"),
        P("expert", "ctx"),
        P(),
        P("expert", None, ("dp", "ctx"), None),
        P("dp", ("ctx", "expert"), None),
        P("dp", ("ctx", "expert"), None),
    )
    out_specs = (P("dp", ("ctx", "expert"), None), P("expert", ("dp", "ctx"), None))

    return jax.shard_map(local, mesh=mesh, in_specs=in_specs, out_specs=out_specs, check_vma=False)
```

```python
import jax
import jax.numpy as jnp
from jax import lax
from jax.sharding import PartitionSpec as P


P_SIZE = 64


def place(received, sources, count):
    slots = []
    for slot in range(count):
        block = received[0]
        for other, source in zip(received[1:], sources[1:]):
            block = jnp.where(source == slot, other, block)
        slots.append(block)
    return jnp.stack(slots)


def gather_blocks(value, axis_name, count):
    me = lax.axis_index(axis_name)
    received = [value]
    sources = [me]
    for shift in range(1, count):
        perm = [(i, (i + shift) % count) for i in range(count)]
        received.append(lax.ppermute(value, axis_name, perm))
        sources.append((me - shift) % count)
    return place(received, sources, count)


def gather_xor(value, axis_name, count):
    me = lax.axis_index(axis_name)
    received = [value]
    sources = [me]
    for shift in range(1, count):
        perm = [(i, i ^ shift) for i in range(count)]
        received.append(lax.ppermute(value, axis_name, perm))
        sources.append(me ^ shift)
    return place(received, sources, count)


def sum_scatter(value, axis_name, count):
    me = lax.axis_index(axis_name)
    pieces = value.reshape(value.shape[:-1] + (count, value.shape[-1] // count))
    total = lax.dynamic_index_in_dim(pieces, me, axis=-2, keepdims=False)
    for shift in range(1, count):
        perm = [(i, i ^ shift) for i in range(count)]
        send = lax.dynamic_index_in_dim(pieces, me ^ shift, axis=-2, keepdims=False)
        total = total + lax.ppermute(send, axis_name, perm)
    return total.astype(jnp.bfloat16)


def split_exact(value):
    high = value.astype(jnp.bfloat16)
    rest = value - high.astype(jnp.float32)
    middle = rest.astype(jnp.bfloat16)
    low = (rest - middle.astype(jnp.float32)).astype(jnp.bfloat16)
    return [high, middle, low]


def join_exact(parts):
    high, middle, low = (part.astype(jnp.float32) for part in parts)
    return (high + middle) + low


def mixer(x_in, b_in, c_in, decay_log, skip):
    highest = lax.Precision.HIGHEST
    seq_count, total_len, width_in = x_in.shape
    head_count = skip.shape[0]
    state_size = b_in.shape[2]
    chunk = total_len if total_len <= 128 else 64
    chunks = total_len // chunk
    x_float = x_in.astype(jnp.float32).reshape(seq_count, chunks, chunk, head_count, P_SIZE)
    b_float = b_in.astype(jnp.float32).reshape(seq_count, chunks, chunk, state_size)
    c_float = c_in.astype(jnp.float32).reshape(seq_count, chunks, chunk, state_size)
    cum_decay = jnp.cumsum(decay_log.reshape(seq_count, chunks, chunk, head_count), axis=2)
    scores = jnp.einsum("sktn,skun->sktu", c_float, b_float, precision=highest)
    causal = (jnp.arange(chunk)[:, None] >= jnp.arange(chunk)[None, :])[None, None, :, :, None]
    spans = cum_decay[:, :, :, None, :] - cum_decay[:, :, None, :, :]
    kernel = jnp.where(causal, jnp.exp(jnp.where(causal, spans, 0.0)), 0.0) * scores[..., None]
    ssd = jnp.einsum("sktuh,skuhp->skthp", kernel, x_float, precision=highest)
    if chunks > 1:
        final_decay = cum_decay[:, :, -1, :]
        tails = jnp.exp(final_decay[:, :, None, :] - cum_decay)
        states = jnp.einsum("skuh,skuhp,skun->skhpn", tails, x_float, b_float, precision=highest)

        def step(carry, inputs):
            decay_k, state_k = inputs
            return decay_k[:, :, None, None] * carry + state_k, carry

        _, incoming = lax.scan(
            step,
            jnp.zeros_like(states[:, 0]),
            (jnp.moveaxis(jnp.exp(final_decay), 1, 0), jnp.moveaxis(states, 1, 0)),
        )
        incoming = jnp.moveaxis(incoming, 0, 1)
        ssd = ssd + jnp.exp(cum_decay)[..., None] * jnp.einsum(
            "sktn,skhpn->skthp", c_float, incoming, precision=highest
        )
    ssd = ssd + skip[None, None, None, :, None] * x_float
    return ssd.reshape(seq_count, total_len, width_in)


def expert_ffn(gate_up, slot_rows):
    both = jnp.einsum("gfd,qd->gfq", gate_up[0], slot_rows, preferred_element_type=jnp.float32)
    return (jax.nn.silu(both[0]) * both[1]).astype(jnp.bfloat16)


def dispatch_routed(partial_value, moe_gain, gate_up, expert_ids, slot_ids, capacity):
    seq_count = partial_value.shape[0]
    model_width = moe_gain.shape[0]
    per_block = expert_ids.shape[1]
    pick_count = expert_ids.shape[2]
    row_count = seq_count * per_block
    ctx_count = lax.axis_size("ctx")
    group_count = lax.axis_size("expert")
    grouped = partial_value.reshape(
        seq_count, ctx_count, group_count, per_block, partial_value.shape[2]
    )
    reduced = lax.psum_scatter(grouped, "expert", scatter_dimension=2, tiled=True).astype(
        jnp.bfloat16
    )
    swapped = lax.all_to_all(reduced, "ctx", split_axis=1, concat_axis=4, tiled=True)
    mamba_out = swapped.reshape(seq_count, per_block, model_width)
    flat = mamba_out.reshape(row_count, model_width).astype(jnp.float32)
    scale = lax.rsqrt(jnp.mean(flat * flat, axis=1, keepdims=True) + 1e-05)
    normed = (flat * scale * moe_gain[None, :]).astype(jnp.bfloat16)
    chosen = expert_ids.reshape(row_count, pick_count)
    placed = slot_ids.reshape(row_count, pick_count)
    match_expert = chosen[:, :, None, None] == jnp.arange(group_count)[None, None, :, None]
    match_slot = placed[:, :, None, None] == jnp.arange(capacity)[None, None, None, :]
    selector = (match_expert & match_slot).astype(jnp.bfloat16)
    outgoing = jnp.einsum(
        "rkec,rd->ecd", selector, normed, preferred_element_type=jnp.float32
    ).astype(jnp.bfloat16)
    arrived = lax.all_to_all(outgoing, "expert", split_axis=0, concat_axis=0, tiled=True)
    piece = lax.all_gather(arrived[None], ("dp", "ctx"), axis=0, tiled=True)
    slot_rows = piece.reshape(-1, piece.shape[3])
    return (mamba_out, expert_ffn(gate_up, slot_rows)[None])


def local(
    x_in, z_in, b_in, c_in, decay_log, skip, out_weight, moe_gain, gate_up, expert_ids, slot_ids
):
    seq_count, block_len, width_in = x_in.shape
    state_size = b_in.shape[2]
    model_width = moe_gain.shape[0]
    col_width = out_weight.shape[1]
    per_block = expert_ids.shape[1]
    pick_count = expert_ids.shape[2]
    dp_count = lax.axis_size("dp")
    ctx_count = lax.axis_size("ctx")
    group_count = lax.axis_size("expert")
    device_count = dp_count * ctx_count * group_count
    row_count = seq_count * per_block
    capacity = max(2, 4 * row_count // group_count)

    head_count = decay_log.shape[2]
    decay_base = 2 * width_in + 2 * state_size

    def front(packed, after=None):
        part_count = packed.shape[0]
        if after is not None:
            _, packed = lax.optimization_barrier((after, packed))
        packed = gather_blocks(packed, "ctx", ctx_count)
        packed = jnp.moveaxis(packed, 0, 1).reshape(
            part_count, ctx_count * block_len, packed.shape[3]
        )
        decay_all = join_exact(
            [packed[:, :, decay_base + i * head_count : decay_base + (i + 1) * head_count] for i in range(3)]
        )
        x_all = packed[:, :, :width_in]
        z_all = packed[:, :, width_in : 2 * width_in]
        b_all = packed[:, :, 2 * width_in : 2 * width_in + state_size]
        c_all = packed[:, :, 2 * width_in + state_size : decay_base]
        ssd = mixer(x_all, b_all, c_all, decay_all, skip)
        gated = (ssd * jax.nn.silu(z_all.astype(jnp.float32))).astype(jnp.bfloat16)
        projected = jnp.einsum("stk,kd->std", gated, out_weight, preferred_element_type=jnp.float32)
        return projected, packed

    if device_count * row_count * model_width * 2 > (8 << 20):
        packed = jnp.concatenate([x_in, z_in, b_in, c_in] + split_exact(decay_log), axis=2)
        partial_value = front(packed)[0]
        return dispatch_routed(partial_value, moe_gain, gate_up, expert_ids, slot_ids, capacity)
    total_len = ctx_count * block_len
    route = jnp.stack([expert_ids, slot_ids], axis=-1).astype(jnp.float32).reshape(-1)
    route_len = route.shape[0]
    extra_rows = -(-(group_count * route_len) // col_width)
    route_row = jnp.zeros((extra_rows * col_width,), jnp.float32)
    route_row = lax.dynamic_update_slice(route_row, route, (lax.axis_index("expert") * route_len,))
    piece_width = col_width // group_count
    split = 2 if seq_count % 2 == 0 else 1
    part_len = seq_count // split
    token_parts = []
    arrived = None
    packed_all = jnp.concatenate([x_in, z_in, b_in, c_in] + split_exact(decay_log), axis=2)
    for part in range(split):
        streams = slice(part * part_len, (part + 1) * part_len)
        partial_value, arrived = front(packed_all[streams], arrived)
        rows = partial_value.reshape(part_len * total_len, col_width)
        if part == split - 1:
            rows = jnp.concatenate([rows, route_row.reshape(extra_rows, col_width)], axis=0)
        piece = sum_scatter(rows, "expert", group_count)
        token_parts.append(gather_blocks(piece, "ctx", ctx_count))
    gathered = jnp.concatenate(token_parts, axis=1)
    gathered = gather_xor(gathered, "expert", group_count)
    row_total = seq_count * total_len
    slot_count = device_count * capacity
    gain = jnp.transpose(moe_gain.reshape(ctx_count, group_count, piece_width), (1, 0, 2))
    me_dp = lax.axis_index("dp")

    def dispatch_block(block, source):
        extra = jnp.transpose(block[:, :, row_total:, :], (1, 2, 0, 3))
        routes = extra.reshape(ctx_count, -1)[:, : group_count * route_len].astype(jnp.int32)
        routes = routes.reshape(ctx_count, group_count, seq_count, per_block, pick_count, 2)
        routes = jnp.transpose(routes, (2, 0, 1, 3, 4, 5))
        flat = block[:, :, :row_total, :].astype(jnp.float32)
        square_sum = jnp.sum(flat * flat, axis=(0, 1, 3), keepdims=True)
        scale = lax.rsqrt(square_sum / model_width + 1e-05)
        normed = (flat * scale * gain[:, :, None, :]).astype(jnp.bfloat16)
        group = (
            (source * ctx_count + jnp.arange(ctx_count)[None, :, None, None]) * group_count
            + jnp.arange(group_count)[None, None, :, None]
        )
        group = jnp.broadcast_to(group, (seq_count, ctx_count, group_count, per_block))
        target = group.reshape(row_total, 1) * capacity + routes[..., 1].reshape(row_total, pick_count)
        mine = routes[..., 0].reshape(row_total, pick_count) == lax.axis_index("expert")
        hit = mine[..., None] & (target[..., None] == jnp.arange(slot_count))
        selector = jnp.any(hit, axis=1)
        return jnp.einsum(
            "rq,ecrk->qcek", selector.astype(jnp.bfloat16), normed, preferred_element_type=jnp.float32
        )

    own = gathered
    mine_rows = own[:, :, :row_total, :].reshape(
        group_count, ctx_count, seq_count, ctx_count * group_count, per_block, piece_width
    )
    mine_block = lax.axis_index("ctx") * group_count + lax.axis_index("expert")
    mine_rows = lax.dynamic_index_in_dim(mine_rows, mine_block, axis=3, keepdims=False)
    mamba_out = jnp.transpose(mine_rows, (2, 3, 1, 0, 4)).reshape(seq_count, per_block, model_width)
    total = dispatch_block(own, me_dp)
    for shift in range(1, dp_count):
        perm = [(i, (i + shift) % dp_count) for i in range(dp_count)]
        other = lax.ppermute(own, "dp", perm)
        total = total + dispatch_block(other, (me_dp - shift) % dp_count)
    dispatched = total.astype(jnp.bfloat16)
    hidden = expert_ffn(gate_up, dispatched.reshape(slot_count, model_width))
    return (mamba_out, hidden[None])


def solution(mesh):
    in_specs = (
        P("dp", "ctx", "expert"),
        P("dp", "ctx", "expert"),
        P("dp", "ctx", None),
        P("dp", "ctx", None),
        P("dp", "ctx", "expert"),
        P("expert"),
        P("expert", "ctx"),
        P(),
        P("expert", None, ("dp", "ctx"), None),
        P("dp", ("ctx", "expert"), None),
        P("dp", ("ctx", "expert"), None),
    )
    out_specs = (P("dp", ("ctx", "expert"), None), P("expert", ("dp", "ctx"), None))

    return jax.shard_map(local, mesh=mesh, in_specs=in_specs, out_specs=out_specs, check_vma=False)
```
